32 devices in a mesh: req: 2 (over x), seq: 16 (over z, y, core).
Axes of the slice: x: 2, y: 2, z: 4, core: 2. Of those that a mesh axis runs over, the one named last changes fastest.
Arguments:
- states: bfloat16 [4, 4, 4544], P(None, 'req', 'seq'), may hold values from -6 to 6
- kv_cache: bfloat16 [4, 8192, 128], P('req', 'seq'), may hold values from -48 to 48, as said below
- lengths: int32 [4], replicated, may hold values from 1 to 8188, as said below
- placement: int32 [4], replicated, may hold values from 0 to 3, each once
- norm_gain: bfloat16 [4544], replicated, may hold values from 0.25 to 1.75
- norm_bias: bfloat16 [4544], replicated, may hold values from -1.5 to 1.5
- w_query: bfloat16 [4544, 4544], P('req', 'seq'), may hold values from -0.09375 to 0.09375
- w_keyval: bfloat16 [4544, 128], P('req'), may hold values from -0.09375 to 0.09375
- w_out: bfloat16 [4544, 4544], P('seq', 'req'), may hold values from -0.09375 to 0.09375
- w_up: bfloat16 [4544, 18176], P('req', 'seq'), may hold values from -0.09375 to 0.09375
- w_down: bfloat16 [18176, 4544], P('seq', 'req'), may hold values from -0.046875 to 0.046875
Outputs:
- new_states: bfloat16 [4, 4, 4544], P(None, 'req', 'seq')
- new_cache: bfloat16 [4, 8192, 128], P('req', 'seq')
The draws below stay inside these ranges and needn't reach their ends.
Inputs may be any that keep to these rules, and one draw needn't show every extreme that they name: Request r's cache holds its first lengths[r] positions; some request has exactly 8188. `kv_cache`: row i is the cache of request placement[i]; positions at or beyond that request's length hold arbitrary values. `placement`: each request is served by exactly one slot.
All inputs are finite; a program needn't handle non-finite values.
Results may differ from the reference program's by a relative error of at most 0.012.
The reference program's roundings to bfloat16 on the way count: a program that leaves them out, or rounds other values in their place, can miss the bound.
Values may be sent and summed in bfloat16 or wider, within the bound.
No kernel may reach another device: no remote copies, remote signals or barrier semaphores. Data moves between devices by JAX's collectives and lax.ppermute only.
A program may use at most 192 MiB of HBM per device.

```python
import jax
import jax.numpy as jnp
from jax import lax

D = 4544
HEADS = 71
HEAD = 64
FF = 18176
STEPS = 4
REQUESTS = 4
CAP = 8192
MAX_LEN = 8188


def draw_lengths(key, part):
    first_key, second_key = jax.random.split(key)
    raw_draw = jax.random.randint(first_key, (REQUESTS,), 0, MAX_LEN, dtype=jnp.int32)
    skewed = 1 + raw_draw * raw_draw // MAX_LEN
    chosen = jax.random.randint(second_key, (), 0, REQUESTS, dtype=jnp.int32)
    return jnp.where(jnp.arange(REQUESTS, dtype=jnp.int32) == chosen, MAX_LEN, skewed).astype(jnp.int32)


def draw_kv_cache(key, part):
    first_key, second_key = jax.random.split(key, 2)
    key_rows = jnp.clip(3.0 * jax.random.normal(first_key, (REQUESTS, CAP, HEAD), jnp.float32), -18.0, 18.0)
    value_rows = jnp.clip(jax.random.normal(second_key, (REQUESTS, CAP, HEAD), jnp.float32), -6.0, 6.0)
    return jnp.concatenate([key_rows, value_rows], axis=-1).astype(jnp.bfloat16)


def shard_levels(rng, dims, cuts, smallest, top_value):
    def one(dim, parts):
        draws = jax.random.uniform(jax.random.fold_in(jax.random.fold_in(rng, 6), dim), (parts,), jnp.float32, smallest / len(cuts), top_value / len(cuts))
        return jnp.repeat(jnp.exp(draws), dims[dim] // parts).reshape((-1,) + (1,) * (len(dims) - dim - 1))

    gain = one(*cuts[0])
    for cut in cuts[1:]:
        gain = gain * one(*cut)
    return gain


def centred(own_key, extent, deviation, limit, cuts=(), held_as=jnp.bfloat16):
    loudness = shard_levels(own_key, extent, cuts, -0.22, 0.18) if cuts else 1.0
    drawn = jax.random.normal(own_key, extent, jnp.float32) * deviation * loudness
    return jnp.minimum(jnp.maximum(drawn, -limit), limit).astype(held_as)


def setup_inputs(seed: int = 0) -> dict:
    splits = jax.random.split(jax.random.key(seed), 12)
    states = centred(splits[0], (STEPS, REQUESTS, D), 1.0, 6.0, ((1, 2), (2, 16)))
    kv_cache = draw_kv_cache(jax.random.fold_in(splits[11], 71), 0)
    lengths = draw_lengths(jax.random.fold_in(splits[11], 71), 0)
    placement = jax.random.permutation(splits[3], REQUESTS).astype(jnp.int32)
    norm_gain = jnp.clip(1.0 + 0.15 * jax.random.normal(splits[4], (D,), jnp.float32), 0.25, 1.75).astype(jnp.bfloat16)
    norm_bias = centred(splits[5], (D,), 0.3, 1.5)
    w_query = centred(splits[6], (D, D), D ** -0.5, 0.09375, ((0, 2), (1, 16)))
    w_keyval = centred(splits[7], (D, 2 * HEAD), D ** -0.5, 0.09375, ((0, 2),))
    w_out = centred(splits[8], (D, D), D ** -0.5, 0.09375, ((0, 16), (1, 2)))
    w_up = centred(splits[9], (D, FF), D ** -0.5, 0.09375, ((0, 2), (1, 16)))
    w_down = centred(splits[10], (FF, D), FF ** -0.5, 0.046875, ((0, 16), (1, 2)))
    return {"states": states, "kv_cache": kv_cache, "lengths": lengths, "placement": placement, "norm_gain": norm_gain, "norm_bias": norm_bias, "w_query": w_query, "w_keyval": w_keyval, "w_out": w_out, "w_up": w_up, "w_down": w_down}


EPSILON = 1e-05

def layer_norm(row_block, norm_gain, norm_bias):
    values = row_block.astype(jnp.float32)
    average = lax.optimization_barrier(jnp.mean(values, axis=-1, keepdims=True))
    centered = values - average
    spread = lax.optimization_barrier(jnp.mean(centered * centered, axis=-1, keepdims=True))
    scaled = centered * lax.rsqrt(spread + EPSILON)
    return (scaled * norm_gain.astype(jnp.float32) + norm_bias.astype(jnp.float32)).astype(jnp.bfloat16)

def rotate(vectors, positions):
    head_width = vectors.shape[-1]
    half_width = head_width // 2
    frequency = 10000.0 ** (-(jnp.arange(half_width, dtype=jnp.float32) * 2.0) / head_width)
    angles = positions.astype(jnp.float32)[:, None] * frequency[None, :]
    cosine = jnp.concatenate([jnp.cos(angles), jnp.cos(angles)], axis=-1)[:, None, :]
    sine_wave = jnp.concatenate([jnp.sin(angles), jnp.sin(angles)], axis=-1)[:, None, :]
    turned = jnp.concatenate([-vectors[..., half_width:], vectors[..., :half_width]], axis=-1)
    return vectors * cosine + turned * sine_wave

def attend_one(packed_inputs):
    query_rows, cache_rows, position = packed_inputs
    head_width = query_rows.shape[-1]
    key_rows = cache_rows[:, :head_width].astype(jnp.float32)
    value_rows = cache_rows[:, head_width:].astype(jnp.float32)
    scores = jnp.einsum('hd,sd->hs', query_rows.astype(jnp.float32), key_rows) * head_width ** (-0.5)
    valid_mask = jnp.arange(cache_rows.shape[0], dtype=jnp.int32) <= position
    masked = jnp.where(valid_mask[None, :], scores, -jnp.inf)
    highest = lax.optimization_barrier(jnp.max(masked, axis=-1, keepdims=True))
    weights = jnp.exp(masked - highest)
    weight_total = lax.optimization_barrier(jnp.sum(weights, axis=-1, keepdims=True))
    return jnp.einsum('hs,sd->hd', weights, value_rows) / weight_total

def reference(states, kv_cache, lengths, placement, norm_gain, norm_bias, w_query, w_keyval, w_out, w_up, w_down):
    request_count = placement.shape[0]
    slot_lengths = lengths[placement]
    rows_index = jnp.arange(request_count, dtype=jnp.int32)
    inverse = jnp.zeros((request_count,), jnp.int32).at[placement].set(rows_index)
    cache_now = kv_cache
    results = []
    for step_index in range(STEPS):
        current = states[step_index][placement]
        normed = layer_norm(current, norm_gain, norm_bias)
        query_raw = jnp.dot(normed, w_query, preferred_element_type=jnp.float32).astype(jnp.bfloat16)
        keyval = jnp.dot(normed, w_keyval, preferred_element_type=jnp.float32)
        positions = slot_lengths + step_index
        query_rows = rotate(query_raw.astype(jnp.float32).reshape(request_count, HEADS, HEAD), positions).astype(jnp.bfloat16)
        new_key = rotate(keyval[:, None, :HEAD], positions)[:, 0, :]
        new_entry = jnp.concatenate([new_key, keyval[:, HEAD:]], axis=-1).astype(jnp.bfloat16)
        cache_now = cache_now.at[rows_index, positions].set(new_entry)
        attended = lax.map(attend_one, (query_rows, cache_now, positions))
        mixed_part = attended.reshape(request_count, HEADS * HEAD).astype(jnp.bfloat16)
        hidden = jax.nn.gelu(jnp.dot(normed, w_up, preferred_element_type=jnp.float32), approximate=False).astype(jnp.bfloat16)
        branch_sum = jnp.dot(mixed_part, w_out, preferred_element_type=jnp.float32) + jnp.dot(hidden, w_down, preferred_element_type=jnp.float32)
        results.append((current.astype(jnp.float32) + branch_sum).astype(jnp.bfloat16))
    stacked = jnp.stack(results)
    return (stacked[:, inverse], cache_now)
```

```python
import jax
import jax.numpy as jnp
from jax import lax
from jax.sharding import PartitionSpec as P


EPSILON = 1e-05
NEGATIVE = -1e30
ALL = ("req", "seq")


def layer_norm(row_block, norm_gain, norm_bias):
    values = row_block.astype(jnp.float32)
    average = jnp.mean(values, axis=-1, keepdims=True)
    centered = values - average
    spread = jnp.mean(centered * centered, axis=-1, keepdims=True)
    scaled = centered * lax.rsqrt(spread + EPSILON)
    return (scaled * norm_gain.astype(jnp.float32) + norm_bias.astype(jnp.float32)).astype(
        jnp.bfloat16
    )


def rotate(vectors, positions):
    head_width = vectors.shape[-1]
    half_width = head_width // 2
    frequency = 10000.0 ** (-(jnp.arange(half_width, dtype=jnp.float32) * 2.0) / head_width)
    angles = positions.astype(jnp.float32)[:, None] * frequency[None, :]
    cosine = jnp.concatenate([jnp.cos(angles), jnp.cos(angles)], axis=-1)[:, None, :]
    sine_wave = jnp.concatenate([jnp.sin(angles), jnp.sin(angles)], axis=-1)[:, None, :]
    turned = jnp.concatenate([-vectors[..., half_width:], vectors[..., :half_width]], axis=-1)
    return vectors * cosine + turned * sine_wave


def shards(
    states,
    kv_cache,
    lengths,
    placement,
    norm_gain,
    norm_bias,
    w_query,
    w_keyval,
    w_out,
    w_up,
    w_down,
):
    steps = states.shape[0]
    group_rows = kv_cache.shape[0]
    seg_length = kv_cache.shape[1]
    head_width = kv_cache.shape[2] // 2
    model_width = norm_gain.shape[0]
    head_count = model_width // head_width
    slice_width = states.shape[2]
    part_width = w_query.shape[0]
    total = placement.shape[0]
    req_size = total // group_rows
    seq_size = model_width // slice_width
    rows = steps * total
    group_index = lax.axis_index("req")
    shard_index = lax.axis_index("seq")

    own_requests = lax.dynamic_slice_in_dim(placement, group_index * group_rows, group_rows, 0)
    slot_lengths = jnp.take(lengths, own_requests)
    step_offsets = jnp.arange(steps, dtype=jnp.int32)
    positions = slot_lengths[None, :] + step_offsets[:, None]

    every = lax.all_gather(states, ALL, axis=0, tiled=False)
    every = every.reshape(req_size, seq_size, steps, group_rows, slice_width)
    every = every.transpose(2, 0, 3, 1, 4).reshape(steps, total, model_width)
    current_all = jnp.take(every, placement, axis=1)
    normed = layer_norm(current_all.reshape(rows, model_width), norm_gain, norm_bias)
    normed_part = lax.dynamic_slice_in_dim(normed, group_index * part_width, part_width, 1)

    part_query = jnp.dot(normed_part, w_query, preferred_element_type=jnp.float32)
    part_keyval = jnp.dot(normed_part, w_keyval, preferred_element_type=jnp.float32)
    part_up = jnp.dot(normed_part, w_up, preferred_element_type=jnp.float32)
    first = lax.psum(jnp.concatenate([part_query, part_keyval, part_up], axis=1), "req")
    query_raw = first[:, :slice_width].astype(jnp.bfloat16).reshape(steps, total, slice_width)
    keyval = first[:, slice_width : slice_width + 2 * head_width].reshape(steps, total, 2 * head_width)
    up_part = first[:, slice_width + 2 * head_width :]

    own_query = lax.dynamic_slice_in_dim(query_raw, group_index * group_rows, group_rows, 1)
    query_all = lax.all_gather(own_query, "seq", axis=2, tiled=True)
    flat_positions = positions.reshape(-1)
    query_rows = rotate(
        query_all.astype(jnp.float32).reshape(steps * group_rows, head_count, head_width),
        flat_positions,
    ).astype(jnp.bfloat16)
    own_keyval = lax.dynamic_slice_in_dim(keyval, group_index * group_rows, group_rows, 1)
    own_keyval = own_keyval.reshape(steps * group_rows, 2 * head_width)
    new_key = rotate(own_keyval[:, None, :head_width], flat_positions)[:, 0, :]
    new_entry = jnp.concatenate([new_key, own_keyval[:, head_width:]], axis=-1).astype(jnp.bfloat16)
    new_entry = new_entry.reshape(steps, group_rows, 2 * head_width)

    local_slots = jnp.arange(seg_length, dtype=jnp.int32)
    global_positions = shard_index * seg_length + local_slots
    cache_now = kv_cache
    for step_index in range(steps):
        write_mask = global_positions[None, :] == positions[step_index][:, None]
        cache_now = jnp.where(write_mask[:, :, None], new_entry[step_index][:, None, :], cache_now)

    key_rows = cache_now[:, :, :head_width]
    value_rows = cache_now[:, :, head_width:]
    query_heads = (
        query_rows.reshape(steps, group_rows, head_count, head_width)
        .transpose(1, 0, 2, 3)
        .reshape(group_rows, steps * head_count, head_width)
    )
    scores = jnp.einsum(
        "gqd,gsd->gqs", query_heads, key_rows, preferred_element_type=jnp.float32
    ) * head_width ** (-0.5)
    valid = global_positions[None, None, :] <= positions.T[:, :, None]
    valid = jnp.broadcast_to(
        valid[:, :, None, :], (group_rows, steps, head_count, seg_length)
    ).reshape(group_rows, steps * head_count, seg_length)
    local_peak = jnp.max(jnp.where(valid, scores, NEGATIVE), axis=-1)
    weights = jnp.where(valid, jnp.exp(scores - local_peak[:, :, None]), 0.0)
    local_total = jnp.sum(weights, axis=-1)
    local_weighted = jnp.einsum(
        "gqs,gsd->gqd", weights, value_rows, preferred_element_type=jnp.float32
    )

    peak_buffer = jnp.full((total, steps * head_count), NEGATIVE, jnp.float32)
    peak_buffer = lax.dynamic_update_slice_in_dim(
        peak_buffer, local_peak, group_index * group_rows, 0
    )
    peak = lax.pmax(peak_buffer, ALL)
    own_peak = lax.dynamic_slice_in_dim(peak, group_index * group_rows, group_rows, 0)
    scale = jnp.exp(local_peak - own_peak)
    packed = jnp.concatenate(
        [local_weighted * scale[:, :, None], (local_total * scale)[:, :, None]], axis=-1
    )
    packed_buffer = jnp.zeros((total, steps * head_count, head_width + 1), jnp.float32)
    packed_buffer = lax.dynamic_update_slice_in_dim(
        packed_buffer, packed, group_index * group_rows, 0
    )
    summed = lax.psum(packed_buffer, ALL)
    mixed = summed[:, :, :head_width] / summed[:, :, head_width:]
    mixed = (
        mixed.reshape(total, steps, model_width)
        .transpose(1, 0, 2)
        .reshape(rows, model_width)
        .astype(jnp.bfloat16)
    )
    mixed_part = lax.dynamic_slice_in_dim(mixed, shard_index * slice_width, slice_width, 1)

    hidden = jax.nn.gelu(up_part, approximate=False).astype(jnp.bfloat16)
    partial_sum = jnp.dot(mixed_part, w_out, preferred_element_type=jnp.float32) + jnp.dot(
        hidden, w_down, preferred_element_type=jnp.float32
    )
    out_buffer = jnp.zeros((rows, model_width), jnp.float32)
    out_buffer = lax.dynamic_update_slice_in_dim(
        out_buffer, partial_sum, group_index * part_width, 1
    )
    branch = lax.psum(out_buffer, ALL).reshape(steps, total, model_width)

    inverse = (
        jnp.zeros((total,), jnp.int32).at[placement].set(jnp.arange(total, dtype=jnp.int32))
    )
    own_inverse = lax.dynamic_slice_in_dim(inverse, group_index * group_rows, group_rows, 0)
    own_branch = jnp.take(branch, own_inverse, axis=1)
    own_branch = lax.dynamic_slice_in_dim(own_branch, shard_index * slice_width, slice_width, 2)
    new_states = (states.astype(jnp.float32) + own_branch).astype(jnp.bfloat16)
    return (new_states, cache_now)


def solution(mesh):
    in_specs = (
        P(None, "req", "seq"),
        P("req", "seq", None),
        P(),
        P(),
        P(),
        P(),
        P("req", "seq"),
        P("req", None),
        P("seq", "req"),
        P("req", "seq"),
        P("seq", "req"),
    )
    out_specs = (P(None, "req", "seq"), P("req", "seq", None))
    return jax.shard_map(shards, mesh=mesh, in_specs=in_specs, out_specs=out_specs, check_vma=False)
```

```python
import jax
import jax.numpy as jnp
from jax import lax
from jax.sharding import PartitionSpec as P


EPSILON = 1e-05
NEGATIVE = -1e30
ALL = ("req", "seq")


def xor_pairs(size, bit):
    return [(index, index ^ bit) for index in range(size)]


def gather_blocks(block, axis, size):
    index = lax.axis_index(axis)
    blocks = block[None]
    bit = 1
    while bit < size:
        other = lax.ppermute(blocks, axis, xor_pairs(size, bit))
        low = (index // bit) % 2 == 0
        blocks = jnp.where(
            low, jnp.concatenate([blocks, other]), jnp.concatenate([other, blocks])
        )
        bit *= 2
    return blocks


def sum_over(value, axis, size):
    bit = 1
    while bit < size:
        value = value + lax.ppermute(value, axis, xor_pairs(size, bit))
        bit *= 2
    return value


def scatter_sum(blocks, axis, size):
    index = lax.axis_index(axis)
    bit = size // 2
    while bit >= 1:
        half = blocks.shape[0] // 2
        high = (index // bit) % 2 == 1
        keep = jnp.where(high, blocks[half:], blocks[:half])
        send = jnp.where(high, blocks[:half], blocks[half:])
        blocks = keep + lax.ppermute(send, axis, xor_pairs(size, bit))
        bit //= 2
    return blocks[0]


def merge_over(packed, axis, size):
    bit = 1
    while bit < size:
        other = lax.ppermute(packed, axis, xor_pairs(size, bit))
        peak_first, peak_second = packed[..., 0], other[..., 0]
        peak = jnp.maximum(peak_first, peak_second)
        scale_first = jnp.exp(peak_first - peak)[..., None]
        scale_second = jnp.exp(peak_second - peak)[..., None]
        merged = packed[..., 1:] * scale_first + other[..., 1:] * scale_second
        packed = jnp.concatenate([peak[..., None], merged], axis=-1)
        bit *= 2
    return packed


def layer_norm(row_block, norm_gain, norm_bias):
    values = row_block.astype(jnp.float32)
    average = jnp.mean(values, axis=-1, keepdims=True)
    centered = values - average
    spread = jnp.mean(centered * centered, axis=-1, keepdims=True)
    scaled = centered * lax.rsqrt(spread + EPSILON)
    return (scaled * norm_gain.astype(jnp.float32) + norm_bias.astype(jnp.float32)).astype(
        jnp.bfloat16
    )


def rotate(vectors, positions):
    head_width = vectors.shape[-1]
    half_width = head_width // 2
    frequency = 10000.0 ** (-(jnp.arange(half_width, dtype=jnp.float32) * 2.0) / head_width)
    angles = positions.astype(jnp.float32)[:, None] * frequency[None, :]
    cosine = jnp.concatenate([jnp.cos(angles), jnp.cos(angles)], axis=-1)[:, None, :]
    sine_wave = jnp.concatenate([jnp.sin(angles), jnp.sin(angles)], axis=-1)[:, None, :]
    turned = jnp.concatenate([-vectors[..., half_width:], vectors[..., :half_width]], axis=-1)
    return vectors * cosine + turned * sine_wave


def shards(
    states,
    kv_cache,
    lengths,
    placement,
    norm_gain,
    norm_bias,
    w_query,
    w_keyval,
    w_out,
    w_up,
    w_down,
):
    steps = states.shape[0]
    group_rows = kv_cache.shape[0]
    seg_length = kv_cache.shape[1]
    head_width = kv_cache.shape[2] // 2
    model_width = norm_gain.shape[0]
    head_count = model_width // head_width
    slice_width = states.shape[2]
    part_width = w_query.shape[0]
    total = placement.shape[0]
    req_size = total // group_rows
    seq_size = model_width // slice_width
    rows = steps * total
    group_index = lax.axis_index("req")
    shard_index = lax.axis_index("seq")

    own_requests = lax.dynamic_slice_in_dim(placement, group_index * group_rows, group_rows, 0)
    slot_lengths = jnp.take(lengths, own_requests)
    step_offsets = jnp.arange(steps, dtype=jnp.int32)
    positions = slot_lengths[None, :] + step_offsets[:, None]

    every = gather_blocks(gather_blocks(states, "seq", seq_size), "req", req_size)
    every = every.transpose(2, 0, 3, 1, 4).reshape(steps, total, model_width)
    current_all = jnp.take(every, placement, axis=1)
    normed = layer_norm(current_all.reshape(rows, model_width), norm_gain, norm_bias)
    normed_part = lax.dynamic_slice_in_dim(normed, group_index * part_width, part_width, 1)

    part_query = jnp.dot(normed_part, w_query, preferred_element_type=jnp.float32)
    part_keyval = jnp.dot(normed_part, w_keyval, preferred_element_type=jnp.float32)
    part_up = jnp.dot(normed_part, w_up, preferred_element_type=jnp.float32)
    first = sum_over(jnp.concatenate([part_query, part_keyval, part_up], axis=1), "req", req_size)
    query_raw = first[:, :slice_width].astype(jnp.bfloat16).reshape(steps, total, slice_width)
    keyval = first[:, slice_width : slice_width + 2 * head_width].reshape(steps, total, 2 * head_width)
    up_part = first[:, slice_width + 2 * head_width :]

    own_query = lax.dynamic_slice_in_dim(query_raw, group_index * group_rows, group_rows, 1)
    query_all = gather_blocks(own_query, "seq", seq_size)
    query_all = query_all.transpose(1, 2, 0, 3).reshape(steps, group_rows, model_width)
    flat_positions = positions.reshape(-1)
    query_rows = rotate(
        query_all.astype(jnp.float32).reshape(steps * group_rows, head_count, head_width),
        flat_positions,
    ).astype(jnp.bfloat16)
    own_keyval = lax.dynamic_slice_in_dim(keyval, group_index * group_rows, group_rows, 1)
    own_keyval = own_keyval.reshape(steps * group_rows, 2 * head_width)
    new_key = rotate(own_keyval[:, None, :head_width], flat_positions)[:, 0, :]
    new_entry = jnp.concatenate([new_key, own_keyval[:, head_width:]], axis=-1).astype(jnp.bfloat16)
    new_entry = new_entry.reshape(steps, group_rows, 2 * head_width)

    local_slots = jnp.arange(seg_length, dtype=jnp.int32)
    global_positions = shard_index * seg_length + local_slots
    cache_now = kv_cache
    for step_index in range(steps):
        write_mask = global_positions[None, :] == positions[step_index][:, None]
        cache_now = jnp.where(write_mask[:, :, None], new_entry[step_index][:, None, :], cache_now)

    key_rows = cache_now[:, :, :head_width]
    value_rows = cache_now[:, :, head_width:]
    query_heads = (
        query_rows.reshape(steps, group_rows, head_count, head_width)
        .transpose(1, 0, 2, 3)
        .reshape(group_rows, steps * head_count, head_width)
    )
    scores = jnp.einsum(
        "gqd,gsd->gqs", query_heads, key_rows, preferred_element_type=jnp.float32
    ) * head_width ** (-0.5)
    valid = global_positions[None, None, :] <= positions.T[:, :, None]
    valid = jnp.broadcast_to(
        valid[:, :, None, :], (group_rows, steps, head_count, seg_length)
    ).reshape(group_rows, steps * head_count, seg_length)
    local_peak = jnp.max(jnp.where(valid, scores, NEGATIVE), axis=-1)
    weights = jnp.where(valid, jnp.exp(scores - local_peak[:, :, None]), 0.0)
    local_total = jnp.sum(weights, axis=-1)
    local_weighted = jnp.einsum(
        "gqs,gsd->gqd", weights, value_rows, preferred_element_type=jnp.float32
    )

    packed = jnp.concatenate(
        [local_peak[:, :, None], local_total[:, :, None], local_weighted], axis=-1
    )
    packed = merge_over(packed, "seq", seq_size)
    mixed = packed[:, :, 2:] / packed[:, :, 1:2]
    mixed = (
        mixed.reshape(group_rows, steps, model_width)
        .transpose(1, 0, 2)
        .astype(jnp.bfloat16)
    )
    own_mixed = lax.dynamic_slice_in_dim(mixed, shard_index * slice_width, slice_width, 2)
    every_mixed = gather_blocks(own_mixed, "req", req_size)
    mixed_part = every_mixed.transpose(1, 0, 2, 3).reshape(rows, slice_width)

    hidden = jax.nn.gelu(up_part, approximate=False).astype(jnp.bfloat16)
    partial_sum = jnp.dot(mixed_part, w_out, preferred_element_type=jnp.float32) + jnp.dot(
        hidden, w_down, preferred_element_type=jnp.float32
    )
    inverse = (
        jnp.zeros((total,), jnp.int32).at[placement].set(jnp.arange(total, dtype=jnp.int32))
    )
    chunks = seq_size // req_size
    by_request = jnp.take(partial_sum.reshape(steps, total, part_width), inverse, axis=1)
    blocks = by_request.reshape(steps, req_size, group_rows, chunks, slice_width)
    blocks = blocks.transpose(1, 3, 0, 2, 4).reshape(seq_size, steps, group_rows, slice_width)
    reduced = scatter_sum(blocks, "seq", seq_size)
    routes = []
    for source_group in range(req_size):
        for block in range(seq_size):
            target = (block // chunks) * seq_size + source_group * chunks + block % chunks
            routes.append((source_group * seq_size + block, target))
    own_branch = lax.ppermute(reduced, ALL, routes)
    new_states = (states.astype(jnp.float32) + own_branch).astype(jnp.bfloat16)
    return (new_states, cache_now)


def solution(mesh):
    in_specs = (
        P(None, "req", "seq"),
        P("req", "seq", None),
        P(),
        P(),
        P(),
        P(),
        P("req", "seq"),
        P("req", None),
        P("seq", "req"),
        P("req", "seq"),
        P("seq", "req"),
    )
    out_specs = (P(None, "req", "seq"), P("req", "seq", None))
    return jax.shard_map(shards, mesh=mesh, in_specs=in_specs, out_specs=out_specs, check_vma=False)
```

```python
import jax
import jax.numpy as jnp
from jax import lax
from jax.sharding import PartitionSpec as P


EPSILON = 1e-05
NEGATIVE = -1e30
ALL = ("req", "seq")


def xor_pairs(size, bit):
    return [(index, index ^ bit) for index in range(size)]


def gather_blocks(block, axis, size):
    index = lax.axis_index(axis)
    levels = size.bit_length() - 1
    blocks = block.reshape((1,) * levels + block.shape)
    for level in range(levels):
        bit = 2 ** (levels - 1 - level)
        other = lax.ppermute(blocks, axis, xor_pairs(size, bit))
        low = (index // bit) % 2 == 0
        blocks = jnp.where(
            low,
            jnp.concatenate([blocks, other], axis=level),
            jnp.concatenate([other, blocks], axis=level),
        )
    return blocks.reshape((size,) + block.shape)


def sum_over(value, axis, size):
    bit = 1
    while bit < size:
        value = value + lax.ppermute(value, axis, xor_pairs(size, bit))
        bit *= 2
    return value


def scatter_sum(blocks, axis, size):
    index = lax.axis_index(axis)
    levels = size.bit_length() - 1
    blocks = blocks.reshape((2,) * levels + blocks.shape[1:])
    for level in range(levels):
        bit = 2 ** level
        place = levels - 1 - level
        high = (index // bit) % 2 == 1
        lower = lax.index_in_dim(blocks, 0, place, keepdims=False)
        upper = lax.index_in_dim(blocks, 1, place, keepdims=False)
        keep = jnp.where(high, upper, lower)
        send = jnp.where(high, lower, upper)
        blocks = keep + lax.ppermute(send, axis, xor_pairs(size, bit))
    return blocks


def split_exact(value):
    high = lax.reduce_precision(value, exponent_bits=8, mantissa_bits=7)
    rest = value - high
    middle = lax.reduce_precision(rest, exponent_bits=8, mantissa_bits=7)
    low = rest - middle
    return [part.astype(jnp.bfloat16) for part in (high, middle, low)]


def join_exact(pieces):
    pieces = pieces.astype(jnp.float32)
    return (pieces[..., 0] + pieces[..., 1]) + pieces[..., 2]


def merge_over(peak, total, weighted, axis, size):
    bit = 1
    while bit < size:
        sent = jnp.concatenate(
            [jnp.stack(split_exact(peak) + split_exact(total), axis=-1), weighted.astype(jnp.bfloat16)],
            axis=-1,
        )
        other = lax.ppermute(sent, axis, xor_pairs(size, bit))
        peak_second = join_exact(other[..., 0:3])
        total_second = join_exact(other[..., 3:6])
        weighted_second = other[..., 6:].astype(jnp.float32)
        merged_peak = jnp.maximum(peak, peak_second)
        scale_first = jnp.exp(peak - merged_peak)
        scale_second = jnp.exp(peak_second - merged_peak)
        total = total * scale_first + total_second * scale_second
        weighted = weighted * scale_first[..., None] + weighted_second * scale_second[..., None]
        peak = merged_peak
        bit *= 2
    return peak, total, weighted


def layer_norm(row_block, norm_gain, norm_bias):
    values = row_block.astype(jnp.float32)
    average = jnp.mean(values, axis=-1, keepdims=True)
    centered = values - average
    spread = jnp.mean(centered * centered, axis=-1, keepdims=True)
    scaled = centered * lax.rsqrt(spread + EPSILON)
    return (scaled * norm_gain.astype(jnp.float32) + norm_bias.astype(jnp.float32)).astype(
        jnp.bfloat16
    )


def rotate(vectors, positions):
    head_width = vectors.shape[-1]
    half_width = head_width // 2
    frequency = 10000.0 ** (-(jnp.arange(half_width, dtype=jnp.float32) * 2.0) / head_width)
    angles = positions.astype(jnp.float32)[:, None] * frequency[None, :]
    cosine = jnp.concatenate([jnp.cos(angles), jnp.cos(angles)], axis=-1)[:, None, :]
    sine_wave = jnp.concatenate([jnp.sin(angles), jnp.sin(angles)], axis=-1)[:, None, :]
    turned = jnp.concatenate([-vectors[..., half_width:], vectors[..., :half_width]], axis=-1)
    return vectors * cosine + turned * sine_wave


def shards(
    states,
    kv_cache,
    lengths,
    placement,
    norm_gain,
    norm_bias,
    w_query,
    w_keyval,
    w_out,
    w_up,
    w_down,
):
    steps = states.shape[0]
    group_rows = kv_cache.shape[0]
    seg_length = kv_cache.shape[1]
    head_width = kv_cache.shape[2] // 2
    model_width = norm_gain.shape[0]
    head_count = model_width // head_width
    slice_width = states.shape[2]
    part_width = w_query.shape[0]
    total = placement.shape[0]
    req_size = total // group_rows
    seq_size = model_width // slice_width
    rows = steps * total
    group_index = lax.axis_index("req")
    shard_index = lax.axis_index("seq")

    own_requests = lax.dynamic_slice_in_dim(placement, group_index * group_rows, group_rows, 0)
    slot_lengths = jnp.take(lengths, own_requests)
    step_offsets = jnp.arange(steps, dtype=jnp.int32)
    positions = slot_lengths[None, :] + step_offsets[:, None]

    every = gather_blocks(gather_blocks(states, "req", req_size), "seq", seq_size)
    every = every.transpose(2, 1, 3, 0, 4).reshape(steps, total, model_width)
    current_all = jnp.take(every, placement, axis=1)
    normed = layer_norm(current_all.reshape(rows, model_width), norm_gain, norm_bias)
    normed_part = lax.dynamic_slice_in_dim(normed, group_index * part_width, part_width, 1)

    part_query = jnp.dot(normed_part, w_query, preferred_element_type=jnp.float32)
    part_keyval = jnp.dot(normed_part, w_keyval, preferred_element_type=jnp.float32)
    first = sum_over(jnp.concatenate([part_query, part_keyval], axis=1), "req", req_size)
    query_raw = first[:, :slice_width].astype(jnp.bfloat16).reshape(steps, total, slice_width)
    keyval = first[:, slice_width:].reshape(steps, total, 2 * head_width)
    part_up = jnp.dot(normed_part, w_up, preferred_element_type=jnp.float32)
    up_part = sum_over(part_up, "req", req_size)
    hidden = jax.nn.gelu(up_part, approximate=False).astype(jnp.bfloat16)
    down_part = jnp.dot(hidden, w_down, preferred_element_type=jnp.float32)

    own_query = lax.dynamic_slice_in_dim(query_raw, group_index * group_rows, group_rows, 1)
    query_all = gather_blocks(own_query, "seq", seq_size)
    query_all = query_all.transpose(1, 2, 0, 3).reshape(steps, group_rows, model_width)
    flat_positions = positions.reshape(-1)
    query_rows = rotate(
        query_all.astype(jnp.float32).reshape(steps * group_rows, head_count, head_width),
        flat_positions,
    ).astype(jnp.bfloat16)
    own_keyval = lax.dynamic_slice_in_dim(keyval, group_index * group_rows, group_rows, 1)
    own_keyval = own_keyval.reshape(steps * group_rows, 2 * head_width)
    new_key = rotate(own_keyval[:, None, :head_width], flat_positions)[:, 0, :]
    new_entry = jnp.concatenate([new_key, own_keyval[:, head_width:]], axis=-1).astype(jnp.bfloat16)
    new_entry = new_entry.reshape(steps, group_rows, 2 * head_width)

    local_slots = jnp.arange(seg_length, dtype=jnp.int32)
    global_positions = shard_index * seg_length + local_slots
    cache_now = kv_cache
    for step_index in range(steps):
        write_mask = global_positions[None, :] == positions[step_index][:, None]
        cache_now = jnp.where(write_mask[:, :, None], new_entry[step_index][:, None, :], cache_now)

    key_rows = cache_now[:, :, :head_width]
    value_rows = cache_now[:, :, head_width:]
    query_heads = (
        query_rows.reshape(steps, group_rows, head_count, head_width)
        .transpose(1, 0, 2, 3)
        .reshape(group_rows, steps * head_count, head_width)
    )
    scores = jnp.einsum(
        "gqd,gsd->gqs", query_heads, key_rows, preferred_element_type=jnp.float32
    ) * head_width ** (-0.5)
    valid = global_positions[None, None, :] <= positions.T[:, :, None]
    valid = jnp.broadcast_to(
        valid[:, :, None, :], (group_rows, steps, head_count, seg_length)
    ).reshape(group_rows, steps * head_count, seg_length)
    local_peak = jnp.max(jnp.where(valid, scores, NEGATIVE), axis=-1)
    weights = jnp.where(valid, jnp.exp(scores - local_peak[:, :, None]), 0.0)
    local_total = jnp.sum(weights, axis=-1)
    local_weighted = jnp.einsum(
        "gqs,gsd->gqd", weights, value_rows, preferred_element_type=jnp.float32
    )

    _, merged_total, merged_weighted = merge_over(
        local_peak, local_total, local_weighted, "seq", seq_size
    )
    mixed = merged_weighted / merged_total[:, :, None]
    mixed = (
        mixed.reshape(group_rows, steps, model_width)
        .transpose(1, 0, 2)
        .astype(jnp.bfloat16)
    )
    own_mixed = lax.dynamic_slice_in_dim(mixed, shard_index * slice_width, slice_width, 2)
    every_mixed = gather_blocks(own_mixed, "req", req_size)
    mixed_part = every_mixed.transpose(1, 0, 2, 3).reshape(rows, slice_width)

    partial_sum = jnp.dot(mixed_part, w_out, preferred_element_type=jnp.float32) + down_part
    inverse = (
        jnp.zeros((total,), jnp.int32).at[placement].set(jnp.arange(total, dtype=jnp.int32))
    )
    chunks = seq_size // req_size
    by_request = jnp.take(partial_sum.reshape(steps, total, part_width), inverse, axis=1)
    blocks = by_request.reshape(steps, req_size, group_rows, chunks, slice_width)
    blocks = blocks.transpose(1, 3, 0, 2, 4).reshape(seq_size, steps, group_rows, slice_width)
    reduced = scatter_sum(blocks, "seq", seq_size)
    routes = []
    for source_group in range(req_size):
        for block in range(seq_size):
            target = (block // chunks) * seq_size + source_group * chunks + block % chunks
            routes.append((source_group * seq_size + block, target))
    own_branch = lax.ppermute(reduced, ALL, routes)
    new_states = (states.astype(jnp.float32) + own_branch).astype(jnp.bfloat16)
    return (new_states, cache_now)


def solution(mesh):
    in_specs = (
        P(None, "req", "seq"),
        P("req", "seq", None),
        P(),
        P(),
        P(),
        P(),
        P("req", "seq"),
        P("req", None),
        P("seq", "req"),
        P("req", "seq"),
        P("seq", "req"),
    )
    out_specs = (P(None, "req", "seq"), P("req", "seq", None))
    return jax.shard_map(shards, mesh=mesh, in_specs=in_specs, out_specs=out_specs, check_vma=False)
```

```python
import jax
import jax.numpy as jnp
from jax import lax
from jax.sharding import PartitionSpec as P


EPSILON = 1e-05
NEGATIVE = -1e30
ALL = ("req", "seq")


def xor_pairs(size, bit):
    return [(index, index ^ bit) for index in range(size)]


def gather_xor(block, axis, size):
    levels = size.bit_length() - 1
    stacked = block
    for level in range(levels):
        bit = 2 ** (levels - 1 - level)
        stacked = jnp.stack([stacked, lax.ppermute(stacked, axis, xor_pairs(size, bit))])
    return stacked.reshape((size,) + block.shape)


def xor_slot(offset, size):
    levels = size.bit_length() - 1
    position = jnp.zeros_like(offset)
    for level in range(levels):
        bit = 2 ** (levels - 1 - level)
        position = position + ((offset // bit) % 2) * (2 ** level)
    return position


def sum_over(value, axis, size):
    bit = 1
    while bit < size:
        value = value + lax.ppermute(value, axis, xor_pairs(size, bit))
        bit *= 2
    return value


def scatter_sum(blocks, axis, size):
    index = lax.axis_index(axis)
    levels = size.bit_length() - 1
    blocks = blocks.reshape((2,) * levels + blocks.shape[1:])
    for level in range(levels):
        bit = 2 ** level
        place = levels - 1 - level
        high = (index // bit) % 2 == 1
        lower = lax.index_in_dim(blocks, 0, place, keepdims=False)
        upper = lax.index_in_dim(blocks, 1, place, keepdims=False)
        keep = jnp.where(high, upper, lower)
        send = jnp.where(high, lower, upper)
        blocks = keep + lax.ppermute(send, axis, xor_pairs(size, bit))
    return blocks


def split_exact(value):
    high = lax.reduce_precision(value, exponent_bits=8, mantissa_bits=7)
    rest = value - high
    middle = lax.reduce_precision(rest, exponent_bits=8, mantissa_bits=7)
    low = rest - middle
    return [part.astype(jnp.bfloat16) for part in (high, middle, low)]


def join_exact(pieces):
    pieces = pieces.astype(jnp.float32)
    return (pieces[..., 0] + pieces[..., 1]) + pieces[..., 2]


def merge_over(peak, total, weighted, axis, size, carried):
    bit = 1
    while bit < size:
        if bit == 4:
            carried, peak, total, weighted = lax.optimization_barrier(
                (carried, peak, total, weighted)
            )
        sent = jnp.concatenate(
            [jnp.stack(split_exact(peak) + split_exact(total), axis=-1), weighted.astype(jnp.bfloat16)],
            axis=-1,
        )
        other = lax.ppermute(sent, axis, xor_pairs(size, bit))
        peak_second = join_exact(other[..., 0:3])
        total_second = join_exact(other[..., 3:6])
        weighted_second = other[..., 6:].astype(jnp.float32)
        merged_peak = jnp.maximum(peak, peak_second)
        scale_first = jnp.exp(peak - merged_peak)
        scale_second = jnp.exp(peak_second - merged_peak)
        total = total * scale_first + total_second * scale_second
        weighted = weighted * scale_first[..., None] + weighted_second * scale_second[..., None]
        peak = merged_peak
        bit *= 2
    return peak, total, weighted, carried


def layer_norm(row_block, norm_gain, norm_bias):
    values = row_block.astype(jnp.float32)
    average = jnp.mean(values, axis=-1, keepdims=True)
    centered = values - average
    spread = jnp.mean(centered * centered, axis=-1, keepdims=True)
    scaled = centered * lax.rsqrt(spread + EPSILON)
    return (scaled * norm_gain.astype(jnp.float32) + norm_bias.astype(jnp.float32)).astype(
        jnp.bfloat16
    )


def rotate(vectors, positions):
    head_width = vectors.shape[-1]
    half_width = head_width // 2
    frequency = 10000.0 ** (-(jnp.arange(half_width, dtype=jnp.float32) * 2.0) / head_width)
    angles = positions.astype(jnp.float32)[:, None] * frequency[None, :]
    cosine = jnp.concatenate([jnp.cos(angles), jnp.cos(angles)], axis=-1)[:, None, :]
    sine_wave = jnp.concatenate([jnp.sin(angles), jnp.sin(angles)], axis=-1)[:, None, :]
    turned = jnp.concatenate([-vectors[..., half_width:], vectors[..., :half_width]], axis=-1)
    return vectors * cosine + turned * sine_wave


def shards(
    states,
    kv_cache,
    lengths,
    placement,
    norm_gain,
    norm_bias,
    w_query,
    w_keyval,
    w_out,
    w_up,
    w_down,
):
    steps = states.shape[0]
    group_rows = kv_cache.shape[0]
    seg_length = kv_cache.shape[1]
    head_width = kv_cache.shape[2] // 2
    model_width = norm_gain.shape[0]
    head_count = model_width // head_width
    slice_width = states.shape[2]
    part_width = w_query.shape[0]
    total = placement.shape[0]
    req_size = total // group_rows
    seq_size = model_width // slice_width
    rows = steps * total
    group_index = lax.axis_index("req")
    shard_index = lax.axis_index("seq")

    request_ids = jnp.arange(total, dtype=jnp.int32)
    serves = placement[:, None] == request_ids[None, :]
    own_serves = lax.dynamic_slice_in_dim(serves, group_index * group_rows, group_rows, 0)
    slot_lengths = jnp.sum(jnp.where(own_serves, lengths[None, :], 0), axis=1)
    step_offsets = jnp.arange(steps, dtype=jnp.int32)
    positions = slot_lengths[None, :] + step_offsets[:, None]
    seq_ids = jnp.arange(seq_size, dtype=jnp.int32)
    req_ids = jnp.arange(req_size, dtype=jnp.int32)
    seq_slots = xor_slot(shard_index ^ seq_ids, seq_size)
    req_slots = xor_slot(group_index ^ req_ids, req_size)

    every = gather_xor(gather_xor(states, "req", req_size), "seq", seq_size)
    slot_req = xor_slot(group_index ^ (placement // group_rows), req_size)
    current_all = every[seq_slots[None, :], slot_req[:, None], :, (placement % group_rows)[:, None], :]
    current_all = current_all.transpose(2, 0, 1, 3).reshape(steps, total, model_width)
    normed = layer_norm(current_all.reshape(rows, model_width), norm_gain, norm_bias)
    normed_part = lax.dynamic_slice_in_dim(normed, group_index * part_width, part_width, 1)

    part_query = jnp.dot(normed_part, w_query, preferred_element_type=jnp.float32)
    part_keyval = jnp.dot(normed_part, w_keyval, preferred_element_type=jnp.float32)
    first = sum_over(jnp.concatenate([part_query, part_keyval], axis=1), "req", req_size)
    part_up = jnp.dot(normed_part, w_up, preferred_element_type=jnp.float32)
    first, part_up = lax.optimization_barrier((first, part_up))
    query_raw = first[:, :slice_width].astype(jnp.bfloat16).reshape(steps, total, slice_width)
    keyval = first[:, slice_width:].reshape(steps, total, 2 * head_width)
    up_part = sum_over(part_up, "req", req_size)
    hidden = jax.nn.gelu(up_part, approximate=False).astype(jnp.bfloat16)
    down_part = jnp.dot(hidden, w_down, preferred_element_type=jnp.float32)

    own_query = lax.dynamic_slice_in_dim(query_raw, group_index * group_rows, group_rows, 1)
    query_all = jnp.take(gather_xor(own_query, "seq", seq_size), seq_slots, axis=0)
    query_all = query_all.transpose(1, 2, 0, 3).reshape(steps, group_rows, model_width)
    flat_positions = positions.reshape(-1)
    query_rows = rotate(
        query_all.astype(jnp.float32).reshape(steps * group_rows, head_count, head_width),
        flat_positions,
    ).astype(jnp.bfloat16)
    own_keyval = lax.dynamic_slice_in_dim(keyval, group_index * group_rows, group_rows, 1)
    own_keyval = own_keyval.reshape(steps * group_rows, 2 * head_width)
    new_key = rotate(own_keyval[:, None, :head_width], flat_positions)[:, 0, :]
    new_entry = jnp.concatenate([new_key, own_keyval[:, head_width:]], axis=-1).astype(jnp.bfloat16)
    new_entry = new_entry.reshape(steps, group_rows, 2 * head_width)

    local_slots = jnp.arange(seg_length, dtype=jnp.int32)
    global_positions = shard_index * seg_length + local_slots
    cache_now = kv_cache
    for step_index in range(steps):
        write_mask = global_positions[None, :] == positions[step_index][:, None]
        cache_now = jnp.where(write_mask[:, :, None], new_entry[step_index][:, None, :], cache_now)

    key_rows = cache_now[:, :, :head_width]
    value_rows = cache_now[:, :, head_width:]
    query_heads = (
        query_rows.reshape(steps, group_rows, head_count, head_width)
        .transpose(1, 0, 2, 3)
        .reshape(group_rows, steps * head_count, head_width)
    )
    scores = jnp.einsum(
        "gqd,gsd->gqs", query_heads, key_rows, preferred_element_type=jnp.float32
    ) * head_width ** (-0.5)
    valid = global_positions[None, None, :] <= positions.T[:, :, None]
    valid = jnp.broadcast_to(
        valid[:, :, None, :], (group_rows, steps, head_count, seg_length)
    ).reshape(group_rows, steps * head_count, seg_length)
    local_peak = jnp.max(jnp.where(valid, scores, NEGATIVE), axis=-1)
    weights = jnp.where(valid, jnp.exp(scores - local_peak[:, :, None]), 0.0)
    local_total = jnp.sum(weights, axis=-1)
    local_weighted = jnp.einsum(
        "gqs,gsd->gqd", weights, value_rows, preferred_element_type=jnp.float32
    )

    _, merged_total, merged_weighted, down_part = merge_over(
        local_peak, local_total, local_weighted, "seq", seq_size, down_part
    )
    mixed = merged_weighted / merged_total[:, :, None]
    mixed = (
        mixed.reshape(group_rows, steps, model_width)
        .transpose(1, 0, 2)
        .astype(jnp.bfloat16)
    )
    own_mixed = lax.dynamic_slice_in_dim(mixed, shard_index * slice_width, slice_width, 2)
    every_mixed = jnp.take(gather_xor(own_mixed, "req", req_size), req_slots, axis=0)
    mixed_part = every_mixed.transpose(1, 0, 2, 3).reshape(rows, slice_width)

    partial_sum = jnp.dot(mixed_part, w_out, preferred_element_type=jnp.float32) + down_part
    inverse = jnp.sum(jnp.where(serves, request_ids[:, None], 0), axis=0)
    chunks = seq_size // req_size
    by_request = jnp.take(partial_sum.reshape(steps, total, part_width), inverse, axis=1)
    blocks = by_request.reshape(steps, req_size, group_rows, chunks, slice_width)
    blocks = blocks.transpose(1, 3, 0, 2, 4).reshape(seq_size, steps, group_rows, slice_width)
    reduced = scatter_sum(blocks, "seq", seq_size)
    routes = []
    for source_group in range(req_size):
        for block in range(seq_size):
            target = (block // chunks) * seq_size + source_group * chunks + block % chunks
            routes.append((source_group * seq_size + block, target))
    own_branch = lax.ppermute(reduced, ALL, routes)
    new_states = (states.astype(jnp.float32) + own_branch).astype(jnp.bfloat16)
    return (new_states, cache_now)


def solution(mesh):
    in_specs = (
        P(None, "req", "seq"),
        P("req", "seq", None),
        P(),
        P(),
        P(),
        P(),
        P("req", "seq"),
        P("req", None),
        P("seq", "req"),
        P("req", "seq"),
        P("seq", "req"),
    )
    out_specs = (P(None, "req", "seq"), P("req", "seq", None))
    return jax.shard_map(shards, mesh=mesh, in_specs=in_specs, out_specs=out_specs, check_vma=False)
```

```python
import jax
import jax.numpy as jnp
from jax import lax
from jax.sharding import PartitionSpec as P


EPSILON = 1e-05
NEGATIVE = -1e30
ALL = ("req", "seq")


def xor_pairs(size, bit):
    return [(index, index ^ bit) for index in range(size)]


def gather_xor(block, axis, size, riders=None):
    levels = size.bit_length() - 1
    riders = dict(riders or {})
    stacked = block
    for level in range(levels):
        bit = 2 ** (levels - 1 - level)
        stacked = jnp.stack([stacked, lax.ppermute(stacked, axis, xor_pairs(size, bit))])
        if level in riders:
            stacked, riders[level] = lax.optimization_barrier((stacked, riders[level]))
    return stacked.reshape((size,) + block.shape), riders


def xor_slot(offset, size):
    levels = size.bit_length() - 1
    position = jnp.zeros_like(offset)
    for level in range(levels):
        bit = 2 ** (levels - 1 - level)
        position = position + ((offset // bit) % 2) * (2 ** level)
    return position


def sum_over(value, axis, size):
    bit = 1
    while bit < size:
        value = value + lax.ppermute(value, axis, xor_pairs(size, bit))
        bit *= 2
    return value


def scatter_sum(blocks, axis, size):
    index = lax.axis_index(axis)
    levels = size.bit_length() - 1
    blocks = blocks.reshape((2,) * levels + blocks.shape[1:])
    for level in range(levels):
        bit = 2 ** level
        place = levels - 1 - level
        high = (index // bit) % 2 == 1
        lower = lax.index_in_dim(blocks, 0, place, keepdims=False)
        upper = lax.index_in_dim(blocks, 1, place, keepdims=False)
        keep = jnp.where(high, upper, lower)
        send = jnp.where(high, lower, upper)
        blocks = keep + lax.ppermute(send, axis, xor_pairs(size, bit))
    return blocks


def split_exact(value):
    high = lax.reduce_precision(value, exponent_bits=8, mantissa_bits=7)
    rest = value - high
    middle = lax.reduce_precision(rest, exponent_bits=8, mantissa_bits=7)
    low = rest - middle
    return [part.astype(jnp.bfloat16) for part in (high, middle, low)]


def join_exact(pieces):
    pieces = pieces.astype(jnp.float32)
    return (pieces[..., 0] + pieces[..., 1]) + pieces[..., 2]


def merge_over(peak, total, weighted, axis, size, carried):
    bit = 1
    while bit < size:
        if bit == 4:
            carried, peak, total, weighted = lax.optimization_barrier(
                (carried, peak, total, weighted)
            )
        sent = jnp.concatenate(
            [jnp.stack(split_exact(peak) + split_exact(total), axis=-1), weighted.astype(jnp.bfloat16)],
            axis=-1,
        )
        other = lax.ppermute(sent, axis, xor_pairs(size, bit))
        peak_second = join_exact(other[..., 0:3])
        total_second = join_exact(other[..., 3:6])
        weighted_second = other[..., 6:].astype(jnp.float32)
        merged_peak = jnp.maximum(peak, peak_second)
        scale_first = jnp.exp(peak - merged_peak)
        scale_second = jnp.exp(peak_second - merged_peak)
        total = total * scale_first + total_second * scale_second
        weighted = weighted * scale_first[..., None] + weighted_second * scale_second[..., None]
        peak = merged_peak
        bit *= 2
    return peak, total, weighted, carried


def layer_norm(row_block, norm_gain, norm_bias):
    values = row_block.astype(jnp.float32)
    average = jnp.mean(values, axis=-1, keepdims=True)
    centered = values - average
    spread = jnp.mean(centered * centered, axis=-1, keepdims=True)
    scaled = centered * lax.rsqrt(spread + EPSILON)
    return (scaled * norm_gain.astype(jnp.float32) + norm_bias.astype(jnp.float32)).astype(
        jnp.bfloat16
    )


def rotate(vectors, positions):
    head_width = vectors.shape[-1]
    half_width = head_width // 2
    frequency = 10000.0 ** (-(jnp.arange(half_width, dtype=jnp.float32) * 2.0) / head_width)
    angles = positions.astype(jnp.float32)[:, None] * frequency[None, :]
    cosine = jnp.concatenate([jnp.cos(angles), jnp.cos(angles)], axis=-1)[:, None, :]
    sine_wave = jnp.concatenate([jnp.sin(angles), jnp.sin(angles)], axis=-1)[:, None, :]
    turned = jnp.concatenate([-vectors[..., half_width:], vectors[..., :half_width]], axis=-1)
    return vectors * cosine + turned * sine_wave


def shards(
    states,
    kv_cache,
    lengths,
    placement,
    norm_gain,
    norm_bias,
    w_query,
    w_keyval,
    w_out,
    w_up,
    w_down,
):
    steps = states.shape[0]
    group_rows = kv_cache.shape[0]
    seg_length = kv_cache.shape[1]
    head_width = kv_cache.shape[2] // 2
    model_width = norm_gain.shape[0]
    head_count = model_width // head_width
    slice_width = states.shape[2]
    part_width = w_query.shape[0]
    total = placement.shape[0]
    req_size = total // group_rows
    seq_size = model_width // slice_width
    rows = steps * total
    group_index = lax.axis_index("req")
    shard_index = lax.axis_index("seq")

    seq_ids = jnp.arange(seq_size, dtype=jnp.int32)
    req_ids = jnp.arange(req_size, dtype=jnp.int32)
    seq_slots = xor_slot(shard_index ^ seq_ids, seq_size)
    req_slots = xor_slot(group_index ^ req_ids, req_size)

    by_request, _ = gather_xor(states, "req", req_size)
    every, riders = gather_xor(by_request, "seq", seq_size, {0: (norm_gain, norm_bias)})
    norm_gain, norm_bias = riders[0]
    every = jnp.take(jnp.take(every, seq_slots, axis=0), req_slots, axis=1)
    current_all = every.transpose(2, 1, 3, 0, 4).reshape(steps, total, model_width)
    normed = layer_norm(current_all.reshape(rows, model_width), norm_gain, norm_bias)
    normed_part = lax.dynamic_slice_in_dim(normed, group_index * part_width, part_width, 1)

    part_query = jnp.dot(normed_part, w_query, preferred_element_type=jnp.float32)
    part_keyval = jnp.dot(normed_part, w_keyval, preferred_element_type=jnp.float32)
    first = sum_over(jnp.concatenate([part_query, part_keyval], axis=1), "req", req_size)
    part_up = jnp.dot(normed_part, w_up, preferred_element_type=jnp.float32)
    first, part_up = lax.optimization_barrier((first, part_up))
    query_raw = first[:, :slice_width].astype(jnp.bfloat16).reshape(steps, total, slice_width)
    keyval = first[:, slice_width:].reshape(steps, total, 2 * head_width)
    up_part = sum_over(part_up, "req", req_size)
    hidden = jax.nn.gelu(up_part, approximate=False).astype(jnp.bfloat16)
    down_part = jnp.dot(hidden, w_down, preferred_element_type=jnp.float32)

    request_ids = jnp.arange(total, dtype=jnp.int32)
    own_requests = lax.dynamic_slice_in_dim(placement, group_index * group_rows, group_rows, 0)
    slot_lengths = jnp.take(lengths, own_requests, mode="clip")
    step_offsets = jnp.arange(steps, dtype=jnp.int32)
    positions = slot_lengths[None, :] + step_offsets[:, None]
    own_query = jnp.take(query_raw, own_requests, axis=1, mode="clip")
    query_all, riders = gather_xor(own_query, "seq", seq_size, {0: kv_cache})
    kv_cache = riders[0]
    query_all = jnp.take(query_all, seq_slots, axis=0)
    query_all = query_all.transpose(1, 2, 0, 3).reshape(steps, group_rows, model_width)
    flat_positions = positions.reshape(-1)
    query_rows = rotate(
        query_all.astype(jnp.float32).reshape(steps * group_rows, head_count, head_width),
        flat_positions,
    ).astype(jnp.bfloat16)
    own_keyval = jnp.take(keyval, own_requests, axis=1, mode="clip")
    own_keyval = own_keyval.reshape(steps * group_rows, 2 * head_width)
    new_key = rotate(own_keyval[:, None, :head_width], flat_positions)[:, 0, :]
    new_entry = jnp.concatenate([new_key, own_keyval[:, head_width:]], axis=-1).astype(jnp.bfloat16)
    new_entry = new_entry.reshape(steps, group_rows, 2 * head_width)

    local_slots = jnp.arange(seg_length, dtype=jnp.int32)
    global_positions = shard_index * seg_length + local_slots
    cache_now = kv_cache
    for step_index in range(steps):
        write_mask = global_positions[None, :] == positions[step_index][:, None]
        cache_now = jnp.where(write_mask[:, :, None], new_entry[step_index][:, None, :], cache_now)

    key_rows = cache_now[:, :, :head_width]
    value_rows = cache_now[:, :, head_width:]
    query_heads = (
        query_rows.reshape(steps, group_rows, head_count, head_width)
        .transpose(1, 0, 2, 3)
        .reshape(group_rows, steps * head_count, head_width)
    )
    scores = jnp.einsum(
        "gqd,gsd->gqs", query_heads, key_rows, preferred_element_type=jnp.float32
    ) * head_width ** (-0.5)
    valid = global_positions[None, None, :] <= positions.T[:, :, None]
    valid = jnp.broadcast_to(
        valid[:, :, None, :], (group_rows, steps, head_count, seg_length)
    ).reshape(group_rows, steps * head_count, seg_length)
    local_peak = jnp.max(jnp.where(valid, scores, NEGATIVE), axis=-1)
    weights = jnp.where(valid, jnp.exp(scores - local_peak[:, :, None]), 0.0)
    local_total = jnp.sum(weights, axis=-1)
    local_weighted = jnp.einsum(
        "gqs,gsd->gqd", weights, value_rows, preferred_element_type=jnp.float32
    )

    _, merged_total, merged_weighted, down_part = merge_over(
        local_peak, local_total, local_weighted, "seq", seq_size, down_part
    )
    mixed = merged_weighted / merged_total[:, :, None]
    mixed = (
        mixed.reshape(group_rows, steps, model_width)
        .transpose(1, 0, 2)
        .astype(jnp.bfloat16)
    )
    own_mixed = lax.dynamic_slice_in_dim(mixed, shard_index * slice_width, slice_width, 2)
    every_mixed = jnp.take(gather_xor(own_mixed, "req", req_size)[0], req_slots, axis=0)
    serves = placement[:, None] == request_ids[None, :]
    inverse = jnp.sum(jnp.where(serves, request_ids[:, None], 0), axis=0)
    mixed_part = every_mixed.transpose(1, 0, 2, 3).reshape(steps, total, slice_width)
    mixed_part = jnp.take(mixed_part, inverse, axis=1, mode="clip").reshape(rows, slice_width)

    partial_sum = jnp.dot(mixed_part, w_out, preferred_element_type=jnp.float32) + down_part
    chunks = seq_size // req_size
    by_request = partial_sum.reshape(steps, total, part_width)
    blocks = by_request.reshape(steps, req_size, group_rows, chunks, slice_width)
    blocks = blocks.transpose(1, 3, 0, 2, 4).reshape(seq_size, steps, group_rows, slice_width)
    reduced = scatter_sum(blocks, "seq", seq_size)
    routes = []
    for source_group in range(req_size):
        for block in range(seq_size):
            target = (block // chunks) * seq_size + source_group * chunks + block % chunks
            routes.append((source_group * seq_size + block, target))
    own_branch = lax.ppermute(reduced, ALL, routes)
    new_states = (states.astype(jnp.float32) + own_branch).astype(jnp.bfloat16)
    return (new_states, cache_now)


def solution(mesh):
    in_specs = (
        P(None, "req", "seq"),
        P("req", "seq", None),
        P(),
        P(),
        P(),
        P(),
        P("req", "seq"),
        P("req", None),
        P("seq", "req"),
        P("req", "seq"),
        P("seq", "req"),
    )
    out_specs = (P(None, "req", "seq"), P("req", "seq", None))
    return jax.shard_map(shards, mesh=mesh, in_specs=in_specs, out_specs=out_specs, check_vma=False)
```

```python
import jax
import jax.numpy as jnp
from jax import lax
from jax.sharding import PartitionSpec as P


EPSILON = 1e-05
NEGATIVE = -1e30
ALL = ("req", "seq")


def xor_pairs(size, bit):
    return [(index, index ^ bit) for index in range(size)]


def gather_xor(block, axis, size, riders=None):
    levels = size.bit_length() - 1
    riders = dict(riders or {})
    stacked = block
    for level in range(levels):
        bit = 2 ** (levels - 1 - level)
        stacked = jnp.stack([stacked, lax.ppermute(stacked, axis, xor_pairs(size, bit))])
        if level in riders:
            stacked, riders[level] = lax.optimization_barrier((stacked, riders[level]))
    return stacked.reshape((size,) + block.shape), riders


def xor_slot(offset, size):
    levels = size.bit_length() - 1
    position = jnp.zeros_like(offset)
    for level in range(levels):
        bit = 2 ** (levels - 1 - level)
        position = position + ((offset // bit) % 2) * (2 ** level)
    return position


def sum_over(value, axis, size):
    bit = 1
    while bit < size:
        value = value + lax.ppermute(value, axis, xor_pairs(size, bit))
        bit *= 2
    return value


def scatter_sum(blocks, axis, size):
    index = lax.axis_index(axis)
    levels = size.bit_length() - 1
    blocks = blocks.reshape((2,) * levels + blocks.shape[1:])
    for level in range(levels):
        bit = 2 ** level
        place = levels - 1 - level
        high = (index // bit) % 2 == 1
        lower = lax.index_in_dim(blocks, 0, place, keepdims=False)
        upper = lax.index_in_dim(blocks, 1, place, keepdims=False)
        keep = jnp.where(high, upper, lower)
        send = jnp.where(high, lower, upper)
        blocks = keep + lax.ppermute(send, axis, xor_pairs(size, bit))
    return blocks


def split_exact(value):
    high = lax.reduce_precision(value, exponent_bits=8, mantissa_bits=7)
    rest = value - high
    middle = lax.reduce_precision(rest, exponent_bits=8, mantissa_bits=7)
    low = rest - middle
    return [part.astype(jnp.bfloat16) for part in (high, middle, low)]


def join_exact(pieces):
    pieces = pieces.astype(jnp.float32)
    return (pieces[..., 0] + pieces[..., 1]) + pieces[..., 2]


def merge_over(peak, total, weighted, axis, size, carried):
    bit = 1
    while bit < size:
        if bit == 4:
            carried, peak, total, weighted = lax.optimization_barrier(
                (carried, peak, total, weighted)
            )
        sent = jnp.concatenate(
            [jnp.stack(split_exact(peak) + split_exact(total), axis=-1), weighted.astype(jnp.bfloat16)],
            axis=-1,
        )
        other = lax.ppermute(sent, axis, xor_pairs(size, bit))
        peak_second = join_exact(other[..., 0:3])
        total_second = join_exact(other[..., 3:6])
        weighted_second = other[..., 6:].astype(jnp.float32)
        merged_peak = jnp.maximum(peak, peak_second)
        scale_first = jnp.exp(peak - merged_peak)
        scale_second = jnp.exp(peak_second - merged_peak)
        total = total * scale_first + total_second * scale_second
        weighted = weighted * scale_first[..., None] + weighted_second * scale_second[..., None]
        peak = merged_peak
        bit *= 2
    return peak, total, weighted, carried


def layer_norm(row_block, norm_gain, norm_bias):
    values = row_block.astype(jnp.float32)
    average = jnp.mean(values, axis=-1, keepdims=True)
    centered = values - average
    spread = jnp.mean(centered * centered, axis=-1, keepdims=True)
    scaled = centered * lax.rsqrt(spread + EPSILON)
    return (scaled * norm_gain.astype(jnp.float32) + norm_bias.astype(jnp.float32)).astype(
        jnp.bfloat16
    )


def rotate(vectors, positions):
    head_width = vectors.shape[-1]
    half_width = head_width // 2
    frequency = 10000.0 ** (-(jnp.arange(half_width, dtype=jnp.float32) * 2.0) / head_width)
    angles = positions.astype(jnp.float32)[:, None] * frequency[None, :]
    cosine = jnp.concatenate([jnp.cos(angles), jnp.cos(angles)], axis=-1)[:, None, :]
    sine_wave = jnp.concatenate([jnp.sin(angles), jnp.sin(angles)], axis=-1)[:, None, :]
    turned = jnp.concatenate([-vectors[..., half_width:], vectors[..., :half_width]], axis=-1)
    return vectors * cosine + turned * sine_wave


def shards(
    states,
    kv_cache,
    lengths,
    placement,
    norm_gain,
    norm_bias,
    w_query,
    w_keyval,
    w_out,
    w_up,
    w_down,
):
    steps = states.shape[0]
    group_rows = kv_cache.shape[0]
    seg_length = kv_cache.shape[1]
    head_width = kv_cache.shape[2] // 2
    model_width = norm_gain.shape[0]
    head_count = model_width // head_width
    slice_width = states.shape[2]
    part_width = w_query.shape[0]
    total = placement.shape[0]
    req_size = total // group_rows
    seq_size = model_width // slice_width
    rows = steps * total
    group_index = lax.axis_index("req")
    shard_index = lax.axis_index("seq")

    seq_ids = jnp.arange(seq_size, dtype=jnp.int32)
    req_ids = jnp.arange(req_size, dtype=jnp.int32)
    seq_slots = xor_slot(shard_index ^ seq_ids, seq_size)
    req_slots = xor_slot(group_index ^ req_ids, req_size)

    by_request, _ = gather_xor(states, "req", req_size)
    every, riders = gather_xor(by_request, "seq", seq_size, {0: (norm_gain, norm_bias)})
    norm_gain, norm_bias = riders[0]
    every = every.reshape((seq_size * req_size,) + every.shape[2:])
    every = jnp.take(every, seq_slots[:, None] * req_size + req_slots[None, :], axis=0, mode="clip")
    current_all = every.transpose(2, 1, 3, 0, 4).reshape(steps, total, model_width)
    normed = layer_norm(current_all.reshape(rows, model_width), norm_gain, norm_bias)
    normed_part = lax.dynamic_slice_in_dim(normed, group_index * part_width, part_width, 1)

    part_query = jnp.dot(normed_part, w_query, preferred_element_type=jnp.float32)
    part_keyval = jnp.dot(normed_part, w_keyval, preferred_element_type=jnp.float32)
    first = sum_over(jnp.concatenate([part_query, part_keyval], axis=1), "req", req_size)
    part_up = jnp.dot(normed_part, w_up, preferred_element_type=jnp.float32)
    first, part_up = lax.optimization_barrier((first, part_up))
    request_ids = jnp.arange(total, dtype=jnp.int32)
    own_requests = lax.dynamic_slice_in_dim(placement, group_index * group_rows, group_rows, 0)
    own_serves = own_requests[:, None] == request_ids[None, :]
    slot_lengths = jnp.sum(jnp.where(own_serves, lengths[None, :], 0), axis=1)
    step_offsets = jnp.arange(steps, dtype=jnp.int32)
    positions = slot_lengths[None, :] + step_offsets[:, None]
    own_first = jnp.sum(
        jnp.where(own_serves[None, :, :, None], first.reshape(steps, 1, total, -1), 0.0), axis=2
    )
    own_query = own_first[:, :, :slice_width].astype(jnp.bfloat16)
    own_keyval = own_first[:, :, slice_width:]
    up_part = sum_over(part_up, "req", req_size)
    hidden = jax.nn.gelu(up_part, approximate=False).astype(jnp.bfloat16)
    down_part = jnp.dot(hidden, w_down, preferred_element_type=jnp.float32)

    query_all, riders = gather_xor(own_query, "seq", seq_size, {0: kv_cache})
    kv_cache = riders[0]
    query_all = jnp.take(query_all, seq_slots, axis=0, mode="clip")
    query_all = query_all.transpose(1, 2, 0, 3).reshape(steps, group_rows, model_width)
    flat_positions = positions.reshape(-1)
    query_rows = rotate(
        query_all.astype(jnp.float32).reshape(steps * group_rows, head_count, head_width),
        flat_positions,
    ).astype(jnp.bfloat16)
    own_keyval = own_keyval.reshape(steps * group_rows, 2 * head_width)
    new_key = rotate(own_keyval[:, None, :head_width], flat_positions)[:, 0, :]
    new_entry = jnp.concatenate([new_key, own_keyval[:, head_width:]], axis=-1).astype(jnp.bfloat16)
    new_entry = new_entry.reshape(steps, group_rows, 2 * head_width)

    local_slots = jnp.arange(seg_length, dtype=jnp.int32)
    global_positions = shard_index * seg_length + local_slots
    cache_now = kv_cache
    for step_index in range(steps):
        write_mask = global_positions[None, :] == positions[step_index][:, None]
        cache_now = jnp.where(write_mask[:, :, None], new_entry[step_index][:, None, :], cache_now)

    key_rows = cache_now[:, :, :head_width]
    value_rows = cache_now[:, :, head_width:]
    query_heads = (
        query_rows.reshape(steps, group_rows, head_count, head_width)
        .transpose(1, 0, 2, 3)
        .reshape(group_rows, steps * head_count, head_width)
    )
    scores = jnp.einsum(
        "gqd,gsd->gqs", query_heads, key_rows, preferred_element_type=jnp.float32
    ) * head_width ** (-0.5)
    head_positions = jnp.repeat(positions.T, head_count, axis=1)
    valid = global_positions[None, None, :] <= head_positions[:, :, None]
    local_peak = jnp.max(jnp.where(valid, scores, NEGATIVE), axis=-1)
    weights = jnp.where(valid, jnp.exp(scores - local_peak[:, :, None]), 0.0)
    local_total = jnp.sum(weights, axis=-1)
    local_weighted = jnp.einsum(
        "gqs,gsd->gqd", weights, value_rows, preferred_element_type=jnp.float32
    )

    _, merged_total, merged_weighted, down_part = merge_over(
        local_peak, local_total, local_weighted, "seq", seq_size, down_part
    )
    mixed = merged_weighted / merged_total[:, :, None]
    mixed = (
        mixed.reshape(group_rows, steps, model_width)
        .transpose(1, 0, 2)
        .astype(jnp.bfloat16)
    )
    own_mixed = lax.dynamic_slice_in_dim(mixed, shard_index * slice_width, slice_width, 2)
    every_mixed = gather_xor(own_mixed, "req", req_size)[0]
    serves = placement[:, None] == request_ids[None, :]
    inverse = jnp.sum(jnp.where(serves, request_ids[:, None], 0), axis=0)
    mixed_rows = xor_slot(group_index ^ (inverse // group_rows), req_size) * group_rows + (
        inverse % group_rows
    )
    mixed_part = every_mixed.transpose(1, 0, 2, 3).reshape(steps, total, slice_width)
    mixed_part = jnp.take(mixed_part, mixed_rows, axis=1, mode="clip").reshape(rows, slice_width)

    partial_sum = jnp.dot(mixed_part, w_out, preferred_element_type=jnp.float32) + down_part
    chunks = seq_size // req_size
    by_request = partial_sum.reshape(steps, total, part_width)
    blocks = by_request.reshape(steps, req_size, group_rows, chunks, slice_width)
    blocks = blocks.transpose(1, 3, 0, 2, 4).reshape(seq_size, steps, group_rows, slice_width)
    reduced = scatter_sum(blocks, "seq", seq_size)
    routes = []
    for source_group in range(req_size):
        for block in range(seq_size):
            target = (block // chunks) * seq_size + source_group * chunks + block % chunks
            routes.append((source_group * seq_size + block, target))
    own_branch = lax.ppermute(reduced, ALL, routes)
    new_states = (states.astype(jnp.float32) + own_branch).astype(jnp.bfloat16)
    return (new_states, cache_now)


def solution(mesh):
    in_specs = (
        P(None, "req", "seq"),
        P("req", "seq", None),
        P(),
        P(),
        P(),
        P(),
        P("req", "seq"),
        P("req", None),
        P("seq", "req"),
        P("req", "seq"),
        P("seq", "req"),
    )
    out_specs = (P(None, "req", "seq"), P("req", "seq", None))
    return jax.shard_map(shards, mesh=mesh, in_specs=in_specs, out_specs=out_specs, check_vma=False)
```

```python
import jax
import jax.numpy as jnp
from jax import lax
from jax.sharding import PartitionSpec as P


EPSILON = 1e-05
NEGATIVE = -1e30
ALL = ("req", "seq")


def xor_pairs(size, bit):
    return [(index, index ^ bit) for index in range(size)]


def gather_xor(block, axis, size, hooks=None, carry=None):
    levels = size.bit_length() - 1
    hooks = hooks or {}
    stacked = block
    for level in range(levels):
        if level in hooks:
            stacked, carry = lax.optimization_barrier((stacked, hooks[level](carry)))
        bit = 2 ** (levels - 1 - level)
        stacked = jnp.stack([stacked, lax.ppermute(stacked, axis, xor_pairs(size, bit))])
    return stacked.reshape((size,) + block.shape), carry


def xor_slot(offset, size):
    levels = size.bit_length() - 1
    position = jnp.zeros_like(offset)
    for level in range(levels):
        bit = 2 ** (levels - 1 - level)
        position = position + ((offset // bit) % 2) * (2 ** level)
    return position


def sum_over(value, axis, size):
    bit = 1
    while bit < size:
        value = value + lax.ppermute(value, axis, xor_pairs(size, bit))
        bit *= 2
    return value


def scatter_sum(blocks, axis, size):
    index = lax.axis_index(axis)
    levels = size.bit_length() - 1
    blocks = blocks.reshape((2,) * levels + blocks.shape[1:])
    for level in range(levels):
        bit = 2 ** level
        place = levels - 1 - level
        high = (index // bit) % 2 == 1
        lower = lax.index_in_dim(blocks, 0, place, keepdims=False)
        upper = lax.index_in_dim(blocks, 1, place, keepdims=False)
        keep = jnp.where(high, upper, lower)
        send = jnp.where(high, lower, upper)
        blocks = keep + lax.ppermute(send, axis, xor_pairs(size, bit))
    return blocks


def split_exact(value):
    high = lax.reduce_precision(value, exponent_bits=8, mantissa_bits=7)
    rest = value - high
    middle = lax.reduce_precision(rest, exponent_bits=8, mantissa_bits=7)
    low = rest - middle
    return [part.astype(jnp.bfloat16) for part in (high, middle, low)]


def join_exact(pieces):
    pieces = pieces.astype(jnp.float32)
    return (pieces[..., 0] + pieces[..., 1]) + pieces[..., 2]


def merge_over(peak, total, weighted, axis, size, carried):
    bit = 1
    while bit < size:
        if bit == 4:
            carried, peak, total, weighted = lax.optimization_barrier(
                (carried, peak, total, weighted)
            )
        sent = jnp.concatenate(
            [jnp.stack(split_exact(peak) + split_exact(total), axis=-1), weighted.astype(jnp.bfloat16)],
            axis=-1,
        )
        other = lax.ppermute(sent, axis, xor_pairs(size, bit))
        peak_second = join_exact(other[..., 0:3])
        total_second = join_exact(other[..., 3:6])
        weighted_second = other[..., 6:].astype(jnp.float32)
        merged_peak = jnp.maximum(peak, peak_second)
        scale_first = jnp.exp(peak - merged_peak)
        scale_second = jnp.exp(peak_second - merged_peak)
        total = total * scale_first + total_second * scale_second
        weighted = weighted * scale_first[..., None] + weighted_second * scale_second[..., None]
        peak = merged_peak
        bit *= 2
    return peak, total, weighted, carried


def layer_norm(row_block, norm_gain, norm_bias):
    values = row_block.astype(jnp.float32)
    average = jnp.mean(values, axis=-1, keepdims=True)
    centered = values - average
    spread = jnp.mean(centered * centered, axis=-1, keepdims=True)
    scaled = centered * lax.rsqrt(spread + EPSILON)
    return (scaled * norm_gain.astype(jnp.float32) + norm_bias.astype(jnp.float32)).astype(
        jnp.bfloat16
    )


def rotate(vectors, positions):
    head_width = vectors.shape[-1]
    half_width = head_width // 2
    frequency = 10000.0 ** (-(jnp.arange(half_width, dtype=jnp.float32) * 2.0) / head_width)
    angles = positions.astype(jnp.float32)[:, None] * frequency[None, :]
    cosine = jnp.concatenate([jnp.cos(angles), jnp.cos(angles)], axis=-1)[:, None, :]
    sine_wave = jnp.concatenate([jnp.sin(angles), jnp.sin(angles)], axis=-1)[:, None, :]
    turned = jnp.concatenate([-vectors[..., half_width:], vectors[..., :half_width]], axis=-1)
    return vectors * cosine + turned * sine_wave


def shards(
    states,
    kv_cache,
    lengths,
    placement,
    norm_gain,
    norm_bias,
    w_query,
    w_keyval,
    w_out,
    w_up,
    w_down,
):
    steps = states.shape[0]
    group_rows = kv_cache.shape[0]
    seg_length = kv_cache.shape[1]
    head_width = kv_cache.shape[2] // 2
    model_width = norm_gain.shape[0]
    head_count = model_width // head_width
    slice_width = states.shape[2]
    part_width = w_query.shape[0]
    total = placement.shape[0]
    req_size = total // group_rows
    seq_size = model_width // slice_width
    rows = steps * total
    group_index = lax.axis_index("req")
    shard_index = lax.axis_index("seq")

    seq_ids = jnp.arange(seq_size, dtype=jnp.int32)
    req_ids = jnp.arange(req_size, dtype=jnp.int32)
    seq_slots = xor_slot(shard_index ^ seq_ids, seq_size)
    req_slots = xor_slot(group_index ^ req_ids, req_size)

    request_ids = jnp.arange(total, dtype=jnp.int32)
    step_offsets = jnp.arange(steps, dtype=jnp.int32)

    def bookkeeping(carried):
        placement_now, lengths_now = carried
        own_requests = lax.dynamic_slice_in_dim(
            placement_now, group_index * group_rows, group_rows, 0
        )
        own_serves = own_requests[:, None] == request_ids[None, :]
        slot_lengths = jnp.sum(jnp.where(own_serves, lengths_now[None, :], 0), axis=1)
        positions = slot_lengths[None, :] + step_offsets[:, None]
        serves = placement_now[:, None] == request_ids[None, :]
        inverse = jnp.sum(jnp.where(serves, request_ids[:, None], 0), axis=0)
        return own_serves, positions, inverse

    by_request, _ = gather_xor(states, "req", req_size)
    hooks = {1: lambda carried: carried}
    if seq_size >= 8:
        hooks[2] = lambda carried: carried
        hooks[3] = lambda carried: (carried[0], bookkeeping(carried[1]))
    every, carried = gather_xor(
        by_request, "seq", seq_size, hooks, ((norm_gain, norm_bias), (placement, lengths))
    )
    (norm_gain, norm_bias), books = carried
    if seq_size < 8:
        books = bookkeeping(books)
    own_serves, positions, inverse = books
    every = every.reshape((seq_size * req_size,) + every.shape[2:])
    every = jnp.take(every, seq_slots[:, None] * req_size + req_slots[None, :], axis=0, mode="clip")
    current_all = every.transpose(2, 1, 3, 0, 4).reshape(steps, total, model_width)
    normed = layer_norm(current_all.reshape(rows, model_width), norm_gain, norm_bias)
    normed_part = lax.dynamic_slice_in_dim(normed, group_index * part_width, part_width, 1)

    part_query = jnp.dot(normed_part, w_query, preferred_element_type=jnp.float32)
    part_keyval = jnp.dot(normed_part, w_keyval, preferred_element_type=jnp.float32)
    first = sum_over(jnp.concatenate([part_query, part_keyval], axis=1), "req", req_size)
    part_up = jnp.dot(normed_part, w_up, preferred_element_type=jnp.float32)
    first, part_up = lax.optimization_barrier((first, part_up))
    own_first = jnp.sum(
        jnp.where(own_serves[None, :, :, None], first.reshape(steps, 1, total, -1), 0.0), axis=2
    )
    own_query = own_first[:, :, :slice_width].astype(jnp.bfloat16)
    own_keyval = own_first[:, :, slice_width:]

    query_hooks = {1: lambda carried: carried}
    if seq_size >= 4:
        query_hooks[2] = lambda carried: (carried[0], sum_over(carried[1], "req", req_size))
    query_all, (kv_cache, up_part) = gather_xor(
        own_query, "seq", seq_size, query_hooks, (kv_cache, part_up)
    )
    if seq_size < 4:
        up_part = sum_over(up_part, "req", req_size)
    hidden = jax.nn.gelu(up_part, approximate=False).astype(jnp.bfloat16)
    down_part = jnp.dot(hidden, w_down, preferred_element_type=jnp.float32)
    query_all = jnp.take(query_all, seq_slots, axis=0, mode="clip")
    query_all = query_all.transpose(1, 2, 0, 3).reshape(steps, group_rows, model_width)
    flat_positions = positions.reshape(-1)
    query_rows = rotate(
        query_all.astype(jnp.float32).reshape(steps * group_rows, head_count, head_width),
        flat_positions,
    ).astype(jnp.bfloat16)
    own_keyval = own_keyval.reshape(steps * group_rows, 2 * head_width)
    new_key = rotate(own_keyval[:, None, :head_width], flat_positions)[:, 0, :]
    new_entry = jnp.concatenate([new_key, own_keyval[:, head_width:]], axis=-1).astype(jnp.bfloat16)
    new_entry = new_entry.reshape(steps, group_rows, 2 * head_width)

    local_slots = jnp.arange(seg_length, dtype=jnp.int32)
    global_positions = shard_index * seg_length + local_slots
    cache_now = kv_cache
    for step_index in range(steps):
        write_mask = global_positions[None, :] == positions[step_index][:, None]
        cache_now = jnp.where(write_mask[:, :, None], new_entry[step_index][:, None, :], cache_now)

    key_rows = cache_now[:, :, :head_width]
    value_rows = cache_now[:, :, head_width:]
    query_heads = (
        query_rows.reshape(steps, group_rows, head_count, head_width)
        .transpose(1, 0, 2, 3)
        .reshape(group_rows, steps * head_count, head_width)
    )
    scores = jnp.einsum(
        "gqd,gsd->gqs", query_heads, key_rows, preferred_element_type=jnp.float32
    ) * head_width ** (-0.5)
    head_positions = jnp.repeat(positions.T, head_count, axis=1)
    valid = global_positions[None, None, :] <= head_positions[:, :, None]
    local_peak = jnp.max(jnp.where(valid, scores, NEGATIVE), axis=-1)
    weights = jnp.where(valid, jnp.exp(scores - local_peak[:, :, None]), 0.0)
    local_total = jnp.sum(weights, axis=-1)
    local_weighted = jnp.einsum(
        "gqs,gsd->gqd", weights, value_rows, preferred_element_type=jnp.float32
    )

    _, merged_total, merged_weighted, down_part = merge_over(
        local_peak, local_total, local_weighted, "seq", seq_size, down_part
    )
    mixed = merged_weighted / merged_total[:, :, None]
    mixed = (
        mixed.reshape(group_rows, steps, model_width)
        .transpose(1, 0, 2)
        .astype(jnp.bfloat16)
    )
    own_mixed = lax.dynamic_slice_in_dim(mixed, shard_index * slice_width, slice_width, 2)
    every_mixed = gather_xor(own_mixed, "req", req_size)[0]
    mixed_rows = xor_slot(group_index ^ (inverse // group_rows), req_size) * group_rows + (
        inverse % group_rows
    )
    mixed_part = every_mixed.transpose(1, 0, 2, 3).reshape(steps, total, slice_width)
    mixed_part = jnp.take(mixed_part, mixed_rows, axis=1, mode="clip").reshape(rows, slice_width)

    partial_sum = jnp.dot(mixed_part, w_out, preferred_element_type=jnp.float32) + down_part
    chunks = seq_size // req_size
    by_request = partial_sum.reshape(steps, total, part_width)
    blocks = by_request.reshape(steps, req_size, group_rows, chunks, slice_width)
    blocks = blocks.transpose(1, 3, 0, 2, 4).reshape(seq_size, steps, group_rows, slice_width)
    reduced = scatter_sum(blocks, "seq", seq_size)
    routes = []
    for source_group in range(req_size):
        for block in range(seq_size):
            target = (block // chunks) * seq_size + source_group * chunks + block % chunks
            routes.append((source_group * seq_size + block, target))
    own_branch = lax.ppermute(reduced, ALL, routes)
    new_states = (states.astype(jnp.float32) + own_branch).astype(jnp.bfloat16)
    return (new_states, cache_now)


def solution(mesh):
    in_specs = (
        P(None, "req", "seq"),
        P("req", "seq", None),
        P(),
        P(),
        P(),
        P(),
        P("req", "seq"),
        P("req", None),
        P("seq", "req"),
        P("req", "seq"),
        P("seq", "req"),
    )
    out_specs = (P(None, "req", "seq"), P("req", "seq", None))
    return jax.shard_map(shards, mesh=mesh, in_specs=in_specs, out_specs=out_specs, check_vma=False)
```

```python
import jax
import jax.numpy as jnp
from jax import lax
from jax.sharding import PartitionSpec as P


EPSILON = 1e-05
NEGATIVE = -1e30
ALL = ("req", "seq")


def xor_pairs(size, bit):
    return [(index, index ^ bit) for index in range(size)]


def gather_xor(block, axis, size, riders=None):
    levels = size.bit_length() - 1
    riders = dict(riders or {})
    stacked = block
    for level in range(levels):
        bit = 2 ** (levels - 1 - level)
        stacked = jnp.stack([stacked, lax.ppermute(stacked, axis, xor_pairs(size, bit))])
        if level in riders:
            stacked, riders[level] = lax.optimization_barrier((stacked, riders[level]))
    return stacked.reshape((size,) + block.shape), riders


def xor_slot(offset, size):
    levels = size.bit_length() - 1
    position = jnp.zeros_like(offset)
    for level in range(levels):
        bit = 2 ** (levels - 1 - level)
        position = position + ((offset // bit) % 2) * (2 ** level)
    return position


def sum_over(value, axis, size):
    bit = 1
    while bit < size:
        value = value + lax.ppermute(value, axis, xor_pairs(size, bit))
        bit *= 2
    return value


def scatter_sum(blocks, axis, size):
    index = lax.axis_index(axis)
    levels = size.bit_length() - 1
    blocks = blocks.reshape((2,) * levels + blocks.shape[1:])
    for level in range(levels):
        bit = 2 ** level
        place = levels - 1 - level
        high = (index // bit) % 2 == 1
        lower = lax.index_in_dim(blocks, 0, place, keepdims=False)
        upper = lax.index_in_dim(blocks, 1, place, keepdims=False)
        keep = jnp.where(high, upper, lower)
        send = jnp.where(high, lower, upper)
        blocks = keep + lax.ppermute(send, axis, xor_pairs(size, bit))
    return blocks


def split_exact(value):
    high = lax.reduce_precision(value, exponent_bits=8, mantissa_bits=7)
    rest = value - high
    middle = lax.reduce_precision(rest, exponent_bits=8, mantissa_bits=7)
    low = rest - middle
    return [part.astype(jnp.bfloat16) for part in (high, middle, low)]


def join_exact(pieces):
    pieces = pieces.astype(jnp.float32)
    return (pieces[..., 0] + pieces[..., 1]) + pieces[..., 2]


def pack_merge(peak, total, weighted):
    return jnp.concatenate(
        [jnp.stack(split_exact(peak) + split_exact(total), axis=-1), weighted.astype(jnp.bfloat16)],
        axis=-1,
    )


def merge_pair(peak, total, weighted, other):
    peak_second = join_exact(other[..., 0:3])
    total_second = join_exact(other[..., 3:6])
    weighted_second = other[..., 6:].astype(jnp.float32)
    merged_peak = jnp.maximum(peak, peak_second)
    scale_first = jnp.exp(peak - merged_peak)
    scale_second = jnp.exp(peak_second - merged_peak)
    total = total * scale_first + total_second * scale_second
    weighted = weighted * scale_first[..., None] + weighted_second * scale_second[..., None]
    return merged_peak, total, weighted


def merge_over(peak, total, weighted, axis, size, carried, steps, chunk_width):
    index = lax.axis_index(axis)
    group_rows, step_heads, head_width = weighted.shape
    head_count = step_heads // steps
    span = min(head_count, (chunk_width + 2 * head_width - 2) // head_width)
    bit = 1
    while bit < size // 2:
        if bit == 4:
            carried, peak, total, weighted = lax.optimization_barrier(
                (carried, peak, total, weighted)
            )
        other = lax.ppermute(pack_merge(peak, total, weighted), axis, xor_pairs(size, bit))
        peak, total, weighted = merge_pair(peak, total, weighted, other)
        bit *= 2

    def first_head(position):
        return jnp.minimum((position * chunk_width) // head_width, head_count - span)

    def window(value, start):
        value = value.reshape((group_rows, steps, head_count) + value.shape[2:])
        return lax.dynamic_slice_in_dim(value, start, span, 2)

    partner_start = first_head(index ^ bit)
    own_start = first_head(index)
    sent = pack_merge(
        window(peak, partner_start), window(total, partner_start), window(weighted, partner_start)
    )
    other = lax.ppermute(sent, axis, xor_pairs(size, bit))
    _, total, weighted = merge_pair(
        window(peak, own_start), window(total, own_start), window(weighted, own_start), other
    )
    mixed = (weighted / total[..., None]).reshape(group_rows, steps, span * head_width)
    offset = index * chunk_width - own_start * head_width
    return lax.dynamic_slice_in_dim(mixed, offset, chunk_width, 2), carried


def layer_norm(row_block, norm_gain, norm_bias):
    values = row_block.astype(jnp.float32)
    average = jnp.mean(values, axis=-1, keepdims=True)
    centered = values - average
    spread = jnp.mean(centered * centered, axis=-1, keepdims=True)
    scaled = centered * lax.rsqrt(spread + EPSILON)
    return (scaled * norm_gain.astype(jnp.float32) + norm_bias.astype(jnp.float32)).astype(
        jnp.bfloat16
    )


def rotate(vectors, positions):
    head_width = vectors.shape[-1]
    half_width = head_width // 2
    frequency = 10000.0 ** (-(jnp.arange(half_width, dtype=jnp.float32) * 2.0) / head_width)
    angles = positions.astype(jnp.float32)[:, None] * frequency[None, :]
    cosine = jnp.concatenate([jnp.cos(angles), jnp.cos(angles)], axis=-1)[:, None, :]
    sine_wave = jnp.concatenate([jnp.sin(angles), jnp.sin(angles)], axis=-1)[:, None, :]
    turned = jnp.concatenate([-vectors[..., half_width:], vectors[..., :half_width]], axis=-1)
    return vectors * cosine + turned * sine_wave


def shards(
    states,
    kv_cache,
    lengths,
    placement,
    norm_gain,
    norm_bias,
    w_query,
    w_keyval,
    w_out,
    w_up,
    w_down,
):
    steps = states.shape[0]
    group_rows = kv_cache.shape[0]
    seg_length = kv_cache.shape[1]
    head_width = kv_cache.shape[2] // 2
    model_width = norm_gain.shape[0]
    head_count = model_width // head_width
    slice_width = states.shape[2]
    part_width = w_query.shape[0]
    total = placement.shape[0]
    req_size = total // group_rows
    seq_size = model_width // slice_width
    rows = steps * total
    group_index = lax.axis_index("req")
    shard_index = lax.axis_index("seq")

    seq_ids = jnp.arange(seq_size, dtype=jnp.int32)
    req_ids = jnp.arange(req_size, dtype=jnp.int32)
    seq_slots = xor_slot(shard_index ^ seq_ids, seq_size)
    req_slots = xor_slot(group_index ^ req_ids, req_size)

    by_request, _ = gather_xor(states, "req", req_size)
    every, riders = gather_xor(by_request, "seq", seq_size, {0: (norm_gain, norm_bias)})
    norm_gain, norm_bias = riders[0]
    every = every.reshape((seq_size * req_size,) + every.shape[2:])
    every = jnp.take(every, seq_slots[:, None] * req_size + req_slots[None, :], axis=0, mode="clip")
    current_all = every.transpose(2, 1, 3, 0, 4).reshape(steps, total, model_width)
    normed = layer_norm(current_all.reshape(rows, model_width), norm_gain, norm_bias)
    normed_part = lax.dynamic_slice_in_dim(normed, group_index * part_width, part_width, 1)

    part_query = jnp.dot(normed_part, w_query, preferred_element_type=jnp.float32)
    part_keyval = jnp.dot(normed_part, w_keyval, preferred_element_type=jnp.float32)
    first = sum_over(jnp.concatenate([part_query, part_keyval], axis=1), "req", req_size)
    part_up = jnp.dot(normed_part, w_up, preferred_element_type=jnp.float32)
    first, part_up = lax.optimization_barrier((first, part_up))
    request_ids = jnp.arange(total, dtype=jnp.int32)
    own_requests = lax.dynamic_slice_in_dim(placement, group_index * group_rows, group_rows, 0)
    own_serves = own_requests[:, None] == request_ids[None, :]
    slot_lengths = jnp.sum(jnp.where(own_serves, lengths[None, :], 0), axis=1)
    step_offsets = jnp.arange(steps, dtype=jnp.int32)
    positions = slot_lengths[None, :] + step_offsets[:, None]
    own_first = jnp.sum(
        jnp.where(own_serves[None, :, :, None], first.reshape(steps, 1, total, -1), 0.0), axis=2
    )
    own_query = own_first[:, :, :slice_width].astype(jnp.bfloat16)
    own_keyval = own_first[:, :, slice_width:]
    up_part = sum_over(part_up, "req", req_size)
    hidden = jax.nn.gelu(up_part, approximate=False).astype(jnp.bfloat16)
    down_part = jnp.dot(hidden, w_down, preferred_element_type=jnp.float32)

    query_all, riders = gather_xor(own_query, "seq", seq_size, {0: kv_cache})
    kv_cache = riders[0]
    query_all = jnp.take(query_all, seq_slots, axis=0, mode="clip")
    query_all = query_all.transpose(1, 2, 0, 3).reshape(steps, group_rows, model_width)
    flat_positions = positions.reshape(-1)
    query_rows = rotate(
        query_all.astype(jnp.float32).reshape(steps * group_rows, head_count, head_width),
        flat_positions,
    ).astype(jnp.bfloat16)
    own_keyval = own_keyval.reshape(steps * group_rows, 2 * head_width)
    new_key = rotate(own_keyval[:, None, :head_width], flat_positions)[:, 0, :]
    new_entry = jnp.concatenate([new_key, own_keyval[:, head_width:]], axis=-1).astype(jnp.bfloat16)
    new_entry = new_entry.reshape(steps, group_rows, 2 * head_width)

    local_slots = jnp.arange(seg_length, dtype=jnp.int32)
    global_positions = shard_index * seg_length + local_slots
    cache_now = kv_cache
    for step_index in range(steps):
        write_mask = global_positions[None, :] == positions[step_index][:, None]
        cache_now = jnp.where(write_mask[:, :, None], new_entry[step_index][:, None, :], cache_now)

    key_rows = cache_now[:, :, :head_width]
    value_rows = cache_now[:, :, head_width:]
    query_heads = (
        query_rows.reshape(steps, group_rows, head_count, head_width)
        .transpose(1, 0, 2, 3)
        .reshape(group_rows, steps * head_count, head_width)
    )
    scores = jnp.einsum(
        "gqd,gsd->gqs", query_heads, key_rows, preferred_element_type=jnp.float32
    ) * head_width ** (-0.5)
    head_positions = jnp.repeat(positions.T, head_count, axis=1)
    valid = global_positions[None, None, :] <= head_positions[:, :, None]
    local_peak = jnp.max(jnp.where(valid, scores, NEGATIVE), axis=-1)
    weights = jnp.where(valid, jnp.exp(scores - local_peak[:, :, None]), 0.0)
    local_total = jnp.sum(weights, axis=-1)
    local_weighted = jnp.einsum(
        "gqs,gsd->gqd", weights, value_rows, preferred_element_type=jnp.float32
    )

    own_mixed, down_part = merge_over(
        local_peak, local_total, local_weighted, "seq", seq_size, down_part, steps, slice_width
    )
    own_mixed = own_mixed.transpose(1, 0, 2).astype(jnp.bfloat16)
    every_mixed = gather_xor(own_mixed, "req", req_size)[0]
    serves = placement[:, None] == request_ids[None, :]
    inverse = jnp.sum(jnp.where(serves, request_ids[:, None], 0), axis=0)
    mixed_rows = xor_slot(group_index ^ (inverse // group_rows), req_size) * group_rows + (
        inverse % group_rows
    )
    mixed_part = every_mixed.transpose(1, 0, 2, 3).reshape(steps, total, slice_width)
    mixed_part = jnp.take(mixed_part, mixed_rows, axis=1, mode="clip").reshape(rows, slice_width)

    partial_sum = jnp.dot(mixed_part, w_out, preferred_element_type=jnp.float32) + down_part
    chunks = seq_size // req_size
    by_request = partial_sum.reshape(steps, total, part_width)
    blocks = by_request.reshape(steps, req_size, group_rows, chunks, slice_width)
    blocks = blocks.transpose(1, 3, 0, 2, 4).reshape(seq_size, steps, group_rows, slice_width)
    reduced = scatter_sum(blocks, "seq", seq_size)
    routes = []
    for source_group in range(req_size):
        for block in range(seq_size):
            target = (block // chunks) * seq_size + source_group * chunks + block % chunks
            routes.append((source_group * seq_size + block, target))
    own_branch = lax.ppermute(reduced, ALL, routes)
    new_states = (states.astype(jnp.float32) + own_branch).astype(jnp.bfloat16)
    return (new_states, cache_now)


def solution(mesh):
    in_specs = (
        P(None, "req", "seq"),
        P("req", "seq", None),
        P(),
        P(),
        P(),
        P(),
        P("req", "seq"),
        P("req", None),
        P("seq", "req"),
        P("req", "seq"),
        P("seq", "req"),
    )
    out_specs = (P(None, "req", "seq"), P("req", "seq", None))
    return jax.shard_map(shards, mesh=mesh, in_specs=in_specs, out_specs=out_specs, check_vma=False)
```

```python
import jax
import jax.numpy as jnp
from jax import lax
from jax.sharding import PartitionSpec as P


EPSILON = 1e-05
NEGATIVE = -1e30
ALL = ("req", "seq")


def xor_pairs(size, bit):
    return [(index, index ^ bit) for index in range(size)]


def gather_xor(block, axis, size, riders=None):
    levels = size.bit_length() - 1
    riders = dict(riders or {})
    stacked = block
    for level in range(levels):
        bit = 2 ** (levels - 1 - level)
        stacked = jnp.stack([stacked, lax.ppermute(stacked, axis, xor_pairs(size, bit))])
        if level in riders:
            stacked, riders[level] = lax.optimization_barrier((stacked, riders[level]))
    return stacked.reshape((size,) + block.shape), riders


def xor_slot(offset, size):
    levels = size.bit_length() - 1
    position = jnp.zeros_like(offset)
    for level in range(levels):
        bit = 2 ** (levels - 1 - level)
        position = position + ((offset // bit) % 2) * (2 ** level)
    return position


def sum_over(value, axis, size):
    bit = 1
    while bit < size:
        value = value + lax.ppermute(value, axis, xor_pairs(size, bit))
        bit *= 2
    return value


def scatter_sum(blocks, axis, size):
    index = lax.axis_index(axis)
    levels = size.bit_length() - 1
    blocks = blocks.reshape((2,) * levels + blocks.shape[1:])
    for level in range(levels):
        bit = 2 ** level
        place = levels - 1 - level
        high = (index // bit) % 2 == 1
        lower = lax.index_in_dim(blocks, 0, place, keepdims=False)
        upper = lax.index_in_dim(blocks, 1, place, keepdims=False)
        keep = jnp.where(high, upper, lower)
        send = jnp.where(high, lower, upper)
        blocks = keep + lax.ppermute(send, axis, xor_pairs(size, bit))
    return blocks


def split_exact(value):
    high = lax.reduce_precision(value, exponent_bits=8, mantissa_bits=7)
    rest = value - high
    middle = lax.reduce_precision(rest, exponent_bits=8, mantissa_bits=7)
    low = rest - middle
    return [part.astype(jnp.bfloat16) for part in (high, middle, low)]


def join_exact(pieces):
    pieces = pieces.astype(jnp.float32)
    return (pieces[..., 0] + pieces[..., 1]) + pieces[..., 2]


def pack_merge(peak, total, weighted):
    return jnp.concatenate(
        [jnp.stack(split_exact(peak) + split_exact(total), axis=-1), weighted.astype(jnp.bfloat16)],
        axis=-1,
    )


def merge_pair(peak, total, weighted, other):
    peak_second = join_exact(other[..., 0:3])
    total_second = join_exact(other[..., 3:6])
    weighted_second = other[..., 6:].astype(jnp.float32)
    merged_peak = jnp.maximum(peak, peak_second)
    scale_first = jnp.exp(peak - merged_peak)
    scale_second = jnp.exp(peak_second - merged_peak)
    total = total * scale_first + total_second * scale_second
    weighted = weighted * scale_first[..., None] + weighted_second * scale_second[..., None]
    return merged_peak, total, weighted


def merge_over(peak, total, weighted, axis, size, carried, steps, chunk_width):
    index = lax.axis_index(axis)
    group_rows, step_heads, head_width = weighted.shape
    head_count = step_heads // steps
    span = min(head_count, (chunk_width + 2 * head_width - 2) // head_width)
    bit = 1
    while bit < size // 2:
        if bit == 4:
            carried, peak, total, weighted = lax.optimization_barrier(
                (carried, peak, total, weighted)
            )
        other = lax.ppermute(pack_merge(peak, total, weighted), axis, xor_pairs(size, bit))
        peak, total, weighted = merge_pair(peak, total, weighted, other)
        bit *= 2

    def first_head(position):
        return jnp.minimum((position * chunk_width) // head_width, head_count - span)

    def window(value, start):
        value = value.reshape((group_rows, steps, head_count) + value.shape[2:])
        return lax.dynamic_slice_in_dim(value, start, span, 2)

    partner_start = first_head(index ^ bit)
    own_start = first_head(index)
    sent = window(pack_merge(peak, total, weighted), partner_start)
    other = lax.ppermute(sent, axis, xor_pairs(size, bit))
    _, total, weighted = merge_pair(
        window(peak, own_start), window(total, own_start), window(weighted, own_start), other
    )
    mixed = (weighted / total[..., None]).reshape(group_rows, steps, span * head_width)
    offset = index * chunk_width - own_start * head_width
    return lax.dynamic_slice_in_dim(mixed, offset, chunk_width, 2), carried


def layer_norm(row_block, norm_gain, norm_bias):
    values = row_block.astype(jnp.float32)
    average = jnp.mean(values, axis=-1, keepdims=True)
    centered = values - average
    spread = jnp.mean(centered * centered, axis=-1, keepdims=True)
    scaled = centered * lax.rsqrt(spread + EPSILON)
    return (scaled * norm_gain.astype(jnp.float32) + norm_bias.astype(jnp.float32)).astype(
        jnp.bfloat16
    )


def rotate(vectors, positions):
    head_width = vectors.shape[-1]
    half_width = head_width // 2
    frequency = 10000.0 ** (-(jnp.arange(half_width, dtype=jnp.float32) * 2.0) / head_width)
    angles = positions.astype(jnp.float32)[:, None] * frequency[None, :]
    cosine = jnp.concatenate([jnp.cos(angles), jnp.cos(angles)], axis=-1)[:, None, :]
    sine_wave = jnp.concatenate([jnp.sin(angles), jnp.sin(angles)], axis=-1)[:, None, :]
    turned = jnp.concatenate([-vectors[..., half_width:], vectors[..., :half_width]], axis=-1)
    return vectors * cosine + turned * sine_wave


def shards(
    states,
    kv_cache,
    lengths,
    placement,
    norm_gain,
    norm_bias,
    w_query,
    w_keyval,
    w_out,
    w_up,
    w_down,
):
    steps = states.shape[0]
    group_rows = kv_cache.shape[0]
    seg_length = kv_cache.shape[1]
    head_width = kv_cache.shape[2] // 2
    model_width = norm_gain.shape[0]
    head_count = model_width // head_width
    slice_width = states.shape[2]
    part_width = w_query.shape[0]
    total = placement.shape[0]
    req_size = total // group_rows
    seq_size = model_width // slice_width
    rows = steps * total
    group_index = lax.axis_index("req")
    shard_index = lax.axis_index("seq")

    seq_ids = jnp.arange(seq_size, dtype=jnp.int32)
    req_ids = jnp.arange(req_size, dtype=jnp.int32)
    seq_slots = xor_slot(shard_index ^ seq_ids, seq_size)
    req_slots = xor_slot(group_index ^ req_ids, req_size)

    by_request, _ = gather_xor(states, "req", req_size)
    every, riders = gather_xor(by_request, "seq", seq_size, {0: (norm_gain, norm_bias)})
    norm_gain, norm_bias = riders[0]
    every = every.reshape((seq_size * req_size,) + every.shape[2:])
    every = jnp.take(every, seq_slots[:, None] * req_size + req_slots[None, :], axis=0, mode="clip")
    current_all = every.transpose(2, 1, 3, 0, 4).reshape(steps, total, model_width)
    normed = layer_norm(current_all.reshape(rows, model_width), norm_gain, norm_bias)
    normed_part = lax.dynamic_slice_in_dim(normed, group_index * part_width, part_width, 1)

    part_query = jnp.dot(normed_part, w_query, preferred_element_type=jnp.float32)
    part_keyval = jnp.dot(normed_part, w_keyval, preferred_element_type=jnp.float32)
    first = sum_over(jnp.concatenate([part_query, part_keyval], axis=1), "req", req_size)
    part_up = jnp.dot(normed_part, w_up, preferred_element_type=jnp.float32)
    first, part_up = lax.optimization_barrier((first, part_up))
    request_ids = jnp.arange(total, dtype=jnp.int32)
    own_requests = lax.dynamic_slice_in_dim(placement, group_index * group_rows, group_rows, 0)
    own_serves = own_requests[:, None] == request_ids[None, :]
    slot_lengths = jnp.sum(jnp.where(own_serves, lengths[None, :], 0), axis=1)
    step_offsets = jnp.arange(steps, dtype=jnp.int32)
    positions = slot_lengths[None, :] + step_offsets[:, None]
    own_first = jnp.sum(
        jnp.where(own_serves[None, :, :, None], first.reshape(steps, 1, total, -1), 0.0), axis=2
    )
    own_query = own_first[:, :, :slice_width].astype(jnp.bfloat16)
    own_keyval = own_first[:, :, slice_width:]
    up_part = sum_over(part_up, "req", req_size)
    hidden = jax.nn.gelu(up_part, approximate=False).astype(jnp.bfloat16)
    down_part = jnp.dot(hidden, w_down, preferred_element_type=jnp.float32)

    query_all, riders = gather_xor(own_query, "seq", seq_size, {0: kv_cache})
    kv_cache = riders[0]
    query_all = jnp.take(query_all, seq_slots, axis=0, mode="clip")
    query_all = query_all.transpose(1, 2, 0, 3).reshape(steps, group_rows, model_width)
    flat_positions = positions.reshape(-1)
    query_rows = rotate(
        query_all.astype(jnp.float32).reshape(steps * group_rows, head_count, head_width),
        flat_positions,
    ).astype(jnp.bfloat16)
    own_keyval = own_keyval.reshape(steps * group_rows, 2 * head_width)
    new_key = rotate(own_keyval[:, None, :head_width], flat_positions)[:, 0, :]
    new_entry = jnp.concatenate([new_key, own_keyval[:, head_width:]], axis=-1).astype(jnp.bfloat16)
    new_entry = new_entry.reshape(steps, group_rows, 2 * head_width)

    local_slots = jnp.arange(seg_length, dtype=jnp.int32)
    global_positions = shard_index * seg_length + local_slots
    cache_now = kv_cache
    for step_index in range(steps):
        write_mask = global_positions[None, :] == positions[step_index][:, None]
        cache_now = jnp.where(write_mask[:, :, None], new_entry[step_index][:, None, :], cache_now)

    key_rows = cache_now[:, :, :head_width]
    value_rows = cache_now[:, :, head_width:]
    query_heads = (
        query_rows.reshape(steps, group_rows, head_count, head_width)
        .transpose(1, 0, 2, 3)
        .reshape(group_rows, steps * head_count, head_width)
    )
    scores = jnp.einsum(
        "gqd,gsd->gqs", query_heads, key_rows, preferred_element_type=jnp.float32
    ) * head_width ** (-0.5)
    head_positions = jnp.repeat(positions.T, head_count, axis=1)
    valid = global_positions[None, None, :] <= head_positions[:, :, None]
    local_peak = jnp.max(jnp.where(valid, scores, NEGATIVE), axis=-1)
    weights = jnp.where(valid, jnp.exp(scores - local_peak[:, :, None]), 0.0)
    local_total = jnp.sum(weights, axis=-1)
    local_weighted = jnp.einsum(
        "gqs,gsd->gqd", weights, value_rows, preferred_element_type=jnp.float32
    )

    own_mixed, down_part = merge_over(
        local_peak, local_total, local_weighted, "seq", seq_size, down_part, steps, slice_width
    )
    own_mixed = own_mixed.transpose(1, 0, 2).astype(jnp.bfloat16)
    every_mixed = gather_xor(own_mixed, "req", req_size)[0]
    serves = placement[:, None] == request_ids[None, :]
    inverse = jnp.sum(jnp.where(serves, request_ids[:, None], 0), axis=0)
    mixed_rows = xor_slot(group_index ^ (inverse // group_rows), req_size) * group_rows + (
        inverse % group_rows
    )
    mixed_part = every_mixed.transpose(1, 0, 2, 3).reshape(steps, total, slice_width)
    mixed_part = jnp.take(mixed_part, mixed_rows, axis=1, mode="clip").reshape(rows, slice_width)

    partial_sum = jnp.dot(mixed_part, w_out, preferred_element_type=jnp.float32) + down_part
    chunks = seq_size // req_size
    by_request = partial_sum.reshape(steps, total, part_width)
    blocks = by_request.reshape(steps, req_size, group_rows, chunks, slice_width)
    blocks = blocks.transpose(1, 3, 0, 2, 4).reshape(seq_size, steps, group_rows, slice_width)
    reduced = scatter_sum(blocks, "seq", seq_size)
    routes = []
    for source_group in range(req_size):
        for block in range(seq_size):
            target = (block // chunks) * seq_size + source_group * chunks + block % chunks
            routes.append((source_group * seq_size + block, target))
    own_branch = lax.ppermute(reduced, ALL, routes)
    new_states = (states.astype(jnp.float32) + own_branch).astype(jnp.bfloat16)
    return (new_states, cache_now)


def solution(mesh):
    in_specs = (
        P(None, "req", "seq"),
        P("req", "seq", None),
        P(),
        P(),
        P(),
        P(),
        P("req", "seq"),
        P("req", None),
        P("seq", "req"),
        P("req", "seq"),
        P("seq", "req"),
    )
    out_specs = (P(None, "req", "seq"), P("req", "seq", None))
    return jax.shard_map(shards, mesh=mesh, in_specs=in_specs, out_specs=out_specs, check_vma=False)
```

```python
import jax
import jax.numpy as jnp
from jax import lax
from jax.sharding import PartitionSpec as P


EPSILON = 1e-05
NEGATIVE = -1e30
ALL = ("req", "seq")


def xor_pairs(size, bit):
    return [(index, index ^ bit) for index in range(size)]


def gather_xor(block, axis, size, riders=None):
    levels = size.bit_length() - 1
    riders = dict(riders or {})
    stacked = block
    for level in range(levels):
        bit = 2 ** (levels - 1 - level)
        stacked = jnp.stack([stacked, lax.ppermute(stacked, axis, xor_pairs(size, bit))])
        if level in riders:
            stacked, riders[level] = lax.optimization_barrier((stacked, riders[level]))
    return stacked.reshape((size,) + block.shape), riders


def xor_slot(offset, size):
    levels = size.bit_length() - 1
    position = jnp.zeros_like(offset)
    for level in range(levels):
        bit = 2 ** (levels - 1 - level)
        position = position + ((offset // bit) % 2) * (2 ** level)
    return position


def sum_over(value, axis, size):
    bit = 1
    while bit < size:
        value = value + lax.ppermute(value, axis, xor_pairs(size, bit))
        bit *= 2
    return value


def scatter_sum(blocks, axis, size, rounds):
    index = lax.axis_index(axis)
    levels = size.bit_length() - 1
    blocks = blocks.reshape((2,) * levels + blocks.shape[1:])
    for level in range(rounds):
        bit = 2 ** level
        place = levels - 1 - level
        high = (index // bit) % 2 == 1
        lower = lax.index_in_dim(blocks, 0, place, keepdims=False)
        upper = lax.index_in_dim(blocks, 1, place, keepdims=False)
        keep = jnp.where(high, upper, lower)
        send = jnp.where(high, lower, upper)
        blocks = keep + lax.ppermute(send, axis, xor_pairs(size, bit))
    return blocks


def split_exact(value):
    high = lax.reduce_precision(value, exponent_bits=8, mantissa_bits=7)
    rest = value - high
    middle = lax.reduce_precision(rest, exponent_bits=8, mantissa_bits=7)
    low = rest - middle
    return [part.astype(jnp.bfloat16) for part in (high, middle, low)]


def join_exact(pieces):
    pieces = pieces.astype(jnp.float32)
    return (pieces[..., 0] + pieces[..., 1]) + pieces[..., 2]


def pack_merge(peak, total, weighted):
    return jnp.concatenate(
        [jnp.stack(split_exact(peak) + split_exact(total), axis=-1), weighted.astype(jnp.bfloat16)],
        axis=-1,
    )


def merge_pair(peak, total, weighted, other):
    peak_second = join_exact(other[..., 0:3])
    total_second = join_exact(other[..., 3:6])
    weighted_second = other[..., 6:].astype(jnp.float32)
    merged_peak = jnp.maximum(peak, peak_second)
    scale_first = jnp.exp(peak - merged_peak)
    scale_second = jnp.exp(peak_second - merged_peak)
    total = total * scale_first + total_second * scale_second
    weighted = weighted * scale_first[..., None] + weighted_second * scale_second[..., None]
    return merged_peak, total, weighted


def merge_over(peak, total, weighted, axis, size, carried, steps, chunk_width):
    index = lax.axis_index(axis)
    group_rows, step_heads, head_width = weighted.shape
    head_count = step_heads // steps
    span = min(head_count, (chunk_width + 2 * head_width - 2) // head_width)
    bit = 1
    while bit < size // 2:
        if bit == 4:
            carried, peak, total, weighted = lax.optimization_barrier(
                (carried, peak, total, weighted)
            )
        other = lax.ppermute(pack_merge(peak, total, weighted), axis, xor_pairs(size, bit))
        peak, total, weighted = merge_pair(peak, total, weighted, other)
        bit *= 2

    def first_head(position):
        return jnp.minimum((position * chunk_width) // head_width, head_count - span)

    def window(value, start):
        value = value.reshape((group_rows, steps, head_count) + value.shape[2:])
        return lax.dynamic_slice_in_dim(value, start, span, 2)

    partner_start = first_head(index ^ bit)
    own_start = first_head(index)
    sent = window(pack_merge(peak, total, weighted), partner_start)
    other = lax.ppermute(sent, axis, xor_pairs(size, bit))
    _, total, weighted = merge_pair(
        window(peak, own_start), window(total, own_start), window(weighted, own_start), other
    )
    mixed = (weighted / total[..., None]).reshape(group_rows, steps, span * head_width)
    offset = index * chunk_width - own_start * head_width
    return lax.dynamic_slice_in_dim(mixed, offset, chunk_width, 2), carried


def layer_norm(row_block, norm_gain, norm_bias):
    values = row_block.astype(jnp.float32)
    average = jnp.mean(values, axis=-1, keepdims=True)
    centered = values - average
    spread = jnp.mean(centered * centered, axis=-1, keepdims=True)
    scaled = centered * lax.rsqrt(spread + EPSILON)
    return (scaled * norm_gain.astype(jnp.float32) + norm_bias.astype(jnp.float32)).astype(
        jnp.bfloat16
    )


def rotate(vectors, positions):
    head_width = vectors.shape[-1]
    half_width = head_width // 2
    frequency = 10000.0 ** (-(jnp.arange(half_width, dtype=jnp.float32) * 2.0) / head_width)
    angles = positions.astype(jnp.float32)[:, None] * frequency[None, :]
    cosine = jnp.concatenate([jnp.cos(angles), jnp.cos(angles)], axis=-1)[:, None, :]
    sine_wave = jnp.concatenate([jnp.sin(angles), jnp.sin(angles)], axis=-1)[:, None, :]
    turned = jnp.concatenate([-vectors[..., half_width:], vectors[..., :half_width]], axis=-1)
    return vectors * cosine + turned * sine_wave


def shards(
    states,
    kv_cache,
    lengths,
    placement,
    norm_gain,
    norm_bias,
    w_query,
    w_keyval,
    w_out,
    w_up,
    w_down,
):
    steps = states.shape[0]
    group_rows = kv_cache.shape[0]
    seg_length = kv_cache.shape[1]
    head_width = kv_cache.shape[2] // 2
    model_width = norm_gain.shape[0]
    head_count = model_width // head_width
    slice_width = states.shape[2]
    part_width = w_query.shape[0]
    total = placement.shape[0]
    req_size = total // group_rows
    seq_size = model_width // slice_width
    rows = steps * total
    group_index = lax.axis_index("req")
    shard_index = lax.axis_index("seq")

    seq_ids = jnp.arange(seq_size, dtype=jnp.int32)
    req_ids = jnp.arange(req_size, dtype=jnp.int32)
    seq_slots = xor_slot(shard_index ^ seq_ids, seq_size)
    req_slots = xor_slot(group_index ^ req_ids, req_size)

    by_request, _ = gather_xor(states, "req", req_size)
    every, riders = gather_xor(by_request, "seq", seq_size, {0: (norm_gain, norm_bias)})
    norm_gain, norm_bias = riders[0]
    every = every.reshape((seq_size * req_size,) + every.shape[2:])
    every = jnp.take(every, seq_slots[:, None] * req_size + req_slots[None, :], axis=0, mode="clip")
    current_all = every.transpose(2, 1, 3, 0, 4).reshape(steps, total, model_width)
    normed = layer_norm(current_all.reshape(rows, model_width), norm_gain, norm_bias)
    normed_part = lax.dynamic_slice_in_dim(normed, group_index * part_width, part_width, 1)

    part_query = jnp.dot(normed_part, w_query, preferred_element_type=jnp.float32)
    part_keyval = jnp.dot(normed_part, w_keyval, preferred_element_type=jnp.float32)
    first = sum_over(jnp.concatenate([part_query, part_keyval], axis=1), "req", req_size)
    part_up = jnp.dot(normed_part, w_up, preferred_element_type=jnp.float32)
    first, part_up = lax.optimization_barrier((first, part_up))
    request_ids = jnp.arange(total, dtype=jnp.int32)
    own_requests = lax.dynamic_slice_in_dim(placement, group_index * group_rows, group_rows, 0)
    own_serves = own_requests[:, None] == request_ids[None, :]
    slot_lengths = jnp.sum(jnp.where(own_serves, lengths[None, :], 0), axis=1)
    step_offsets = jnp.arange(steps, dtype=jnp.int32)
    positions = slot_lengths[None, :] + step_offsets[:, None]
    own_first = jnp.sum(
        jnp.where(own_serves[None, :, :, None], first.reshape(steps, 1, total, -1), 0.0), axis=2
    )
    own_query = own_first[:, :, :slice_width].astype(jnp.bfloat16)
    own_keyval = own_first[:, :, slice_width:]
    up_part = sum_over(part_up, "req", req_size)
    hidden = jax.nn.gelu(up_part, approximate=False).astype(jnp.bfloat16)
    down_part = jnp.dot(hidden, w_down, preferred_element_type=jnp.float32)

    query_all, riders = gather_xor(own_query, "seq", seq_size, {0: kv_cache})
    kv_cache = riders[0]
    query_all = jnp.take(query_all, seq_slots, axis=0, mode="clip")
    query_all = query_all.transpose(1, 2, 0, 3).reshape(steps, group_rows, model_width)
    flat_positions = positions.reshape(-1)
    query_rows = rotate(
        query_all.astype(jnp.float32).reshape(steps * group_rows, head_count, head_width),
        flat_positions,
    ).astype(jnp.bfloat16)
    own_keyval = own_keyval.reshape(steps * group_rows, 2 * head_width)
    new_key = rotate(own_keyval[:, None, :head_width], flat_positions)[:, 0, :]
    new_entry = jnp.concatenate([new_key, own_keyval[:, head_width:]], axis=-1).astype(jnp.bfloat16)
    new_entry = new_entry.reshape(steps, group_rows, 2 * head_width)

    local_slots = jnp.arange(seg_length, dtype=jnp.int32)
    global_positions = shard_index * seg_length + local_slots
    cache_now = kv_cache
    for step_index in range(steps):
        write_mask = global_positions[None, :] == positions[step_index][:, None]
        cache_now = jnp.where(write_mask[:, :, None], new_entry[step_index][:, None, :], cache_now)

    key_rows = cache_now[:, :, :head_width]
    value_rows = cache_now[:, :, head_width:]
    query_heads = (
        query_rows.reshape(steps, group_rows, head_count, head_width)
        .transpose(1, 0, 2, 3)
        .reshape(group_rows, steps * head_count, head_width)
    )
    scores = jnp.einsum(
        "gqd,gsd->gqs", query_heads, key_rows, preferred_element_type=jnp.float32
    ) * head_width ** (-0.5)
    head_positions = jnp.repeat(positions.T, head_count, axis=1)
    valid = global_positions[None, None, :] <= head_positions[:, :, None]
    local_peak = jnp.max(jnp.where(valid, scores, NEGATIVE), axis=-1)
    weights = jnp.where(valid, jnp.exp(scores - local_peak[:, :, None]), 0.0)
    local_total = jnp.sum(weights, axis=-1)
    local_weighted = jnp.einsum(
        "gqs,gsd->gqd", weights, value_rows, preferred_element_type=jnp.float32
    )

    own_mixed, down_part = merge_over(
        local_peak, local_total, local_weighted, "seq", seq_size, down_part, steps, slice_width
    )
    own_mixed = own_mixed.transpose(1, 0, 2).astype(jnp.bfloat16)
    every_mixed = gather_xor(own_mixed, "req", req_size)[0]
    serves = placement[:, None] == request_ids[None, :]
    inverse = jnp.sum(jnp.where(serves, request_ids[:, None], 0), axis=0)
    mixed_rows = xor_slot(group_index ^ (inverse // group_rows), req_size) * group_rows + (
        inverse % group_rows
    )
    mixed_part = every_mixed.transpose(1, 0, 2, 3).reshape(steps, total, slice_width)
    mixed_part = jnp.take(mixed_part, mixed_rows, axis=1, mode="clip").reshape(rows, slice_width)

    partial_sum = jnp.dot(mixed_part, w_out, preferred_element_type=jnp.float32) + down_part
    chunks = seq_size // req_size
    by_request = partial_sum.reshape(steps, total, part_width)
    blocks = by_request.reshape(steps, req_size, group_rows, chunks, slice_width)
    blocks = blocks.transpose(1, 3, 0, 2, 4).reshape(seq_size, steps, group_rows, slice_width)
    levels = seq_size.bit_length() - 1
    half = seq_size // 2
    pair = scatter_sum(blocks, "seq", seq_size, levels - 1)
    high = shard_index >= half
    own_block = jnp.where(high, pair[1], pair[0])
    other_block = jnp.where(high, pair[0], pair[1])

    def owner(source_group, block):
        return (block // chunks) * seq_size + source_group * chunks + block % chunks

    own_routes, other_routes = [], []
    for source_group in range(req_size):
        for block in range(seq_size):
            source = source_group * seq_size + block
            own_routes.append((source, owner(source_group, block)))
            other_routes.append((source, owner(source_group, block ^ half)))
    own_branch = lax.ppermute(own_block, ALL, own_routes) + lax.ppermute(
        other_block, ALL, other_routes
    )
    new_states = (states.astype(jnp.float32) + own_branch).astype(jnp.bfloat16)
    return (new_states, cache_now)


def solution(mesh):
    in_specs = (
        P(None, "req", "seq"),
        P("req", "seq", None),
        P(),
        P(),
        P(),
        P(),
        P("req", "seq"),
        P("req", None),
        P("seq", "req"),
        P("req", "seq"),
        P("seq", "req"),
    )
    out_specs = (P(None, "req", "seq"), P("req", "seq", None))
    return jax.shard_map(shards, mesh=mesh, in_specs=in_specs, out_specs=out_specs, check_vma=False)
```

```python
import jax
import jax.numpy as jnp
from jax import lax
from jax.sharding import PartitionSpec as P


EPSILON = 1e-05
NEGATIVE = -1e30
ALL = ("req", "seq")


def xor_pairs(size, bit):
    return [(index, index ^ bit) for index in range(size)]


def gather_xor(block, axis, size, riders=None):
    levels = size.bit_length() - 1
    riders = dict(riders or {})
    stacked = block
    for level in range(levels):
        bit = 2 ** (levels - 1 - level)
        stacked = jnp.stack([stacked, lax.ppermute(stacked, axis, xor_pairs(size, bit))])
        if level in riders:
            stacked, riders[level] = lax.optimization_barrier((stacked, riders[level]))
    return stacked.reshape((size,) + block.shape), riders


def xor_slot(offset, size):
    levels = size.bit_length() - 1
    position = jnp.zeros_like(offset)
    for level in range(levels):
        bit = 2 ** (levels - 1 - level)
        position = position + ((offset // bit) % 2) * (2 ** level)
    return position


def sum_over(value, axis, size):
    bit = 1
    while bit < size:
        value = value + lax.ppermute(value, axis, xor_pairs(size, bit))
        bit *= 2
    return value


def scatter_sum(blocks, axis, size, rounds):
    index = lax.axis_index(axis)
    levels = size.bit_length() - 1
    blocks = blocks.reshape((2,) * levels + blocks.shape[1:])
    for level in range(rounds):
        bit = 2 ** level
        place = levels - 1 - level
        high = (index // bit) % 2 == 1
        lower = lax.index_in_dim(blocks, 0, place, keepdims=False)
        upper = lax.index_in_dim(blocks, 1, place, keepdims=False)
        keep = jnp.where(high, upper, lower)
        send = jnp.where(high, lower, upper)
        blocks = keep + lax.ppermute(send, axis, xor_pairs(size, bit))
    return blocks


def split_exact(value):
    high = lax.reduce_precision(value, exponent_bits=8, mantissa_bits=7)
    rest = value - high
    middle = lax.reduce_precision(rest, exponent_bits=8, mantissa_bits=7)
    low = rest - middle
    return [part.astype(jnp.bfloat16) for part in (high, middle, low)]


def join_exact(pieces):
    pieces = pieces.astype(jnp.float32)
    return (pieces[..., 0] + pieces[..., 1]) + pieces[..., 2]


def pack_merge(peak, total, weighted):
    return jnp.concatenate(
        [jnp.stack(split_exact(peak) + split_exact(total), axis=-1), weighted.astype(jnp.bfloat16)],
        axis=-1,
    )


def merge_pair(peak, total, weighted, other):
    peak_second = join_exact(other[..., 0:3])
    total_second = join_exact(other[..., 3:6])
    weighted_second = other[..., 6:].astype(jnp.float32)
    merged_peak = jnp.maximum(peak, peak_second)
    scale_first = jnp.exp(peak - merged_peak)
    scale_second = jnp.exp(peak_second - merged_peak)
    total = total * scale_first + total_second * scale_second
    weighted = weighted * scale_first[..., None] + weighted_second * scale_second[..., None]
    return merged_peak, total, weighted


def merge_over(peak, total, weighted, axis, size, carried, steps, chunk_width, cross=False):
    index = lax.axis_index(axis)
    group_rows, step_heads, head_width = weighted.shape
    head_count = step_heads // steps
    span = min(head_count, (chunk_width + 2 * head_width - 2) // head_width)
    bit = 1
    while bit < size // 2:
        if bit == 4:
            carried, peak, total, weighted = lax.optimization_barrier(
                (carried, peak, total, weighted)
            )
        other = lax.ppermute(pack_merge(peak, total, weighted), axis, xor_pairs(size, bit))
        peak, total, weighted = merge_pair(peak, total, weighted, other)
        bit *= 2

    def first_head(position):
        return jnp.minimum((position * chunk_width) // head_width, head_count - span)

    def window(value, start):
        value = value.reshape((group_rows, steps, head_count) + value.shape[2:])
        return lax.dynamic_slice_in_dim(value, start, span, 2)

    def finish(total, weighted):
        mixed = (weighted / total[..., None]).reshape(group_rows, steps, span * head_width)
        offset = index * chunk_width - own_start * head_width
        return lax.dynamic_slice_in_dim(mixed, offset, chunk_width, 2)

    partner_start = first_head(index ^ bit)
    own_start = first_head(index)
    sent = window(pack_merge(peak, total, weighted), partner_start)
    other = lax.ppermute(sent, axis, xor_pairs(size, bit))
    results = []
    if cross:
        def whole(start):
            return jnp.concatenate(
                [window(peak, start)[..., None], window(total, start)[..., None], window(weighted, start)],
                axis=-1,
            )

        same_routes = [(g * size + s, (1 - g) * size + s) for g in range(2) for s in range(size)]
        partner_routes = [
            (g * size + s, (1 - g) * size + (s ^ bit)) for g in range(2) for s in range(size)
        ]
        cross_same = lax.ppermute(whole(own_start), ALL, same_routes)
        cross_partner = lax.ppermute(whole(partner_start), ALL, partner_routes)
    _, own_total, own_weighted = merge_pair(
        window(peak, own_start), window(total, own_start), window(weighted, own_start), other
    )
    results.append(finish(own_total, own_weighted))
    if cross:
        peak_first, peak_second = cross_same[..., 0], cross_partner[..., 0]
        merged_peak = jnp.maximum(peak_first, peak_second)
        scale_first = jnp.exp(peak_first - merged_peak)
        scale_second = jnp.exp(peak_second - merged_peak)
        cross_total = cross_same[..., 1] * scale_first + cross_partner[..., 1] * scale_second
        cross_weighted = (
            cross_same[..., 2:] * scale_first[..., None] + cross_partner[..., 2:] * scale_second[..., None]
        )
        results.append(finish(cross_total, cross_weighted))
    return results, carried


def layer_norm(row_block, norm_gain, norm_bias):
    values = row_block.astype(jnp.float32)
    average = jnp.mean(values, axis=-1, keepdims=True)
    centered = values - average
    spread = jnp.mean(centered * centered, axis=-1, keepdims=True)
    scaled = centered * lax.rsqrt(spread + EPSILON)
    return (scaled * norm_gain.astype(jnp.float32) + norm_bias.astype(jnp.float32)).astype(
        jnp.bfloat16
    )


def rotate(vectors, positions):
    head_width = vectors.shape[-1]
    half_width = head_width // 2
    frequency = 10000.0 ** (-(jnp.arange(half_width, dtype=jnp.float32) * 2.0) / head_width)
    angles = positions.astype(jnp.float32)[:, None] * frequency[None, :]
    cosine = jnp.concatenate([jnp.cos(angles), jnp.cos(angles)], axis=-1)[:, None, :]
    sine_wave = jnp.concatenate([jnp.sin(angles), jnp.sin(angles)], axis=-1)[:, None, :]
    turned = jnp.concatenate([-vectors[..., half_width:], vectors[..., :half_width]], axis=-1)
    return vectors * cosine + turned * sine_wave


def shards(
    states,
    kv_cache,
    lengths,
    placement,
    norm_gain,
    norm_bias,
    w_query,
    w_keyval,
    w_out,
    w_up,
    w_down,
):
    steps = states.shape[0]
    group_rows = kv_cache.shape[0]
    seg_length = kv_cache.shape[1]
    head_width = kv_cache.shape[2] // 2
    model_width = norm_gain.shape[0]
    head_count = model_width // head_width
    slice_width = states.shape[2]
    part_width = w_query.shape[0]
    total = placement.shape[0]
    req_size = total // group_rows
    seq_size = model_width // slice_width
    rows = steps * total
    group_index = lax.axis_index("req")
    shard_index = lax.axis_index("seq")

    seq_ids = jnp.arange(seq_size, dtype=jnp.int32)
    req_ids = jnp.arange(req_size, dtype=jnp.int32)
    seq_slots = xor_slot(shard_index ^ seq_ids, seq_size)
    req_slots = xor_slot(group_index ^ req_ids, req_size)

    by_request, _ = gather_xor(states, "req", req_size)
    every, riders = gather_xor(by_request, "seq", seq_size, {0: (norm_gain, norm_bias)})
    norm_gain, norm_bias = riders[0]
    every = every.reshape((seq_size * req_size,) + every.shape[2:])
    every = jnp.take(every, seq_slots[:, None] * req_size + req_slots[None, :], axis=0, mode="clip")
    current_all = every.transpose(2, 1, 3, 0, 4).reshape(steps, total, model_width)
    normed = layer_norm(current_all.reshape(rows, model_width), norm_gain, norm_bias)
    normed_part = lax.dynamic_slice_in_dim(normed, group_index * part_width, part_width, 1)

    part_query = jnp.dot(normed_part, w_query, preferred_element_type=jnp.float32)
    part_keyval = jnp.dot(normed_part, w_keyval, preferred_element_type=jnp.float32)
    first = sum_over(jnp.concatenate([part_query, part_keyval], axis=1), "req", req_size)
    part_up = jnp.dot(normed_part, w_up, preferred_element_type=jnp.float32)
    first, part_up = lax.optimization_barrier((first, part_up))
    request_ids = jnp.arange(total, dtype=jnp.int32)
    own_requests = lax.dynamic_slice_in_dim(placement, group_index * group_rows, group_rows, 0)
    own_serves = own_requests[:, None] == request_ids[None, :]
    slot_lengths = jnp.sum(jnp.where(own_serves, lengths[None, :], 0), axis=1)
    step_offsets = jnp.arange(steps, dtype=jnp.int32)
    positions = slot_lengths[None, :] + step_offsets[:, None]
    own_first = jnp.sum(
        jnp.where(own_serves[None, :, :, None], first.reshape(steps, 1, total, -1), 0.0), axis=2
    )
    own_query = own_first[:, :, :slice_width].astype(jnp.bfloat16)
    own_keyval = own_first[:, :, slice_width:]
    up_part = sum_over(part_up, "req", req_size)
    hidden = jax.nn.gelu(up_part, approximate=False).astype(jnp.bfloat16)
    down_part = jnp.dot(hidden, w_down, preferred_element_type=jnp.float32)

    query_all, riders = gather_xor(own_query, "seq", seq_size, {0: kv_cache})
    kv_cache = riders[0]
    query_all = jnp.take(query_all, seq_slots, axis=0, mode="clip")
    query_all = query_all.transpose(1, 2, 0, 3).reshape(steps, group_rows, model_width)
    flat_positions = positions.reshape(-1)
    query_rows = rotate(
        query_all.astype(jnp.float32).reshape(steps * group_rows, head_count, head_width),
        flat_positions,
    ).astype(jnp.bfloat16)
    own_keyval = own_keyval.reshape(steps * group_rows, 2 * head_width)
    new_key = rotate(own_keyval[:, None, :head_width], flat_positions)[:, 0, :]
    new_entry = jnp.concatenate([new_key, own_keyval[:, head_width:]], axis=-1).astype(jnp.bfloat16)
    new_entry = new_entry.reshape(steps, group_rows, 2 * head_width)

    local_slots = jnp.arange(seg_length, dtype=jnp.int32)
    global_positions = shard_index * seg_length + local_slots
    cache_now = kv_cache
    for step_index in range(steps):
        write_mask = global_positions[None, :] == positions[step_index][:, None]
        cache_now = jnp.where(write_mask[:, :, None], new_entry[step_index][:, None, :], cache_now)

    key_rows = cache_now[:, :, :head_width]
    value_rows = cache_now[:, :, head_width:]
    query_heads = (
        query_rows.reshape(steps, group_rows, head_count, head_width)
        .transpose(1, 0, 2, 3)
        .reshape(group_rows, steps * head_count, head_width)
    )
    scores = jnp.einsum(
        "gqd,gsd->gqs", query_heads, key_rows, preferred_element_type=jnp.float32
    ) * head_width ** (-0.5)
    head_positions = jnp.repeat(positions.T, head_count, axis=1)
    valid = global_positions[None, None, :] <= head_positions[:, :, None]
    local_peak = jnp.max(jnp.where(valid, scores, NEGATIVE), axis=-1)
    weights = jnp.where(valid, jnp.exp(scores - local_peak[:, :, None]), 0.0)
    local_total = jnp.sum(weights, axis=-1)
    local_weighted = jnp.einsum(
        "gqs,gsd->gqd", weights, value_rows, preferred_element_type=jnp.float32
    )

    fold = req_size == 2
    chunk_mixed, down_part = merge_over(
        local_peak, local_total, local_weighted, "seq", seq_size, down_part, steps, slice_width, fold
    )
    chunk_mixed = [part.transpose(1, 0, 2).astype(jnp.bfloat16) for part in chunk_mixed]
    serves = placement[:, None] == request_ids[None, :]
    inverse = jnp.sum(jnp.where(serves, request_ids[:, None], 0), axis=0)
    if fold:
        own_mixed, other_mixed = chunk_mixed
        every_mixed = jnp.where(
            group_index == 0,
            jnp.stack([own_mixed, other_mixed]),
            jnp.stack([other_mixed, own_mixed]),
        )
        mixed_rows = inverse
    else:
        every_mixed = gather_xor(chunk_mixed[0], "req", req_size)[0]
        mixed_rows = xor_slot(group_index ^ (inverse // group_rows), req_size) * group_rows + (
            inverse % group_rows
        )
    mixed_part = every_mixed.transpose(1, 0, 2, 3).reshape(steps, total, slice_width)
    mixed_part = jnp.take(mixed_part, mixed_rows, axis=1, mode="clip").reshape(rows, slice_width)

    partial_sum = jnp.dot(mixed_part, w_out, preferred_element_type=jnp.float32) + down_part
    chunks = seq_size // req_size
    by_request = partial_sum.reshape(steps, total, part_width)
    blocks = by_request.reshape(steps, req_size, group_rows, chunks, slice_width)
    blocks = blocks.transpose(1, 3, 0, 2, 4).reshape(seq_size, steps, group_rows, slice_width)
    levels = seq_size.bit_length() - 1
    half = seq_size // 2
    pair = scatter_sum(blocks, "seq", seq_size, levels - 1)
    high = shard_index >= half
    own_block = jnp.where(high, pair[1], pair[0])
    other_block = jnp.where(high, pair[0], pair[1])

    def owner(source_group, block):
        return (block // chunks) * seq_size + source_group * chunks + block % chunks

    own_routes, other_routes = [], []
    for source_group in range(req_size):
        for block in range(seq_size):
            source = source_group * seq_size + block
            own_routes.append((source, owner(source_group, block)))
            other_routes.append((source, owner(source_group, block ^ half)))
    own_branch = lax.ppermute(own_block, ALL, own_routes) + lax.ppermute(
        other_block, ALL, other_routes
    )
    new_states = (states.astype(jnp.float32) + own_branch).astype(jnp.bfloat16)
    return (new_states, cache_now)


def solution(mesh):
    in_specs = (
        P(None, "req", "seq"),
        P("req", "seq", None),
        P(),
        P(),
        P(),
        P(),
        P("req", "seq"),
        P("req", None),
        P("seq", "req"),
        P("req", "seq"),
        P("seq", "req"),
    )
    out_specs = (P(None, "req", "seq"), P("req", "seq", None))
    return jax.shard_map(shards, mesh=mesh, in_specs=in_specs, out_specs=out_specs, check_vma=False)
```

```python
import jax
import jax.numpy as jnp
from jax import lax
from jax.sharding import PartitionSpec as P


EPSILON = 1e-05
NEGATIVE = -1e30
ALL = ("req", "seq")


def xor_pairs(size, bit):
    return [(index, index ^ bit) for index in range(size)]


def gather_xor(block, axis, size, riders=None):
    levels = size.bit_length() - 1
    riders = dict(riders or {})
    stacked = block
    for level in range(levels):
        bit = 2 ** (levels - 1 - level)
        stacked = jnp.stack([stacked, lax.ppermute(stacked, axis, xor_pairs(size, bit))])
        if level in riders:
            stacked, riders[level] = lax.optimization_barrier((stacked, riders[level]))
    return stacked.reshape((size,) + block.shape), riders


def xor_slot(offset, size):
    levels = size.bit_length() - 1
    position = jnp.zeros_like(offset)
    for level in range(levels):
        bit = 2 ** (levels - 1 - level)
        position = position + ((offset // bit) % 2) * (2 ** level)
    return position


def sum_over(value, axis, size):
    bit = 1
    while bit < size:
        value = value + lax.ppermute(value, axis, xor_pairs(size, bit))
        bit *= 2
    return value


def scatter_sum(blocks, axis, size, rounds):
    index = lax.axis_index(axis)
    levels = size.bit_length() - 1
    blocks = blocks.reshape((2,) * levels + blocks.shape[1:])
    for level in range(rounds):
        bit = 2 ** level
        place = levels - 1 - level
        high = (index // bit) % 2 == 1
        lower = lax.index_in_dim(blocks, 0, place, keepdims=False)
        upper = lax.index_in_dim(blocks, 1, place, keepdims=False)
        keep = jnp.where(high, upper, lower)
        send = jnp.where(high, lower, upper)
        blocks = keep + lax.ppermute(send, axis, xor_pairs(size, bit))
    return blocks


def split_exact(value):
    high = lax.reduce_precision(value, exponent_bits=8, mantissa_bits=7)
    rest = value - high
    middle = lax.reduce_precision(rest, exponent_bits=8, mantissa_bits=7)
    low = rest - middle
    return [part.astype(jnp.bfloat16) for part in (high, middle, low)]


def join_exact(pieces):
    pieces = pieces.astype(jnp.float32)
    return (pieces[..., 0] + pieces[..., 1]) + pieces[..., 2]


def pack_merge(peak, total, weighted):
    return jnp.concatenate(
        [jnp.stack(split_exact(peak) + split_exact(total), axis=-1), weighted.astype(jnp.bfloat16)],
        axis=-1,
    )


def merge_pair(peak, total, weighted, other):
    peak_second = join_exact(other[..., 0:3])
    total_second = join_exact(other[..., 3:6])
    weighted_second = other[..., 6:].astype(jnp.float32)
    merged_peak = jnp.maximum(peak, peak_second)
    scale_first = jnp.exp(peak - merged_peak)
    scale_second = jnp.exp(peak_second - merged_peak)
    total = total * scale_first + total_second * scale_second
    weighted = weighted * scale_first[..., None] + weighted_second * scale_second[..., None]
    return merged_peak, total, weighted


def merge_over(peak, total, weighted, axis, size, carried, steps, chunk_width):
    index = lax.axis_index(axis)
    group_rows, step_heads, head_width = weighted.shape
    head_count = step_heads // steps
    span = min(head_count, (chunk_width + 2 * head_width - 2) // head_width)
    bit = 1
    while bit < size // 2:
        if bit == 4:
            carried, peak, total, weighted = lax.optimization_barrier(
                (carried, peak, total, weighted)
            )
        other = lax.ppermute(pack_merge(peak, total, weighted), axis, xor_pairs(size, bit))
        peak, total, weighted = merge_pair(peak, total, weighted, other)
        bit *= 2

    def first_head(position):
        return jnp.minimum((position * chunk_width) // head_width, head_count - span)

    def window(value, start):
        value = value.reshape((group_rows, steps, head_count) + value.shape[2:])
        return lax.dynamic_slice_in_dim(value, start, span, 2)

    partner_start = first_head(index ^ bit)
    own_start = first_head(index)
    sent = window(pack_merge(peak, total, weighted), partner_start)
    other = lax.ppermute(sent, axis, xor_pairs(size, bit))
    _, total, weighted = merge_pair(
        window(peak, own_start), window(total, own_start), window(weighted, own_start), other
    )
    mixed = (weighted / total[..., None]).reshape(group_rows, steps, span * head_width)
    offset = index * chunk_width - own_start * head_width
    return lax.dynamic_slice_in_dim(mixed, offset, chunk_width, 2), carried


def layer_norm(row_block, norm_gain, norm_bias):
    values = row_block.astype(jnp.float32)
    average = jnp.mean(values, axis=-1, keepdims=True)
    centered = values - average
    spread = jnp.mean(centered * centered, axis=-1, keepdims=True)
    scaled = centered * lax.rsqrt(spread + EPSILON)
    return (scaled * norm_gain.astype(jnp.float32) + norm_bias.astype(jnp.float32)).astype(
        jnp.bfloat16
    )


def rotate(vectors, positions):
    head_width = vectors.shape[-1]
    half_width = head_width // 2
    frequency = 10000.0 ** (-(jnp.arange(half_width, dtype=jnp.float32) * 2.0) / head_width)
    angles = positions.astype(jnp.float32)[:, None] * frequency[None, :]
    cosine = jnp.concatenate([jnp.cos(angles), jnp.cos(angles)], axis=-1)[:, None, :]
    sine_wave = jnp.concatenate([jnp.sin(angles), jnp.sin(angles)], axis=-1)[:, None, :]
    turned = jnp.concatenate([-vectors[..., half_width:], vectors[..., :half_width]], axis=-1)
    return vectors * cosine + turned * sine_wave


def shards(
    states,
    kv_cache,
    lengths,
    placement,
    norm_gain,
    norm_bias,
    w_query,
    w_keyval,
    w_out,
    w_up,
    w_down,
):
    steps = states.shape[0]
    group_rows = kv_cache.shape[0]
    seg_length = kv_cache.shape[1]
    head_width = kv_cache.shape[2] // 2
    model_width = norm_gain.shape[0]
    head_count = model_width // head_width
    slice_width = states.shape[2]
    part_width = w_query.shape[0]
    total = placement.shape[0]
    req_size = total // group_rows
    seq_size = model_width // slice_width
    rows = steps * total
    group_index = lax.axis_index("req")
    shard_index = lax.axis_index("seq")

    seq_ids = jnp.arange(seq_size, dtype=jnp.int32)
    req_ids = jnp.arange(req_size, dtype=jnp.int32)
    seq_slots = xor_slot(shard_index ^ seq_ids, seq_size)
    req_slots = xor_slot(group_index ^ req_ids, req_size)

    rounds = [("seq", seq_size, 1)] + [("req", req_size, 2 ** b) for b in range(req_size.bit_length() - 2, -1, -1)]
    rounds += [("seq", seq_size, 2 ** b) for b in range(seq_size.bit_length() - 2, 0, -1)]
    stacked = states
    for number, (axis, size, bit) in enumerate(rounds):
        stacked = jnp.stack([stacked, lax.ppermute(stacked, axis, xor_pairs(size, bit))])
        if number == 1:
            stacked, (norm_gain, norm_bias) = lax.optimization_barrier(
                (stacked, (norm_gain, norm_bias))
            )
    every = stacked.reshape((2 ** len(rounds),) + states.shape)
    seq_offsets = shard_index ^ seq_ids
    req_offsets = group_index ^ req_ids
    positions_all = jnp.zeros((seq_size, req_size), jnp.int32)
    for number, (axis, size, bit) in enumerate(rounds):
        offsets = seq_offsets[:, None] if axis == "seq" else req_offsets[None, :]
        positions_all = positions_all + ((offsets // bit) % 2) * (2 ** number)
    every = jnp.take(every, positions_all, axis=0, mode="clip")
    current_all = every.transpose(2, 1, 3, 0, 4).reshape(steps, total, model_width)
    normed = layer_norm(current_all.reshape(rows, model_width), norm_gain, norm_bias)
    normed_part = lax.dynamic_slice_in_dim(normed, group_index * part_width, part_width, 1)

    part_query = jnp.dot(normed_part, w_query, preferred_element_type=jnp.float32)
    part_keyval = jnp.dot(normed_part, w_keyval, preferred_element_type=jnp.float32)
    first = sum_over(jnp.concatenate([part_query, part_keyval], axis=1), "req", req_size)
    part_up = jnp.dot(normed_part, w_up, preferred_element_type=jnp.float32)
    first, part_up = lax.optimization_barrier((first, part_up))
    request_ids = jnp.arange(total, dtype=jnp.int32)
    own_requests = lax.dynamic_slice_in_dim(placement, group_index * group_rows, group_rows, 0)
    own_serves = own_requests[:, None] == request_ids[None, :]
    slot_lengths = jnp.sum(jnp.where(own_serves, lengths[None, :], 0), axis=1)
    step_offsets = jnp.arange(steps, dtype=jnp.int32)
    positions = slot_lengths[None, :] + step_offsets[:, None]
    own_first = jnp.sum(
        jnp.where(own_serves[None, :, :, None], first.reshape(steps, 1, total, -1), 0.0), axis=2
    )
    own_query = own_first[:, :, :slice_width].astype(jnp.bfloat16)
    own_keyval = own_first[:, :, slice_width:]
    up_part = sum_over(part_up, "req", req_size)
    hidden = jax.nn.gelu(up_part, approximate=False).astype(jnp.bfloat16)
    down_part = jnp.dot(hidden, w_down, preferred_element_type=jnp.float32)

    query_all, riders = gather_xor(own_query, "seq", seq_size, {0: kv_cache})
    kv_cache = riders[0]
    query_all = jnp.take(query_all, seq_slots, axis=0, mode="clip")
    query_all = query_all.transpose(1, 2, 0, 3).reshape(steps, group_rows, model_width)
    flat_positions = positions.reshape(-1)
    query_rows = rotate(
        query_all.astype(jnp.float32).reshape(steps * group_rows, head_count, head_width),
        flat_positions,
    ).astype(jnp.bfloat16)
    own_keyval = own_keyval.reshape(steps * group_rows, 2 * head_width)
    new_key = rotate(own_keyval[:, None, :head_width], flat_positions)[:, 0, :]
    new_entry = jnp.concatenate([new_key, own_keyval[:, head_width:]], axis=-1).astype(jnp.bfloat16)
    new_entry = new_entry.reshape(steps, group_rows, 2 * head_width)

    local_slots = jnp.arange(seg_length, dtype=jnp.int32)
    global_positions = shard_index * seg_length + local_slots
    cache_now = kv_cache
    for step_index in range(steps):
        write_mask = global_positions[None, :] == positions[step_index][:, None]
        cache_now = jnp.where(write_mask[:, :, None], new_entry[step_index][:, None, :], cache_now)

    key_rows = cache_now[:, :, :head_width]
    value_rows = cache_now[:, :, head_width:]
    query_heads = (
        query_rows.reshape(steps, group_rows, head_count, head_width)
        .transpose(1, 0, 2, 3)
        .reshape(group_rows, steps * head_count, head_width)
    )
    scores = jnp.einsum(
        "gqd,gsd->gqs", query_heads, key_rows, preferred_element_type=jnp.float32
    ) * head_width ** (-0.5)
    head_positions = jnp.repeat(positions.T, head_count, axis=1)
    valid = global_positions[None, None, :] <= head_positions[:, :, None]
    local_peak = jnp.max(jnp.where(valid, scores, NEGATIVE), axis=-1)
    weights = jnp.where(valid, jnp.exp(scores - local_peak[:, :, None]), 0.0)
    local_total = jnp.sum(weights, axis=-1)
    local_weighted = jnp.einsum(
        "gqs,gsd->gqd", weights, value_rows, preferred_element_type=jnp.float32
    )

    own_mixed, down_part = merge_over(
        local_peak, local_total, local_weighted, "seq", seq_size, down_part, steps, slice_width
    )
    own_mixed = own_mixed.transpose(1, 0, 2).astype(jnp.bfloat16)
    every_mixed = gather_xor(own_mixed, "req", req_size)[0]
    serves = placement[:, None] == request_ids[None, :]
    inverse = jnp.sum(jnp.where(serves, request_ids[:, None], 0), axis=0)
    mixed_rows = xor_slot(group_index ^ (inverse // group_rows), req_size) * group_rows + (
        inverse % group_rows
    )
    mixed_part = every_mixed.transpose(1, 0, 2, 3).reshape(steps, total, slice_width)
    mixed_part = jnp.take(mixed_part, mixed_rows, axis=1, mode="clip").reshape(rows, slice_width)

    partial_sum = jnp.dot(mixed_part, w_out, preferred_element_type=jnp.float32) + down_part
    chunks = seq_size // req_size
    by_request = partial_sum.reshape(steps, total, part_width)
    blocks = by_request.reshape(steps, req_size, group_rows, chunks, slice_width)
    blocks = blocks.transpose(1, 3, 0, 2, 4).reshape(seq_size, steps, group_rows, slice_width)
    levels = seq_size.bit_length() - 1
    half = seq_size // 2
    pair = scatter_sum(blocks, "seq", seq_size, levels - 1)
    high = shard_index >= half
    own_block = jnp.where(high, pair[1], pair[0])
    other_block = jnp.where(high, pair[0], pair[1])

    def owner(source_group, block):
        return (block // chunks) * seq_size + source_group * chunks + block % chunks

    own_routes, other_routes = [], []
    for source_group in range(req_size):
        for block in range(seq_size):
            source = source_group * seq_size + block
            own_routes.append((source, owner(source_group, block)))
            other_routes.append((source, owner(source_group, block ^ half)))
    own_branch = lax.ppermute(own_block, ALL, own_routes) + lax.ppermute(
        other_block, ALL, other_routes
    )
    new_states = (states.astype(jnp.float32) + own_branch).astype(jnp.bfloat16)
    return (new_states, cache_now)


def solution(mesh):
    in_specs = (
        P(None, "req", "seq"),
        P("req", "seq", None),
        P(),
        P(),
        P(),
        P(),
        P("req", "seq"),
        P("req", None),
        P("seq", "req"),
        P("req", "seq"),
        P("seq", "req"),
    )
    out_specs = (P(None, "req", "seq"), P("req", "seq", None))
    return jax.shard_map(shards, mesh=mesh, in_specs=in_specs, out_specs=out_specs, check_vma=False)
```

```python
import jax
import jax.numpy as jnp
from jax import lax
from jax.sharding import PartitionSpec as P


EPSILON = 1e-05
NEGATIVE = -1e30
ALL = ("req", "seq")


def xor_pairs(size, bit):
    return [(index, index ^ bit) for index in range(size)]


def gather_xor(block, axis, size, riders=None):
    levels = size.bit_length() - 1
    riders = dict(riders or {})
    stacked = block
    for level in range(levels):
        bit = 2 ** (levels - 1 - level)
        stacked = jnp.stack([stacked, lax.ppermute(stacked, axis, xor_pairs(size, bit))])
        if level in riders:
            stacked, riders[level] = lax.optimization_barrier((stacked, riders[level]))
    return stacked.reshape((size,) + block.shape), riders


def xor_slot(offset, size):
    levels = size.bit_length() - 1
    position = jnp.zeros_like(offset)
    for level in range(levels):
        bit = 2 ** (levels - 1 - level)
        position = position + ((offset // bit) % 2) * (2 ** level)
    return position


def sum_over(value, axis, size):
    bit = 1
    while bit < size:
        value = value + lax.ppermute(value, axis, xor_pairs(size, bit))
        bit *= 2
    return value


def scatter_sum(blocks, axis, size, rounds):
    index = lax.axis_index(axis)
    levels = size.bit_length() - 1
    blocks = blocks.reshape((2,) * levels + blocks.shape[1:])
    for level in range(rounds):
        bit = 2 ** level
        place = levels - 1 - level
        high = (index // bit) % 2 == 1
        lower = lax.index_in_dim(blocks, 0, place, keepdims=False)
        upper = lax.index_in_dim(blocks, 1, place, keepdims=False)
        keep = jnp.where(high, upper, lower)
        send = jnp.where(high, lower, upper)
        blocks = keep + lax.ppermute(send, axis, xor_pairs(size, bit))
    return blocks


def split_exact(value):
    high = lax.reduce_precision(value, exponent_bits=8, mantissa_bits=7)
    rest = value - high
    middle = lax.reduce_precision(rest, exponent_bits=8, mantissa_bits=7)
    low = rest - middle
    return [part.astype(jnp.bfloat16) for part in (high, middle, low)]


def join_exact(pieces):
    pieces = pieces.astype(jnp.float32)
    return (pieces[..., 0] + pieces[..., 1]) + pieces[..., 2]


def pack_merge(peak, total, weighted):
    return jnp.concatenate(
        [jnp.stack(split_exact(peak) + split_exact(total), axis=-1), weighted.astype(jnp.bfloat16)],
        axis=-1,
    )


def merge_pair(peak, total, weighted, other):
    peak_second = join_exact(other[..., 0:3])
    total_second = join_exact(other[..., 3:6])
    weighted_second = other[..., 6:].astype(jnp.float32)
    merged_peak = jnp.maximum(peak, peak_second)
    scale_first = jnp.exp(peak - merged_peak)
    scale_second = jnp.exp(peak_second - merged_peak)
    total = total * scale_first + total_second * scale_second
    weighted = weighted * scale_first[..., None] + weighted_second * scale_second[..., None]
    return merged_peak, total, weighted


def merge_over(peak, total, weighted, axis, size, carried, steps, chunk_width):
    index = lax.axis_index(axis)
    group_rows, step_heads, head_width = weighted.shape
    head_count = step_heads // steps
    span = min(head_count, (chunk_width + 2 * head_width - 2) // head_width)
    bit = 1
    while bit < size // 2:
        if bit == 4:
            carried[0], peak, total, weighted = lax.optimization_barrier(
                (carried[0], peak, total, weighted)
            )
        other = lax.ppermute(pack_merge(peak, total, weighted), axis, xor_pairs(size, bit))
        peak, total, weighted = merge_pair(peak, total, weighted, other)
        bit *= 2

    def first_head(position):
        return jnp.minimum((position * chunk_width) // head_width, head_count - span)

    def window(value, start):
        value = value.reshape((group_rows, steps, head_count) + value.shape[2:])
        return lax.dynamic_slice_in_dim(value, start, span, 2)

    if size >= 16:
        carried[1], peak, total, weighted = lax.optimization_barrier(
            (carried[1], peak, total, weighted)
        )
    partner_start = first_head(index ^ bit)
    own_start = first_head(index)
    sent = window(pack_merge(peak, total, weighted), partner_start)
    other = lax.ppermute(sent, axis, xor_pairs(size, bit))
    _, total, weighted = merge_pair(
        window(peak, own_start), window(total, own_start), window(weighted, own_start), other
    )
    mixed = (weighted / total[..., None]).reshape(group_rows, steps, span * head_width)
    offset = index * chunk_width - own_start * head_width
    return lax.dynamic_slice_in_dim(mixed, offset, chunk_width, 2), carried


def layer_norm(row_block, norm_gain, norm_bias):
    values = row_block.astype(jnp.float32)
    average = jnp.mean(values, axis=-1, keepdims=True)
    centered = values - average
    spread = jnp.mean(centered * centered, axis=-1, keepdims=True)
    scaled = centered * lax.rsqrt(spread + EPSILON)
    return (scaled * norm_gain.astype(jnp.float32) + norm_bias.astype(jnp.float32)).astype(
        jnp.bfloat16
    )


def rotate(vectors, positions):
    head_width = vectors.shape[-1]
    half_width = head_width // 2
    frequency = 10000.0 ** (-(jnp.arange(half_width, dtype=jnp.float32) * 2.0) / head_width)
    angles = positions.astype(jnp.float32)[:, None] * frequency[None, :]
    cosine = jnp.concatenate([jnp.cos(angles), jnp.cos(angles)], axis=-1)[:, None, :]
    sine_wave = jnp.concatenate([jnp.sin(angles), jnp.sin(angles)], axis=-1)[:, None, :]
    turned = jnp.concatenate([-vectors[..., half_width:], vectors[..., :half_width]], axis=-1)
    return vectors * cosine + turned * sine_wave


def shards(
    states,
    kv_cache,
    lengths,
    placement,
    norm_gain,
    norm_bias,
    w_query,
    w_keyval,
    w_out,
    w_up,
    w_down,
):
    steps = states.shape[0]
    group_rows = kv_cache.shape[0]
    seg_length = kv_cache.shape[1]
    head_width = kv_cache.shape[2] // 2
    model_width = norm_gain.shape[0]
    head_count = model_width // head_width
    slice_width = states.shape[2]
    part_width = w_query.shape[0]
    total = placement.shape[0]
    req_size = total // group_rows
    seq_size = model_width // slice_width
    rows = steps * total
    group_index = lax.axis_index("req")
    shard_index = lax.axis_index("seq")

    seq_ids = jnp.arange(seq_size, dtype=jnp.int32)
    req_ids = jnp.arange(req_size, dtype=jnp.int32)
    seq_slots = xor_slot(shard_index ^ seq_ids, seq_size)
    req_slots = xor_slot(group_index ^ req_ids, req_size)

    by_request, _ = gather_xor(states, "req", req_size)
    every, riders = gather_xor(by_request, "seq", seq_size, {0: (norm_gain, norm_bias)})
    norm_gain, norm_bias = riders[0]
    every = every.reshape((seq_size * req_size,) + every.shape[2:])
    every = jnp.take(every, seq_slots[:, None] * req_size + req_slots[None, :], axis=0, mode="clip")
    current_all = every.transpose(2, 1, 3, 0, 4).reshape(steps, total, model_width)
    normed = layer_norm(current_all.reshape(rows, model_width), norm_gain, norm_bias)
    normed_part = lax.dynamic_slice_in_dim(normed, group_index * part_width, part_width, 1)

    part_query = jnp.dot(normed_part, w_query, preferred_element_type=jnp.float32)
    part_keyval = jnp.dot(normed_part, w_keyval, preferred_element_type=jnp.float32)
    first = sum_over(jnp.concatenate([part_query, part_keyval], axis=1), "req", req_size)
    part_up = jnp.dot(normed_part, w_up, preferred_element_type=jnp.float32)
    first, part_up = lax.optimization_barrier((first, part_up))
    request_ids = jnp.arange(total, dtype=jnp.int32)
    own_requests = lax.dynamic_slice_in_dim(placement, group_index * group_rows, group_rows, 0)
    own_serves = own_requests[:, None] == request_ids[None, :]
    slot_lengths = jnp.sum(jnp.where(own_serves, lengths[None, :], 0), axis=1)
    step_offsets = jnp.arange(steps, dtype=jnp.int32)
    positions = slot_lengths[None, :] + step_offsets[:, None]
    own_first = jnp.sum(
        jnp.where(own_serves[None, :, :, None], first.reshape(steps, 1, total, -1), 0.0), axis=2
    )
    own_query = own_first[:, :, :slice_width].astype(jnp.bfloat16)
    own_keyval = own_first[:, :, slice_width:]
    up_part = sum_over(part_up, "req", req_size)
    hidden = jax.nn.gelu(up_part, approximate=False).astype(jnp.bfloat16)
    down_half = w_down.shape[1] // 2
    down_parts = [
        jnp.dot(hidden, w_down[:, :down_half], preferred_element_type=jnp.float32),
        jnp.dot(hidden, w_down[:, down_half:], preferred_element_type=jnp.float32),
    ]

    query_all, riders = gather_xor(own_query, "seq", seq_size, {0: kv_cache})
    kv_cache = riders[0]
    query_all = jnp.take(query_all, seq_slots, axis=0, mode="clip")
    query_all = query_all.transpose(1, 2, 0, 3).reshape(steps, group_rows, model_width)
    flat_positions = positions.reshape(-1)
    query_rows = rotate(
        query_all.astype(jnp.float32).reshape(steps * group_rows, head_count, head_width),
        flat_positions,
    ).astype(jnp.bfloat16)
    own_keyval = own_keyval.reshape(steps * group_rows, 2 * head_width)
    new_key = rotate(own_keyval[:, None, :head_width], flat_positions)[:, 0, :]
    new_entry = jnp.concatenate([new_key, own_keyval[:, head_width:]], axis=-1).astype(jnp.bfloat16)
    new_entry = new_entry.reshape(steps, group_rows, 2 * head_width)

    local_slots = jnp.arange(seg_length, dtype=jnp.int32)
    global_positions = shard_index * seg_length + local_slots
    cache_now = kv_cache
    for step_index in range(steps):
        write_mask = global_positions[None, :] == positions[step_index][:, None]
        cache_now = jnp.where(write_mask[:, :, None], new_entry[step_index][:, None, :], cache_now)

    key_rows = cache_now[:, :, :head_width]
    value_rows = cache_now[:, :, head_width:]
    query_heads = (
        query_rows.reshape(steps, group_rows, head_count, head_width)
        .transpose(1, 0, 2, 3)
        .reshape(group_rows, steps * head_count, head_width)
    )
    scores = jnp.einsum(
        "gqd,gsd->gqs", query_heads, key_rows, preferred_element_type=jnp.float32
    ) * head_width ** (-0.5)
    head_positions = jnp.repeat(positions.T, head_count, axis=1)
    valid = global_positions[None, None, :] <= head_positions[:, :, None]
    local_peak = jnp.max(jnp.where(valid, scores, NEGATIVE), axis=-1)
    weights = jnp.where(valid, jnp.exp(scores - local_peak[:, :, None]), 0.0)
    local_total = jnp.sum(weights, axis=-1)
    local_weighted = jnp.einsum(
        "gqs,gsd->gqd", weights, value_rows, preferred_element_type=jnp.float32
    )

    own_mixed, down_parts = merge_over(
        local_peak, local_total, local_weighted, "seq", seq_size, down_parts, steps, slice_width
    )
    own_mixed = own_mixed.transpose(1, 0, 2).astype(jnp.bfloat16)
    every_mixed = gather_xor(own_mixed, "req", req_size)[0]
    serves = placement[:, None] == request_ids[None, :]
    inverse = jnp.sum(jnp.where(serves, request_ids[:, None], 0), axis=0)
    mixed_rows = xor_slot(group_index ^ (inverse // group_rows), req_size) * group_rows + (
        inverse % group_rows
    )
    mixed_part = every_mixed.transpose(1, 0, 2, 3).reshape(steps, total, slice_width)
    mixed_part = jnp.take(mixed_part, mixed_rows, axis=1, mode="clip").reshape(rows, slice_width)

    down_part = jnp.concatenate(down_parts, axis=1)
    partial_sum = jnp.dot(mixed_part, w_out, preferred_element_type=jnp.float32) + down_part
    chunks = seq_size // req_size
    by_request = partial_sum.reshape(steps, total, part_width)
    blocks = by_request.reshape(steps, req_size, group_rows, chunks, slice_width)
    blocks = blocks.transpose(1, 3, 0, 2, 4).reshape(seq_size, steps, group_rows, slice_width)
    levels = seq_size.bit_length() - 1
    half = seq_size // 2
    pair = scatter_sum(blocks, "seq", seq_size, levels - 1)
    high = shard_index >= half
    own_block = jnp.where(high, pair[1], pair[0])
    other_block = jnp.where(high, pair[0], pair[1])

    def owner(source_group, block):
        return (block // chunks) * seq_size + source_group * chunks + block % chunks

    own_routes, other_routes = [], []
    for source_group in range(req_size):
        for block in range(seq_size):
            source = source_group * seq_size + block
            own_routes.append((source, owner(source_group, block)))
            other_routes.append((source, owner(source_group, block ^ half)))
    own_branch = lax.ppermute(own_block, ALL, own_routes) + lax.ppermute(
        other_block, ALL, other_routes
    )
    new_states = (states.astype(jnp.float32) + own_branch).astype(jnp.bfloat16)
    return (new_states, cache_now)


def solution(mesh):
    in_specs = (
        P(None, "req", "seq"),
        P("req", "seq", None),
        P(),
        P(),
        P(),
        P(),
        P("req", "seq"),
        P("req", None),
        P("seq", "req"),
        P("req", "seq"),
        P("seq", "req"),
    )
    out_specs = (P(None, "req", "seq"), P("req", "seq", None))
    return jax.shard_map(shards, mesh=mesh, in_specs=in_specs, out_specs=out_specs, check_vma=False)
```

```python
import jax
import jax.numpy as jnp
from jax import lax
from jax.sharding import PartitionSpec as P


EPSILON = 1e-05
NEGATIVE = -1e30
ALL = ("req", "seq")


def xor_pairs(size, bit):
    return [(index, index ^ bit) for index in range(size)]


def gather_xor(block, axis, size, riders=None):
    levels = size.bit_length() - 1
    riders = dict(riders or {})
    stacked = block
    for level in range(levels):
        bit = 2 ** (levels - 1 - level)
        stacked = jnp.stack([stacked, lax.ppermute(stacked, axis, xor_pairs(size, bit))])
        if level in riders:
            stacked, riders[level] = lax.optimization_barrier((stacked, riders[level]))
    return stacked.reshape((size,) + block.shape), riders


def xor_slot(offset, size):
    levels = size.bit_length() - 1
    position = jnp.zeros_like(offset)
    for level in range(levels):
        bit = 2 ** (levels - 1 - level)
        position = position + ((offset // bit) % 2) * (2 ** level)
    return position


def sum_over(value, axis, size):
    bit = 1
    while bit < size:
        value = value + lax.ppermute(value, axis, xor_pairs(size, bit))
        bit *= 2
    return value


def scatter_sum(blocks, axis, size, rounds):
    index = lax.axis_index(axis)
    levels = size.bit_length() - 1
    blocks = blocks.reshape((2,) * levels + blocks.shape[1:])
    for level in range(rounds):
        bit = 2 ** level
        place = levels - 1 - level
        high = (index // bit) % 2 == 1
        lower = lax.index_in_dim(blocks, 0, place, keepdims=False)
        upper = lax.index_in_dim(blocks, 1, place, keepdims=False)
        keep = jnp.where(high, upper, lower)
        send = jnp.where(high, lower, upper)
        blocks = keep + lax.ppermute(send, axis, xor_pairs(size, bit))
    return blocks


def split_exact(value):
    high = lax.reduce_precision(value, exponent_bits=8, mantissa_bits=7)
    rest = value - high
    middle = lax.reduce_precision(rest, exponent_bits=8, mantissa_bits=7)
    low = rest - middle
    return [part.astype(jnp.bfloat16) for part in (high, middle, low)]


def join_exact(pieces):
    pieces = pieces.astype(jnp.float32)
    return (pieces[..., 0] + pieces[..., 1]) + pieces[..., 2]


def pack_merge(peak, total, weighted):
    return jnp.concatenate(
        [jnp.stack(split_exact(peak) + split_exact(total), axis=-1), weighted.astype(jnp.bfloat16)],
        axis=-1,
    )


def merge_pair(peak, total, weighted, other):
    peak_second = join_exact(other[..., 0:3])
    total_second = join_exact(other[..., 3:6])
    weighted_second = other[..., 6:].astype(jnp.float32)
    merged_peak = jnp.maximum(peak, peak_second)
    scale_first = jnp.exp(peak - merged_peak)
    scale_second = jnp.exp(peak_second - merged_peak)
    total = total * scale_first + total_second * scale_second
    weighted = weighted * scale_first[..., None] + weighted_second * scale_second[..., None]
    return merged_peak, total, weighted


def merge_over(peak, total, weighted, axis, size, carried, steps, chunk_width):
    index = lax.axis_index(axis)
    group_rows, step_heads, head_width = weighted.shape
    head_count = step_heads // steps
    span = min(head_count, (chunk_width + 2 * head_width - 2) // head_width)
    bit = 1
    while bit < size // 2:
        if bit == 4:
            carried[0], peak, total, weighted = lax.optimization_barrier(
                (carried[0], peak, total, weighted)
            )
        other = lax.ppermute(pack_merge(peak, total, weighted), axis, xor_pairs(size, bit))
        peak, total, weighted = merge_pair(peak, total, weighted, other)
        bit *= 2

    def first_head(position):
        return jnp.minimum((position * chunk_width) // head_width, head_count - span)

    def window(value, start):
        value = value.reshape((group_rows, steps, head_count) + value.shape[2:])
        return lax.dynamic_slice_in_dim(value, start, span, 2)

    if size >= 16:
        carried[1], peak, total, weighted = lax.optimization_barrier(
            (carried[1], peak, total, weighted)
        )
    partner_start = first_head(index ^ bit)
    own_start = first_head(index)
    sent = window(pack_merge(peak, total, weighted), partner_start)
    other = lax.ppermute(sent, axis, xor_pairs(size, bit))
    _, total, weighted = merge_pair(
        window(peak, own_start), window(total, own_start), window(weighted, own_start), other
    )
    mixed = (weighted / total[..., None]).reshape(group_rows, steps, span * head_width)
    offset = index * chunk_width - own_start * head_width
    return lax.dynamic_slice_in_dim(mixed, offset, chunk_width, 2), carried


def layer_norm(row_block, norm_gain, norm_bias):
    values = row_block.astype(jnp.float32)
    average = jnp.mean(values, axis=-1, keepdims=True)
    centered = values - average
    spread = jnp.mean(centered * centered, axis=-1, keepdims=True)
    scaled = centered * lax.rsqrt(spread + EPSILON)
    return (scaled * norm_gain.astype(jnp.float32) + norm_bias.astype(jnp.float32)).astype(
        jnp.bfloat16
    )


def rotate(vectors, positions):
    head_width = vectors.shape[-1]
    half_width = head_width // 2
    frequency = 10000.0 ** (-(jnp.arange(half_width, dtype=jnp.float32) * 2.0) / head_width)
    angles = positions.astype(jnp.float32)[:, None] * frequency[None, :]
    cosine = jnp.concatenate([jnp.cos(angles), jnp.cos(angles)], axis=-1)[:, None, :]
    sine_wave = jnp.concatenate([jnp.sin(angles), jnp.sin(angles)], axis=-1)[:, None, :]
    turned = jnp.concatenate([-vectors[..., half_width:], vectors[..., :half_width]], axis=-1)
    return vectors * cosine + turned * sine_wave


def shards(
    states,
    kv_cache,
    lengths,
    placement,
    norm_gain,
    norm_bias,
    w_query,
    w_keyval,
    w_out,
    w_up,
    w_down,
):
    steps = states.shape[0]
    group_rows = kv_cache.shape[0]
    seg_length = kv_cache.shape[1]
    head_width = kv_cache.shape[2] // 2
    model_width = norm_gain.shape[0]
    head_count = model_width // head_width
    slice_width = states.shape[2]
    part_width = w_query.shape[0]
    total = placement.shape[0]
    req_size = total // group_rows
    seq_size = model_width // slice_width
    rows = steps * total
    group_index = lax.axis_index("req")
    shard_index = lax.axis_index("seq")

    seq_ids = jnp.arange(seq_size, dtype=jnp.int32)
    req_ids = jnp.arange(req_size, dtype=jnp.int32)
    seq_slots = xor_slot(shard_index ^ seq_ids, seq_size)
    req_slots = xor_slot(group_index ^ req_ids, req_size)

    by_request, _ = gather_xor(states, "req", req_size)
    every, riders = gather_xor(by_request, "seq", seq_size, {0: (norm_gain, norm_bias)})
    norm_gain, norm_bias = riders[0]
    every = every.reshape((seq_size * req_size,) + every.shape[2:])
    every = jnp.take(every, seq_slots[:, None] * req_size + req_slots[None, :], axis=0, mode="clip")
    current_all = every.transpose(2, 1, 3, 0, 4).reshape(steps, total, model_width)
    normed = layer_norm(current_all.reshape(rows, model_width), norm_gain, norm_bias)
    normed_part = lax.dynamic_slice_in_dim(normed, group_index * part_width, part_width, 1)

    part_query = jnp.dot(normed_part, w_query, preferred_element_type=jnp.float32)
    part_keyval = jnp.dot(normed_part, w_keyval, preferred_element_type=jnp.float32)
    first = sum_over(jnp.concatenate([part_query, part_keyval], axis=1), "req", req_size)
    part_up = jnp.dot(normed_part, w_up, preferred_element_type=jnp.float32)
    first, part_up = lax.optimization_barrier((first, part_up))
    request_ids = jnp.arange(total, dtype=jnp.int32)
    own_requests = lax.dynamic_slice_in_dim(placement, group_index * group_rows, group_rows, 0)
    own_serves = own_requests[:, None] == request_ids[None, :]
    slot_lengths = jnp.sum(jnp.where(own_serves, lengths[None, :], 0), axis=1)
    step_offsets = jnp.arange(steps, dtype=jnp.int32)
    positions = slot_lengths[None, :] + step_offsets[:, None]
    own_first = jnp.sum(
        jnp.where(own_serves[None, :, :, None], first.reshape(steps, 1, total, -1), 0.0), axis=2
    )
    own_query = own_first[:, :, :slice_width].astype(jnp.bfloat16)
    own_keyval = own_first[:, :, slice_width:]
    query_levels = seq_size.bit_length() - 1
    query_all = own_query
    up_part = None
    for level in range(query_levels):
        bit = 2 ** (query_levels - 1 - level)
        query_all = jnp.stack([query_all, lax.ppermute(query_all, "seq", xor_pairs(seq_size, bit))])
        if level == 0:
            query_all, (kv_cache, part_up) = lax.optimization_barrier((query_all, (kv_cache, part_up)))
        if level == 1:
            query_all, up_part = lax.optimization_barrier(
                (query_all, sum_over(part_up, "req", req_size))
            )
    if up_part is None:
        up_part = sum_over(part_up, "req", req_size)
    query_all = query_all.reshape((seq_size,) + own_query.shape)
    hidden = jax.nn.gelu(up_part, approximate=False).astype(jnp.bfloat16)
    down_half = w_down.shape[1] // 2
    down_parts = [
        jnp.dot(hidden, w_down[:, :down_half], preferred_element_type=jnp.float32),
        jnp.dot(hidden, w_down[:, down_half:], preferred_element_type=jnp.float32),
    ]
    query_all = jnp.take(query_all, seq_slots, axis=0, mode="clip")
    query_all = query_all.transpose(1, 2, 0, 3).reshape(steps, group_rows, model_width)
    flat_positions = positions.reshape(-1)
    query_rows = rotate(
        query_all.astype(jnp.float32).reshape(steps * group_rows, head_count, head_width),
        flat_positions,
    ).astype(jnp.bfloat16)
    own_keyval = own_keyval.reshape(steps * group_rows, 2 * head_width)
    new_key = rotate(own_keyval[:, None, :head_width], flat_positions)[:, 0, :]
    new_entry = jnp.concatenate([new_key, own_keyval[:, head_width:]], axis=-1).astype(jnp.bfloat16)
    new_entry = new_entry.reshape(steps, group_rows, 2 * head_width)

    local_slots = jnp.arange(seg_length, dtype=jnp.int32)
    global_positions = shard_index * seg_length + local_slots
    cache_now = kv_cache
    for step_index in range(steps):
        write_mask = global_positions[None, :] == positions[step_index][:, None]
        cache_now = jnp.where(write_mask[:, :, None], new_entry[step_index][:, None, :], cache_now)

    key_rows = cache_now[:, :, :head_width]
    value_rows = cache_now[:, :, head_width:]
    query_heads = (
        query_rows.reshape(steps, group_rows, head_count, head_width)
        .transpose(1, 0, 2, 3)
        .reshape(group_rows, steps * head_count, head_width)
    )
    scores = jnp.einsum(
        "gqd,gsd->gqs", query_heads, key_rows, preferred_element_type=jnp.float32
    ) * head_width ** (-0.5)
    head_positions = jnp.repeat(positions.T, head_count, axis=1)
    valid = global_positions[None, None, :] <= head_positions[:, :, None]
    local_peak = jnp.max(jnp.where(valid, scores, NEGATIVE), axis=-1)
    weights = jnp.where(valid, jnp.exp(scores - local_peak[:, :, None]), 0.0)
    local_total = jnp.sum(weights, axis=-1)
    local_weighted = jnp.einsum(
        "gqs,gsd->gqd", weights, value_rows, preferred_element_type=jnp.float32
    )

    own_mixed, down_parts = merge_over(
        local_peak, local_total, local_weighted, "seq", seq_size, down_parts, steps, slice_width
    )
    own_mixed = own_mixed.transpose(1, 0, 2).astype(jnp.bfloat16)
    every_mixed = gather_xor(own_mixed, "req", req_size)[0]
    serves = placement[:, None] == request_ids[None, :]
    inverse = jnp.sum(jnp.where(serves, request_ids[:, None], 0), axis=0)
    mixed_rows = xor_slot(group_index ^ (inverse // group_rows), req_size) * group_rows + (
        inverse % group_rows
    )
    mixed_part = every_mixed.transpose(1, 0, 2, 3).reshape(steps, total, slice_width)
    mixed_part = jnp.take(mixed_part, mixed_rows, axis=1, mode="clip").reshape(rows, slice_width)

    down_part = jnp.concatenate(down_parts, axis=1)
    partial_sum = jnp.dot(mixed_part, w_out, preferred_element_type=jnp.float32) + down_part
    chunks = seq_size // req_size
    by_request = partial_sum.reshape(steps, total, part_width)
    blocks = by_request.reshape(steps, req_size, group_rows, chunks, slice_width)
    blocks = blocks.transpose(1, 3, 0, 2, 4).reshape(seq_size, steps, group_rows, slice_width)
    levels = seq_size.bit_length() - 1
    half = seq_size // 2
    pair = scatter_sum(blocks, "seq", seq_size, levels - 1)
    high = shard_index >= half
    own_block = jnp.where(high, pair[1], pair[0])
    other_block = jnp.where(high, pair[0], pair[1])

    def owner(source_group, block):
        return (block // chunks) * seq_size + source_group * chunks + block % chunks

    own_routes, other_routes = [], []
    for source_group in range(req_size):
        for block in range(seq_size):
            source = source_group * seq_size + block
            own_routes.append((source, owner(source_group, block)))
            other_routes.append((source, owner(source_group, block ^ half)))
    own_branch = lax.ppermute(own_block, ALL, own_routes) + lax.ppermute(
        other_block, ALL, other_routes
    )
    new_states = (states.astype(jnp.float32) + own_branch).astype(jnp.bfloat16)
    return (new_states, cache_now)


def solution(mesh):
    in_specs = (
        P(None, "req", "seq"),
        P("req", "seq", None),
        P(),
        P(),
        P(),
        P(),
        P("req", "seq"),
        P("req", None),
        P("seq", "req"),
        P("req", "seq"),
        P("seq", "req"),
    )
    out_specs = (P(None, "req", "seq"), P("req", "seq", None))
    return jax.shard_map(shards, mesh=mesh, in_specs=in_specs, out_specs=out_specs, check_vma=False)
```

```python
import jax
import jax.numpy as jnp
from jax import lax
from jax.sharding import PartitionSpec as P


EPSILON = 1e-05
NEGATIVE = -1e30
ALL = ("req", "seq")


def xor_pairs(size, bit):
    return [(index, index ^ bit) for index in range(size)]


def gather_xor(block, axis, size, riders=None):
    levels = size.bit_length() - 1
    riders = dict(riders or {})
    stacked = block
    for level in range(levels):
        bit = 2 ** (levels - 1 - level)
        stacked = jnp.stack([stacked, lax.ppermute(stacked, axis, xor_pairs(size, bit))])
        if level in riders:
            stacked, riders[level] = lax.optimization_barrier((stacked, riders[level]))
    return stacked.reshape((size,) + block.shape), riders


def xor_slot(offset, size):
    levels = size.bit_length() - 1
    position = jnp.zeros_like(offset)
    for level in range(levels):
        bit = 2 ** (levels - 1 - level)
        position = position + ((offset // bit) % 2) * (2 ** level)
    return position


def sum_over(value, axis, size):
    bit = 1
    while bit < size:
        value = value + lax.ppermute(value, axis, xor_pairs(size, bit))
        bit *= 2
    return value


def scatter_sum(blocks, axis, size, rounds):
    index = lax.axis_index(axis)
    levels = size.bit_length() - 1
    blocks = blocks.reshape((2,) * levels + blocks.shape[1:])
    for level in range(rounds):
        bit = 2 ** level
        place = levels - 1 - level
        high = (index // bit) % 2 == 1
        lower = lax.index_in_dim(blocks, 0, place, keepdims=False)
        upper = lax.index_in_dim(blocks, 1, place, keepdims=False)
        keep = jnp.where(high, upper, lower)
        send = jnp.where(high, lower, upper)
        blocks = keep + lax.ppermute(send, axis, xor_pairs(size, bit))
    return blocks


def split_exact(value):
    high = lax.reduce_precision(value, exponent_bits=8, mantissa_bits=7)
    rest = value - high
    middle = lax.reduce_precision(rest, exponent_bits=8, mantissa_bits=7)
    low = rest - middle
    return [part.astype(jnp.bfloat16) for part in (high, middle, low)]


def join_exact(pieces):
    pieces = pieces.astype(jnp.float32)
    return (pieces[..., 0] + pieces[..., 1]) + pieces[..., 2]


def pack_merge(peak, total, weighted):
    return jnp.concatenate(
        [jnp.stack(split_exact(peak) + split_exact(total), axis=-1), weighted.astype(jnp.bfloat16)],
        axis=-1,
    )


def merge_pair(peak, total, weighted, other):
    peak_second = join_exact(other[..., 0:3])
    total_second = join_exact(other[..., 3:6])
    weighted_second = other[..., 6:].astype(jnp.float32)
    merged_peak = jnp.maximum(peak, peak_second)
    scale_first = jnp.exp(peak - merged_peak)
    scale_second = jnp.exp(peak_second - merged_peak)
    total = total * scale_first + total_second * scale_second
    weighted = weighted * scale_first[..., None] + weighted_second * scale_second[..., None]
    return merged_peak, total, weighted


def merge_over(peak, total, weighted, axis, size, carried, steps, chunk_width):
    index = lax.axis_index(axis)
    group_rows, step_heads, head_width = weighted.shape
    head_count = step_heads // steps
    span = min(head_count, (chunk_width + 2 * head_width - 2) // head_width)
    bit = 1
    while bit < size // 2:
        if bit == 4:
            carried[0], peak, total, weighted = lax.optimization_barrier(
                (carried[0], peak, total, weighted)
            )
        other = lax.ppermute(pack_merge(peak, total, weighted), axis, xor_pairs(size, bit))
        peak, total, weighted = merge_pair(peak, total, weighted, other)
        bit *= 2

    def first_head(position):
        return jnp.minimum((position * chunk_width) // head_width, head_count - span)

    def window(value, start):
        value = value.reshape((group_rows, steps, head_count) + value.shape[2:])
        return lax.dynamic_slice_in_dim(value, start, span, 2)

    if size >= 16:
        carried[1], peak, total, weighted = lax.optimization_barrier(
            (carried[1], peak, total, weighted)
        )
    partner_start = first_head(index ^ bit)
    own_start = first_head(index)
    sent = window(pack_merge(peak, total, weighted), partner_start)
    other = lax.ppermute(sent, axis, xor_pairs(size, bit))
    _, total, weighted = merge_pair(
        window(peak, own_start), window(total, own_start), window(weighted, own_start), other
    )
    mixed = (weighted / total[..., None]).reshape(group_rows, steps, span * head_width)
    offset = index * chunk_width - own_start * head_width
    return lax.dynamic_slice_in_dim(mixed, offset, chunk_width, 2), carried


def layer_norm(row_block, norm_gain, norm_bias):
    values = row_block.astype(jnp.float32)
    average = jnp.mean(values, axis=-1, keepdims=True)
    centered = values - average
    spread = jnp.mean(centered * centered, axis=-1, keepdims=True)
    scaled = centered * lax.rsqrt(spread + EPSILON)
    return (scaled * norm_gain.astype(jnp.float32) + norm_bias.astype(jnp.float32)).astype(
        jnp.bfloat16
    )


def rotate(vectors, positions):
    head_width = vectors.shape[-1]
    half_width = head_width // 2
    frequency = 10000.0 ** (-(jnp.arange(half_width, dtype=jnp.float32) * 2.0) / head_width)
    angles = positions.astype(jnp.float32)[:, None] * frequency[None, :]
    cosine = jnp.concatenate([jnp.cos(angles), jnp.cos(angles)], axis=-1)[:, None, :]
    sine_wave = jnp.concatenate([jnp.sin(angles), jnp.sin(angles)], axis=-1)[:, None, :]
    turned = jnp.concatenate([-vectors[..., half_width:], vectors[..., :half_width]], axis=-1)
    return vectors * cosine + turned * sine_wave


def shards(
    states,
    kv_cache,
    lengths,
    placement,
    norm_gain,
    norm_bias,
    w_query,
    w_keyval,
    w_out,
    w_up,
    w_down,
):
    steps = states.shape[0]
    group_rows = kv_cache.shape[0]
    seg_length = kv_cache.shape[1]
    head_width = kv_cache.shape[2] // 2
    model_width = norm_gain.shape[0]
    head_count = model_width // head_width
    slice_width = states.shape[2]
    part_width = w_query.shape[0]
    total = placement.shape[0]
    req_size = total // group_rows
    seq_size = model_width // slice_width
    rows = steps * total
    group_index = lax.axis_index("req")
    shard_index = lax.axis_index("seq")

    seq_ids = jnp.arange(seq_size, dtype=jnp.int32)
    req_ids = jnp.arange(req_size, dtype=jnp.int32)
    seq_slots = xor_slot(shard_index ^ seq_ids, seq_size)
    req_slots = xor_slot(group_index ^ req_ids, req_size)

    by_request, _ = gather_xor(states, "req", req_size)
    every, riders = gather_xor(by_request, "seq", seq_size, {0: (norm_gain, norm_bias)})
    norm_gain, norm_bias = riders[0]
    every = every.reshape((seq_size * req_size,) + every.shape[2:])
    every = jnp.take(every, seq_slots[:, None] * req_size + req_slots[None, :], axis=0, mode="clip")
    current_all = every.transpose(2, 1, 3, 0, 4).reshape(steps, total, model_width)
    normed = layer_norm(current_all.reshape(rows, model_width), norm_gain, norm_bias)
    normed_part = lax.dynamic_slice_in_dim(normed, group_index * part_width, part_width, 1)

    part_query = jnp.dot(normed_part, w_query, preferred_element_type=jnp.float32)
    part_keyval = jnp.dot(normed_part, w_keyval, preferred_element_type=jnp.float32)
    first = sum_over(jnp.concatenate([part_query, part_keyval], axis=1), "req", req_size)
    part_up = jnp.dot(normed_part, w_up, preferred_element_type=jnp.float32)
    first, part_up = lax.optimization_barrier((first, part_up))
    request_ids = jnp.arange(total, dtype=jnp.int32)
    own_requests = lax.dynamic_slice_in_dim(placement, group_index * group_rows, group_rows, 0)
    own_serves = own_requests[:, None] == request_ids[None, :]
    slot_lengths = jnp.sum(jnp.where(own_serves, lengths[None, :], 0), axis=1)
    step_offsets = jnp.arange(steps, dtype=jnp.int32)
    positions = slot_lengths[None, :] + step_offsets[:, None]
    own_first = jnp.sum(
        jnp.where(own_serves[None, :, :, None], first.reshape(steps, 1, total, -1), 0.0), axis=2
    )
    own_query = own_first[:, :, :slice_width].astype(jnp.bfloat16)
    own_keyval = own_first[:, :, slice_width:]
    up_part = sum_over(part_up, "req", req_size)
    hidden = jax.nn.gelu(up_part, approximate=False).astype(jnp.bfloat16)
    down_half = w_down.shape[1] // 2
    down_parts = [
        jnp.dot(hidden, w_down[:, :down_half], preferred_element_type=jnp.float32),
        jnp.dot(hidden, w_down[:, down_half:], preferred_element_type=jnp.float32),
    ]

    cache_input = kv_cache
    query_all, riders = gather_xor(own_query, "seq", seq_size, {0: kv_cache})
    kv_cache = riders[0]
    query_all = jnp.take(query_all, seq_slots, axis=0, mode="clip")
    query_all = query_all.transpose(1, 2, 0, 3).reshape(steps, group_rows, model_width)
    flat_positions = positions.reshape(-1)
    query_rows = rotate(
        query_all.astype(jnp.float32).reshape(steps * group_rows, head_count, head_width),
        flat_positions,
    ).astype(jnp.bfloat16)
    own_keyval = own_keyval.reshape(steps * group_rows, 2 * head_width)
    new_key = rotate(own_keyval[:, None, :head_width], flat_positions)[:, 0, :]
    new_entry = jnp.concatenate([new_key, own_keyval[:, head_width:]], axis=-1).astype(jnp.bfloat16)
    new_entry = new_entry.reshape(steps, group_rows, 2 * head_width)

    local_slots = jnp.arange(seg_length, dtype=jnp.int32)
    global_positions = shard_index * seg_length + local_slots
    cache_now = kv_cache
    for step_index in range(steps):
        write_mask = global_positions[None, :] == positions[step_index][:, None]
        cache_now = jnp.where(write_mask[:, :, None], new_entry[step_index][:, None, :], cache_now)

    cache_out = cache_input
    for step_index in range(steps):
        write_mask = global_positions[None, :] == positions[step_index][:, None]
        cache_out = jnp.where(write_mask[:, :, None], new_entry[step_index][:, None, :], cache_out)

    key_rows = cache_now[:, :, :head_width]
    value_rows = cache_now[:, :, head_width:]
    query_heads = (
        query_rows.reshape(steps, group_rows, head_count, head_width)
        .transpose(1, 0, 2, 3)
        .reshape(group_rows, steps * head_count, head_width)
    )
    scores = jnp.einsum(
        "gqd,gsd->gqs", query_heads, key_rows, preferred_element_type=jnp.float32
    ) * head_width ** (-0.5)
    head_positions = jnp.repeat(positions.T, head_count, axis=1)
    valid = global_positions[None, None, :] <= head_positions[:, :, None]
    local_peak = jnp.max(jnp.where(valid, scores, NEGATIVE), axis=-1)
    weights = jnp.where(valid, jnp.exp(scores - local_peak[:, :, None]), 0.0)
    local_total = jnp.sum(weights, axis=-1)
    local_weighted = jnp.einsum(
        "gqs,gsd->gqd", weights, value_rows, preferred_element_type=jnp.float32
    )

    own_mixed, down_parts = merge_over(
        local_peak, local_total, local_weighted, "seq", seq_size, down_parts, steps, slice_width
    )
    own_mixed = own_mixed.transpose(1, 0, 2).astype(jnp.bfloat16)
    every_mixed = gather_xor(own_mixed, "req", req_size)[0]
    serves = placement[:, None] == request_ids[None, :]
    inverse = jnp.sum(jnp.where(serves, request_ids[:, None], 0), axis=0)
    mixed_rows = xor_slot(group_index ^ (inverse // group_rows), req_size) * group_rows + (
        inverse % group_rows
    )
    mixed_part = every_mixed.transpose(1, 0, 2, 3).reshape(steps, total, slice_width)
    mixed_part = jnp.take(mixed_part, mixed_rows, axis=1, mode="clip").reshape(rows, slice_width)

    down_part = jnp.concatenate(down_parts, axis=1)
    partial_sum = jnp.dot(mixed_part, w_out, preferred_element_type=jnp.float32) + down_part
    chunks = seq_size // req_size
    by_request = partial_sum.reshape(steps, total, part_width)
    blocks = by_request.reshape(steps, req_size, group_rows, chunks, slice_width)
    blocks = blocks.transpose(1, 3, 0, 2, 4).reshape(seq_size, steps, group_rows, slice_width)
    levels = seq_size.bit_length() - 1
    half = seq_size // 2
    pair = scatter_sum(blocks, "seq", seq_size, levels - 1)
    high = shard_index >= half
    own_block = jnp.where(high, pair[1], pair[0])
    other_block = jnp.where(high, pair[0], pair[1])

    def owner(source_group, block):
        return (block // chunks) * seq_size + source_group * chunks + block % chunks

    own_routes, other_routes = [], []
    for source_group in range(req_size):
        for block in range(seq_size):
            source = source_group * seq_size + block
            own_routes.append((source, owner(source_group, block)))
            other_routes.append((source, owner(source_group, block ^ half)))
    own_branch = lax.ppermute(own_block, ALL, own_routes) + lax.ppermute(
        other_block, ALL, other_routes
    )
    new_states = (states.astype(jnp.float32) + own_branch).astype(jnp.bfloat16)
    return (new_states, cache_out)


def solution(mesh):
    in_specs = (
        P(None, "req", "seq"),
        P("req", "seq", None),
        P(),
        P(),
        P(),
        P(),
        P("req", "seq"),
        P("req", None),
        P("seq", "req"),
        P("req", "seq"),
        P("seq", "req"),
    )
    out_specs = (P(None, "req", "seq"), P("req", "seq", None))
    return jax.shard_map(shards, mesh=mesh, in_specs=in_specs, out_specs=out_specs, check_vma=False)
```

```python
import jax
import jax.numpy as jnp
from jax import lax
from jax.sharding import PartitionSpec as P


EPSILON = 1e-05
NEGATIVE = -1e30
ALL = ("req", "seq")


def xor_pairs(size, bit):
    return [(index, index ^ bit) for index in range(size)]


def gather_xor(block, axis, size, riders=None):
    levels = size.bit_length() - 1
    riders = dict(riders or {})
    stacked = block
    for level in range(levels):
        bit = 2 ** (levels - 1 - level)
        stacked = jnp.stack([stacked, lax.ppermute(stacked, axis, xor_pairs(size, bit))])
        if level in riders:
            stacked, riders[level] = lax.optimization_barrier((stacked, riders[level]))
    return stacked.reshape((size,) + block.shape), riders


def xor_slot(offset, size):
    levels = size.bit_length() - 1
    position = jnp.zeros_like(offset)
    for level in range(levels):
        bit = 2 ** (levels - 1 - level)
        position = position + ((offset // bit) % 2) * (2 ** level)
    return position


def sum_over(value, axis, size):
    bit = 1
    while bit < size:
        value = value + lax.ppermute(value, axis, xor_pairs(size, bit))
        bit *= 2
    return value


def scatter_sum(blocks, axis, size, rounds):
    index = lax.axis_index(axis)
    levels = size.bit_length() - 1
    blocks = blocks.reshape((2,) * levels + blocks.shape[1:])
    for level in range(rounds):
        bit = 2 ** level
        place = levels - 1 - level
        high = (index // bit) % 2 == 1
        lower = lax.index_in_dim(blocks, 0, place, keepdims=False)
        upper = lax.index_in_dim(blocks, 1, place, keepdims=False)
        keep = jnp.where(high, upper, lower)
        send = jnp.where(high, lower, upper)
        blocks = keep + lax.ppermute(send, axis, xor_pairs(size, bit))
    return blocks


def split_exact(value):
    high = lax.reduce_precision(value, exponent_bits=8, mantissa_bits=7)
    rest = value - high
    middle = lax.reduce_precision(rest, exponent_bits=8, mantissa_bits=7)
    low = rest - middle
    return [part.astype(jnp.bfloat16) for part in (high, middle, low)]


def join_exact(pieces):
    pieces = pieces.astype(jnp.float32)
    return (pieces[..., 0] + pieces[..., 1]) + pieces[..., 2]


def pack_merge(peak, total, weighted):
    return jnp.concatenate(
        [jnp.stack(split_exact(peak) + split_exact(total), axis=-1), weighted.astype(jnp.bfloat16)],
        axis=-1,
    )


def merge_pair(peak, total, weighted, other):
    peak_second = join_exact(other[..., 0:3])
    total_second = join_exact(other[..., 3:6])
    weighted_second = other[..., 6:].astype(jnp.float32)
    merged_peak = jnp.maximum(peak, peak_second)
    scale_first = jnp.exp(peak - merged_peak)
    scale_second = jnp.exp(peak_second - merged_peak)
    total = total * scale_first + total_second * scale_second
    weighted = weighted * scale_first[..., None] + weighted_second * scale_second[..., None]
    return merged_peak, total, weighted


def merge_over(peak, total, weighted, axis, size, carried, steps, chunk_width):
    index = lax.axis_index(axis)
    group_rows, step_heads, head_width = weighted.shape
    head_count = step_heads // steps
    span = min(head_count, (chunk_width + 2 * head_width - 2) // head_width)
    bit = 1
    while bit < size // 2:
        if bit == 4:
            carried[0], peak, total, weighted = lax.optimization_barrier(
                (carried[0], peak, total, weighted)
            )
        other = lax.ppermute(pack_merge(peak, total, weighted), axis, xor_pairs(size, bit))
        peak, total, weighted = merge_pair(peak, total, weighted, other)
        bit *= 2

    def first_head(position):
        return jnp.minimum((position * chunk_width) // head_width, head_count - span)

    def window(value, start):
        value = value.reshape((group_rows, steps, head_count) + value.shape[2:])
        return lax.dynamic_slice_in_dim(value, start, span, 2)

    if size >= 16:
        carried[1], peak, total, weighted = lax.optimization_barrier(
            (carried[1], peak, total, weighted)
        )
    partner_start = first_head(index ^ bit)
    own_start = first_head(index)
    sent = window(pack_merge(peak, total, weighted), partner_start)
    other = lax.ppermute(sent, axis, xor_pairs(size, bit))
    other, carried[2] = lax.optimization_barrier((other, carried[2]))
    _, total, weighted = merge_pair(
        window(peak, own_start), window(total, own_start), window(weighted, own_start), other
    )
    mixed = (weighted / total[..., None]).reshape(group_rows, steps, span * head_width)
    offset = index * chunk_width - own_start * head_width
    return lax.dynamic_slice_in_dim(mixed, offset, chunk_width, 2), carried


def layer_norm(row_block, norm_gain, norm_bias):
    values = row_block.astype(jnp.float32)
    average = jnp.mean(values, axis=-1, keepdims=True)
    centered = values - average
    spread = jnp.mean(centered * centered, axis=-1, keepdims=True)
    scaled = centered * lax.rsqrt(spread + EPSILON)
    return (scaled * norm_gain.astype(jnp.float32) + norm_bias.astype(jnp.float32)).astype(
        jnp.bfloat16
    )


def rotate(vectors, positions):
    head_width = vectors.shape[-1]
    half_width = head_width // 2
    frequency = 10000.0 ** (-(jnp.arange(half_width, dtype=jnp.float32) * 2.0) / head_width)
    angles = positions.astype(jnp.float32)[:, None] * frequency[None, :]
    cosine = jnp.concatenate([jnp.cos(angles), jnp.cos(angles)], axis=-1)[:, None, :]
    sine_wave = jnp.concatenate([jnp.sin(angles), jnp.sin(angles)], axis=-1)[:, None, :]
    turned = jnp.concatenate([-vectors[..., half_width:], vectors[..., :half_width]], axis=-1)
    return vectors * cosine + turned * sine_wave


def shards(
    states,
    kv_cache,
    lengths,
    placement,
    norm_gain,
    norm_bias,
    w_query,
    w_keyval,
    w_out,
    w_up,
    w_down,
):
    steps = states.shape[0]
    group_rows = kv_cache.shape[0]
    seg_length = kv_cache.shape[1]
    head_width = kv_cache.shape[2] // 2
    model_width = norm_gain.shape[0]
    head_count = model_width // head_width
    slice_width = states.shape[2]
    part_width = w_query.shape[0]
    total = placement.shape[0]
    req_size = total // group_rows
    seq_size = model_width // slice_width
    rows = steps * total
    group_index = lax.axis_index("req")
    shard_index = lax.axis_index("seq")

    seq_ids = jnp.arange(seq_size, dtype=jnp.int32)
    req_ids = jnp.arange(req_size, dtype=jnp.int32)
    seq_slots = xor_slot(shard_index ^ seq_ids, seq_size)
    req_slots = xor_slot(group_index ^ req_ids, req_size)

    by_request, _ = gather_xor(states, "req", req_size)
    every, riders = gather_xor(by_request, "seq", seq_size, {0: (norm_gain, norm_bias)})
    norm_gain, norm_bias = riders[0]
    every = every.reshape((seq_size * req_size,) + every.shape[2:])
    every = jnp.take(every, seq_slots[:, None] * req_size + req_slots[None, :], axis=0, mode="clip")
    current_all = every.transpose(2, 1, 3, 0, 4).reshape(steps, total, model_width)
    normed = layer_norm(current_all.reshape(rows, model_width), norm_gain, norm_bias)
    normed_part = lax.dynamic_slice_in_dim(normed, group_index * part_width, part_width, 1)

    part_query = jnp.dot(normed_part, w_query, preferred_element_type=jnp.float32)
    part_keyval = jnp.dot(normed_part, w_keyval, preferred_element_type=jnp.float32)
    first = sum_over(jnp.concatenate([part_query, part_keyval], axis=1), "req", req_size)
    part_up = jnp.dot(normed_part, w_up, preferred_element_type=jnp.float32)
    first, part_up = lax.optimization_barrier((first, part_up))
    request_ids = jnp.arange(total, dtype=jnp.int32)
    own_requests = lax.dynamic_slice_in_dim(placement, group_index * group_rows, group_rows, 0)
    own_serves = own_requests[:, None] == request_ids[None, :]
    slot_lengths = jnp.sum(jnp.where(own_serves, lengths[None, :], 0), axis=1)
    step_offsets = jnp.arange(steps, dtype=jnp.int32)
    positions = slot_lengths[None, :] + step_offsets[:, None]
    own_first = jnp.sum(
        jnp.where(own_serves[None, :, :, None], first.reshape(steps, 1, total, -1), 0.0), axis=2
    )
    own_query = own_first[:, :, :slice_width].astype(jnp.bfloat16)
    own_keyval = own_first[:, :, slice_width:]
    up_part = sum_over(part_up, "req", req_size)
    hidden = jax.nn.gelu(up_part, approximate=False).astype(jnp.bfloat16)
    down_cuts = [0, w_down.shape[1] * 3 // 8, w_down.shape[1] * 3 // 4, w_down.shape[1]]
    down_parts = [
        jnp.dot(hidden, w_down[:, start:stop], preferred_element_type=jnp.float32)
        for start, stop in zip(down_cuts[:-1], down_cuts[1:])
    ]

    query_all, riders = gather_xor(own_query, "seq", seq_size, {0: kv_cache})
    kv_cache = riders[0]
    query_all = jnp.take(query_all, seq_slots, axis=0, mode="clip")
    query_all = query_all.transpose(1, 2, 0, 3).reshape(steps, group_rows, model_width)
    flat_positions = positions.reshape(-1)
    query_rows = rotate(
        query_all.astype(jnp.float32).reshape(steps * group_rows, head_count, head_width),
        flat_positions,
    ).astype(jnp.bfloat16)
    own_keyval = own_keyval.reshape(steps * group_rows, 2 * head_width)
    new_key = rotate(own_keyval[:, None, :head_width], flat_positions)[:, 0, :]
    new_entry = jnp.concatenate([new_key, own_keyval[:, head_width:]], axis=-1).astype(jnp.bfloat16)
    new_entry = new_entry.reshape(steps, group_rows, 2 * head_width)

    local_slots = jnp.arange(seg_length, dtype=jnp.int32)
    global_positions = shard_index * seg_length + local_slots
    cache_now = kv_cache
    for step_index in range(steps):
        write_mask = global_positions[None, :] == positions[step_index][:, None]
        cache_now = jnp.where(write_mask[:, :, None], new_entry[step_index][:, None, :], cache_now)

    key_rows = cache_now[:, :, :head_width]
    value_rows = cache_now[:, :, head_width:]
    query_heads = (
        query_rows.reshape(steps, group_rows, head_count, head_width)
        .transpose(1, 0, 2, 3)
        .reshape(group_rows, steps * head_count, head_width)
    )
    scores = jnp.einsum(
        "gqd,gsd->gqs", query_heads, key_rows, preferred_element_type=jnp.float32
    ) * head_width ** (-0.5)
    head_positions = jnp.repeat(positions.T, head_count, axis=1)
    valid = global_positions[None, None, :] <= head_positions[:, :, None]
    local_peak = jnp.max(jnp.where(valid, scores, NEGATIVE), axis=-1)
    weights = jnp.where(valid, jnp.exp(scores - local_peak[:, :, None]), 0.0)
    local_total = jnp.sum(weights, axis=-1)
    local_weighted = jnp.einsum(
        "gqs,gsd->gqd", weights, value_rows, preferred_element_type=jnp.float32
    )

    own_mixed, down_parts = merge_over(
        local_peak, local_total, local_weighted, "seq", seq_size, down_parts, steps, slice_width
    )
    own_mixed = own_mixed.transpose(1, 0, 2).astype(jnp.bfloat16)
    every_mixed = gather_xor(own_mixed, "req", req_size)[0]
    serves = placement[:, None] == request_ids[None, :]
    inverse = jnp.sum(jnp.where(serves, request_ids[:, None], 0), axis=0)
    mixed_rows = xor_slot(group_index ^ (inverse // group_rows), req_size) * group_rows + (
        inverse % group_rows
    )
    mixed_part = every_mixed.transpose(1, 0, 2, 3).reshape(steps, total, slice_width)
    mixed_part = jnp.take(mixed_part, mixed_rows, axis=1, mode="clip").reshape(rows, slice_width)

    down_part = jnp.concatenate(down_parts, axis=1)
    partial_sum = jnp.dot(mixed_part, w_out, preferred_element_type=jnp.float32) + down_part
    chunks = seq_size // req_size
    by_request = partial_sum.reshape(steps, total, part_width)
    blocks = by_request.reshape(steps, req_size, group_rows, chunks, slice_width)
    blocks = blocks.transpose(1, 3, 0, 2, 4).reshape(seq_size, steps, group_rows, slice_width)
    levels = seq_size.bit_length() - 1
    half = seq_size // 2
    pair = scatter_sum(blocks, "seq", seq_size, levels - 1)
    high = shard_index >= half
    own_block = jnp.where(high, pair[1], pair[0])
    other_block = jnp.where(high, pair[0], pair[1])

    def owner(source_group, block):
        return (block // chunks) * seq_size + source_group * chunks + block % chunks

    own_routes, other_routes = [], []
    for source_group in range(req_size):
        for block in range(seq_size):
            source = source_group * seq_size + block
            own_routes.append((source, owner(source_group, block)))
            other_routes.append((source, owner(source_group, block ^ half)))
    own_branch = lax.ppermute(own_block, ALL, own_routes) + lax.ppermute(
        other_block, ALL, other_routes
    )
    new_states = (states.astype(jnp.float32) + own_branch).astype(jnp.bfloat16)
    return (new_states, cache_now)


def solution(mesh):
    in_specs = (
        P(None, "req", "seq"),
        P("req", "seq", None),
        P(),
        P(),
        P(),
        P(),
        P("req", "seq"),
        P("req", None),
        P("seq", "req"),
        P("req", "seq"),
        P("seq", "req"),
    )
    out_specs = (P(None, "req", "seq"), P("req", "seq", None))
    return jax.shard_map(shards, mesh=mesh, in_specs=in_specs, out_specs=out_specs, check_vma=False)
```

```python
import jax
import jax.numpy as jnp
from jax import lax
from jax.sharding import PartitionSpec as P


EPSILON = 1e-05
NEGATIVE = -1e30
ALL = ("req", "seq")


def xor_pairs(size, bit):
    return [(index, index ^ bit) for index in range(size)]


def gather_xor(block, axis, size, riders=None):
    levels = size.bit_length() - 1
    riders = dict(riders or {})
    stacked = block
    for level in range(levels):
        bit = 2 ** (levels - 1 - level)
        stacked = jnp.stack([stacked, lax.ppermute(stacked, axis, xor_pairs(size, bit))])
        if level in riders:
            stacked, riders[level] = lax.optimization_barrier((stacked, riders[level]))
    return stacked.reshape((size,) + block.shape), riders


def xor_slot(offset, size):
    levels = size.bit_length() - 1
    position = jnp.zeros_like(offset)
    for level in range(levels):
        bit = 2 ** (levels - 1 - level)
        position = position + ((offset // bit) % 2) * (2 ** level)
    return position


def sum_over(value, axis, size):
    bit = 1
    while bit < size:
        value = value + lax.ppermute(value, axis, xor_pairs(size, bit))
        bit *= 2
    return value


def scatter_sum(blocks, axis, size, rounds):
    index = lax.axis_index(axis)
    levels = size.bit_length() - 1
    blocks = blocks.reshape((2,) * levels + blocks.shape[1:])
    for level in range(rounds):
        bit = 2 ** level
        place = levels - 1 - level
        high = (index // bit) % 2 == 1
        lower = lax.index_in_dim(blocks, 0, place, keepdims=False)
        upper = lax.index_in_dim(blocks, 1, place, keepdims=False)
        keep = jnp.where(high, upper, lower)
        send = jnp.where(high, lower, upper)
        blocks = keep + lax.ppermute(send, axis, xor_pairs(size, bit))
    return blocks


def split_exact(value):
    high = lax.reduce_precision(value, exponent_bits=8, mantissa_bits=7)
    rest = value - high
    middle = lax.reduce_precision(rest, exponent_bits=8, mantissa_bits=7)
    low = rest - middle
    return [part.astype(jnp.bfloat16) for part in (high, middle, low)]


def join_exact(pieces):
    pieces = pieces.astype(jnp.float32)
    return (pieces[..., 0] + pieces[..., 1]) + pieces[..., 2]


def pack_merge(peak, total, weighted):
    return jnp.concatenate(
        [jnp.stack(split_exact(peak) + split_exact(total), axis=-1), weighted.astype(jnp.bfloat16)],
        axis=-1,
    )


def merge_pair(peak, total, weighted, other):
    peak_second = join_exact(other[..., 0:3])
    total_second = join_exact(other[..., 3:6])
    weighted_second = other[..., 6:].astype(jnp.float32)
    merged_peak = jnp.maximum(peak, peak_second)
    scale_first = jnp.exp(peak - merged_peak)
    scale_second = jnp.exp(peak_second - merged_peak)
    total = total * scale_first + total_second * scale_second
    weighted = weighted * scale_first[..., None] + weighted_second * scale_second[..., None]
    return merged_peak, total, weighted


def merge_over(peak, total, weighted, axis, size, carried, steps, chunk_width):
    index = lax.axis_index(axis)
    group_rows, step_heads, head_width = weighted.shape
    head_count = step_heads // steps
    span = min(head_count, (chunk_width + 2 * head_width - 2) // head_width)
    bit = 1
    while bit < size // 2:
        if bit == 4:
            carried[0], peak, total, weighted = lax.optimization_barrier(
                (carried[0], peak, total, weighted)
            )
        other = lax.ppermute(pack_merge(peak, total, weighted), axis, xor_pairs(size, bit))
        peak, total, weighted = merge_pair(peak, total, weighted, other)
        bit *= 2

    def first_head(position):
        return jnp.minimum((position * chunk_width) // head_width, head_count - span)

    def window(value, start):
        value = value.reshape((group_rows, steps, head_count) + value.shape[2:])
        return lax.dynamic_slice_in_dim(value, start, span, 2)

    if size >= 16:
        carried[1], peak, total, weighted = lax.optimization_barrier(
            (carried[1], peak, total, weighted)
        )
    partner_start = first_head(index ^ bit)
    own_start = first_head(index)
    sent = window(pack_merge(peak, total, weighted), partner_start)
    other = lax.ppermute(sent, axis, xor_pairs(size, bit))
    _, total, weighted = merge_pair(
        window(peak, own_start), window(total, own_start), window(weighted, own_start), other
    )
    mixed = (weighted / total[..., None]).reshape(group_rows, steps, span * head_width)
    offset = index * chunk_width - own_start * head_width
    return lax.dynamic_slice_in_dim(mixed, offset, chunk_width, 2), carried


def layer_norm(row_block, norm_gain, norm_bias):
    values = row_block.astype(jnp.float32)
    average = jnp.mean(values, axis=-1, keepdims=True)
    centered = values - average
    spread = jnp.mean(centered * centered, axis=-1, keepdims=True)
    scaled = centered * lax.rsqrt(spread + EPSILON)
    return (scaled * norm_gain.astype(jnp.float32) + norm_bias.astype(jnp.float32)).astype(
        jnp.bfloat16
    )


def rotate(vectors, positions):
    head_width = vectors.shape[-1]
    half_width = head_width // 2
    frequency = 10000.0 ** (-(jnp.arange(half_width, dtype=jnp.float32) * 2.0) / head_width)
    angles = positions.astype(jnp.float32)[:, None] * frequency[None, :]
    cosine = jnp.concatenate([jnp.cos(angles), jnp.cos(angles)], axis=-1)[:, None, :]
    sine_wave = jnp.concatenate([jnp.sin(angles), jnp.sin(angles)], axis=-1)[:, None, :]
    turned = jnp.concatenate([-vectors[..., half_width:], vectors[..., :half_width]], axis=-1)
    return vectors * cosine + turned * sine_wave


def shards(
    states,
    kv_cache,
    lengths,
    placement,
    norm_gain,
    norm_bias,
    w_query,
    w_keyval,
    w_out,
    w_up,
    w_down,
):
    steps = states.shape[0]
    group_rows = kv_cache.shape[0]
    seg_length = kv_cache.shape[1]
    head_width = kv_cache.shape[2] // 2
    model_width = norm_gain.shape[0]
    head_count = model_width // head_width
    slice_width = states.shape[2]
    part_width = w_query.shape[0]
    total = placement.shape[0]
    req_size = total // group_rows
    seq_size = model_width // slice_width
    rows = steps * total
    group_index = lax.axis_index("req")
    shard_index = lax.axis_index("seq")

    seq_ids = jnp.arange(seq_size, dtype=jnp.int32)
    req_ids = jnp.arange(req_size, dtype=jnp.int32)
    seq_slots = xor_slot(shard_index ^ seq_ids, seq_size)
    req_slots = xor_slot(group_index ^ req_ids, req_size)

    by_request, _ = gather_xor(states, "req", req_size)
    gain_level = min(1, seq_size.bit_length() - 2)
    every, riders = gather_xor(by_request, "seq", seq_size, {gain_level: (norm_gain, norm_bias)})
    norm_gain, norm_bias = riders[gain_level]
    every = every.reshape((seq_size * req_size,) + every.shape[2:])
    every = jnp.take(every, seq_slots[:, None] * req_size + req_slots[None, :], axis=0, mode="clip")
    current_all = every.transpose(2, 1, 3, 0, 4).reshape(steps, total, model_width)
    normed = layer_norm(current_all.reshape(rows, model_width), norm_gain, norm_bias)
    normed_part = lax.dynamic_slice_in_dim(normed, group_index * part_width, part_width, 1)

    part_query = jnp.dot(normed_part, w_query, preferred_element_type=jnp.float32)
    part_keyval = jnp.dot(normed_part, w_keyval, preferred_element_type=jnp.float32)
    first = sum_over(jnp.concatenate([part_query, part_keyval], axis=1), "req", req_size)
    part_up = jnp.dot(normed_part, w_up, preferred_element_type=jnp.float32)
    first, part_up = lax.optimization_barrier((first, part_up))
    request_ids = jnp.arange(total, dtype=jnp.int32)
    own_requests = lax.dynamic_slice_in_dim(placement, group_index * group_rows, group_rows, 0)
    own_serves = own_requests[:, None] == request_ids[None, :]
    slot_lengths = jnp.sum(jnp.where(own_serves, lengths[None, :], 0), axis=1)
    step_offsets = jnp.arange(steps, dtype=jnp.int32)
    positions = slot_lengths[None, :] + step_offsets[:, None]
    own_first = jnp.sum(
        jnp.where(own_serves[None, :, :, None], first.reshape(steps, 1, total, -1), 0.0), axis=2
    )
    own_query = own_first[:, :, :slice_width].astype(jnp.bfloat16)
    own_keyval = own_first[:, :, slice_width:]
    up_part = sum_over(part_up, "req", req_size)
    hidden = jax.nn.gelu(up_part, approximate=False).astype(jnp.bfloat16)
    down_half = w_down.shape[1] // 2
    down_parts = [
        jnp.dot(hidden, w_down[:, :down_half], preferred_element_type=jnp.float32),
        jnp.dot(hidden, w_down[:, down_half:], preferred_element_type=jnp.float32),
    ]

    query_all, riders = gather_xor(own_query, "seq", seq_size, {0: kv_cache})
    kv_cache = riders[0]
    query_all = jnp.take(query_all, seq_slots, axis=0, mode="clip")
    query_all = query_all.transpose(1, 2, 0, 3).reshape(steps, group_rows, model_width)
    flat_positions = positions.reshape(-1)
    query_rows = rotate(
        query_all.astype(jnp.float32).reshape(steps * group_rows, head_count, head_width),
        flat_positions,
    ).astype(jnp.bfloat16)
    own_keyval = own_keyval.reshape(steps * group_rows, 2 * head_width)
    new_key = rotate(own_keyval[:, None, :head_width], flat_positions)[:, 0, :]
    new_entry = jnp.concatenate([new_key, own_keyval[:, head_width:]], axis=-1).astype(jnp.bfloat16)
    new_entry = new_entry.reshape(steps, group_rows, 2 * head_width)

    local_slots = jnp.arange(seg_length, dtype=jnp.int32)
    global_positions = shard_index * seg_length + local_slots
    cache_now = kv_cache
    for step_index in range(steps):
        write_mask = global_positions[None, :] == positions[step_index][:, None]
        cache_now = jnp.where(write_mask[:, :, None], new_entry[step_index][:, None, :], cache_now)

    key_rows = cache_now[:, :, :head_width]
    value_rows = cache_now[:, :, head_width:]
    query_heads = (
        query_rows.reshape(steps, group_rows, head_count, head_width)
        .transpose(1, 0, 2, 3)
        .reshape(group_rows, steps * head_count, head_width)
    )
    scores = jnp.einsum(
        "gqd,gsd->gqs", query_heads, key_rows, preferred_element_type=jnp.float32
    ) * head_width ** (-0.5)
    head_positions = jnp.repeat(positions.T, head_count, axis=1)
    valid = global_positions[None, None, :] <= head_positions[:, :, None]
    local_peak = jnp.max(jnp.where(valid, scores, NEGATIVE), axis=-1)
    weights = jnp.where(valid, jnp.exp(scores - local_peak[:, :, None]), 0.0)
    local_total = jnp.sum(weights, axis=-1)
    local_weighted = jnp.einsum(
        "gqs,gsd->gqd", weights, value_rows, preferred_element_type=jnp.float32
    )

    own_mixed, down_parts = merge_over(
        local_peak, local_total, local_weighted, "seq", seq_size, down_parts, steps, slice_width
    )
    own_mixed = own_mixed.transpose(1, 0, 2).astype(jnp.bfloat16)
    every_mixed = gather_xor(own_mixed, "req", req_size)[0]
    serves = placement[:, None] == request_ids[None, :]
    inverse = jnp.sum(jnp.where(serves, request_ids[:, None], 0), axis=0)
    mixed_rows = xor_slot(group_index ^ (inverse // group_rows), req_size) * group_rows + (
        inverse % group_rows
    )
    mixed_part = every_mixed.transpose(1, 0, 2, 3).reshape(steps, total, slice_width)
    mixed_part = jnp.take(mixed_part, mixed_rows, axis=1, mode="clip").reshape(rows, slice_width)

    down_part = jnp.concatenate(down_parts, axis=1)
    partial_sum = jnp.dot(mixed_part, w_out, preferred_element_type=jnp.float32) + down_part
    chunks = seq_size // req_size
    by_request = partial_sum.reshape(steps, total, part_width)
    blocks = by_request.reshape(steps, req_size, group_rows, chunks, slice_width)
    blocks = blocks.transpose(1, 3, 0, 2, 4).reshape(seq_size, steps, group_rows, slice_width)
    levels = seq_size.bit_length() - 1
    half = seq_size // 2
    pair = scatter_sum(blocks, "seq", seq_size, levels - 1)
    high = shard_index >= half
    own_block = jnp.where(high, pair[1], pair[0])
    other_block = jnp.where(high, pair[0], pair[1])

    def owner(source_group, block):
        return (block // chunks) * seq_size + source_group * chunks + block % chunks

    own_routes, other_routes = [], []
    for source_group in range(req_size):
        for block in range(seq_size):
            source = source_group * seq_size + block
            own_routes.append((source, owner(source_group, block)))
            other_routes.append((source, owner(source_group, block ^ half)))
    own_branch = lax.ppermute(own_block, ALL, own_routes) + lax.ppermute(
        other_block, ALL, other_routes
    )
    new_states = (states.astype(jnp.float32) + own_branch).astype(jnp.bfloat16)
    return (new_states, cache_now)


def solution(mesh):
    in_specs = (
        P(None, "req", "seq"),
        P("req", "seq", None),
        P(),
        P(),
        P(),
        P(),
        P("req", "seq"),
        P("req", None),
        P("seq", "req"),
        P("req", "seq"),
        P("seq", "req"),
    )
    out_specs = (P(None, "req", "seq"), P("req", "seq", None))
    return jax.shard_map(shards, mesh=mesh, in_specs=in_specs, out_specs=out_specs, check_vma=False)
```

```python
import jax
import jax.numpy as jnp
from jax import lax
from jax.sharding import PartitionSpec as P


EPSILON = 1e-05
NEGATIVE = -1e30
ALL = ("req", "seq")


def xor_pairs(size, bit):
    return [(index, index ^ bit) for index in range(size)]


def gather_xor(block, axis, size, riders=None):
    levels = size.bit_length() - 1
    riders = dict(riders or {})
    stacked = block
    for level in range(levels):
        bit = 2 ** (levels - 1 - level)
        stacked = jnp.stack([stacked, lax.ppermute(stacked, axis, xor_pairs(size, bit))])
        if level in riders:
            stacked, riders[level] = lax.optimization_barrier((stacked, riders[level]))
    return stacked.reshape((size,) + block.shape), riders


def xor_slot(offset, size):
    levels = size.bit_length() - 1
    position = jnp.zeros_like(offset)
    for level in range(levels):
        bit = 2 ** (levels - 1 - level)
        position = position + ((offset // bit) % 2) * (2 ** level)
    return position


def sum_over(value, axis, size):
    bit = 1
    while bit < size:
        value = value + lax.ppermute(value, axis, xor_pairs(size, bit))
        bit *= 2
    return value


def scatter_sum(blocks, axis, size, rounds):
    index = lax.axis_index(axis)
    levels = size.bit_length() - 1
    blocks = blocks.reshape((2,) * levels + blocks.shape[1:])
    for level in range(rounds):
        bit = 2 ** level
        place = levels - 1 - level
        high = (index // bit) % 2 == 1
        lower = lax.index_in_dim(blocks, 0, place, keepdims=False)
        upper = lax.index_in_dim(blocks, 1, place, keepdims=False)
        keep = jnp.where(high, upper, lower)
        send = jnp.where(high, lower, upper)
        blocks = keep + lax.ppermute(send, axis, xor_pairs(size, bit))
    return blocks


def split_exact(value):
    high = lax.reduce_precision(value, exponent_bits=8, mantissa_bits=7)
    rest = value - high
    middle = lax.reduce_precision(rest, exponent_bits=8, mantissa_bits=7)
    low = rest - middle
    return [part.astype(jnp.bfloat16) for part in (high, middle, low)]


def join_exact(pieces):
    pieces = pieces.astype(jnp.float32)
    return (pieces[..., 0] + pieces[..., 1]) + pieces[..., 2]


def pack_merge(peak, total, weighted):
    return jnp.concatenate(
        [jnp.stack(split_exact(peak) + split_exact(total), axis=-1), weighted.astype(jnp.bfloat16)],
        axis=-1,
    )


def merge_pair(peak, total, weighted, other):
    peak_second = join_exact(other[..., 0:3])
    total_second = join_exact(other[..., 3:6])
    weighted_second = other[..., 6:].astype(jnp.float32)
    merged_peak = jnp.maximum(peak, peak_second)
    scale_first = jnp.exp(peak - merged_peak)
    scale_second = jnp.exp(peak_second - merged_peak)
    total = total * scale_first + total_second * scale_second
    weighted = weighted * scale_first[..., None] + weighted_second * scale_second[..., None]
    return merged_peak, total, weighted


def merge_over(peak, total, weighted, axis, size, carried, steps, chunk_width):
    index = lax.axis_index(axis)
    group_rows, step_heads, head_width = weighted.shape
    head_count = step_heads // steps
    span = min(head_count, (chunk_width + 2 * head_width - 2) // head_width)
    bit = 1
    while bit < size // 2:
        if bit == 4:
            carried[0], peak, total, weighted = lax.optimization_barrier(
                (carried[0], peak, total, weighted)
            )
        other = lax.ppermute(pack_merge(peak, total, weighted), axis, xor_pairs(size, bit))
        peak, total, weighted = merge_pair(peak, total, weighted, other)
        bit *= 2

    def first_head(position):
        return jnp.minimum((position * chunk_width) // head_width, head_count - span)

    def window(value, start):
        value = value.reshape((group_rows, steps, head_count) + value.shape[2:])
        return lax.dynamic_slice_in_dim(value, start, span, 2)

    if size >= 16:
        carried[1], peak, total, weighted = lax.optimization_barrier(
            (carried[1], peak, total, weighted)
        )
    partner_start = first_head(index ^ bit)
    own_start = first_head(index)
    sent = window(pack_merge(peak, total, weighted), partner_start)
    other = lax.ppermute(sent, axis, xor_pairs(size, bit))
    _, total, weighted = merge_pair(
        window(peak, own_start), window(total, own_start), window(weighted, own_start), other
    )
    mixed = (weighted / total[..., None]).reshape(group_rows, steps, span * head_width)
    offset = index * chunk_width - own_start * head_width
    return lax.dynamic_slice_in_dim(mixed, offset, chunk_width, 2), carried


def layer_norm(row_block, norm_gain, norm_bias):
    values = row_block.astype(jnp.float32)
    average = jnp.mean(values, axis=-1, keepdims=True)
    centered = values - average
    spread = jnp.mean(centered * centered, axis=-1, keepdims=True)
    scaled = centered * lax.rsqrt(spread + EPSILON)
    return (scaled * norm_gain.astype(jnp.float32) + norm_bias.astype(jnp.float32)).astype(
        jnp.bfloat16
    )


def rotate(vectors, positions):
    head_width = vectors.shape[-1]
    half_width = head_width // 2
    frequency = 10000.0 ** (-(jnp.arange(half_width, dtype=jnp.float32) * 2.0) / head_width)
    angles = positions.astype(jnp.float32)[:, None] * frequency[None, :]
    cosine = jnp.concatenate([jnp.cos(angles), jnp.cos(angles)], axis=-1)[:, None, :]
    sine_wave = jnp.concatenate([jnp.sin(angles), jnp.sin(angles)], axis=-1)[:, None, :]
    turned = jnp.concatenate([-vectors[..., half_width:], vectors[..., :half_width]], axis=-1)
    return vectors * cosine + turned * sine_wave


def shards(
    states,
    kv_cache,
    lengths,
    placement,
    norm_gain,
    norm_bias,
    w_query,
    w_keyval,
    w_out,
    w_up,
    w_down,
):
    steps = states.shape[0]
    group_rows = kv_cache.shape[0]
    seg_length = kv_cache.shape[1]
    head_width = kv_cache.shape[2] // 2
    model_width = norm_gain.shape[0]
    head_count = model_width // head_width
    slice_width = states.shape[2]
    part_width = w_query.shape[0]
    total = placement.shape[0]
    req_size = total // group_rows
    seq_size = model_width // slice_width
    rows = steps * total
    group_index = lax.axis_index("req")
    shard_index = lax.axis_index("seq")

    seq_ids = jnp.arange(seq_size, dtype=jnp.int32)
    req_ids = jnp.arange(req_size, dtype=jnp.int32)
    seq_slots = xor_slot(shard_index ^ seq_ids, seq_size)
    req_slots = xor_slot(group_index ^ req_ids, req_size)

    by_request, _ = gather_xor(states, "req", req_size)
    gain_level = min(2, seq_size.bit_length() - 2)
    every, riders = gather_xor(by_request, "seq", seq_size, {gain_level: (norm_gain, norm_bias)})
    norm_gain, norm_bias = riders[gain_level]
    every = every.reshape((seq_size * req_size,) + every.shape[2:])
    every = jnp.take(every, seq_slots[:, None] * req_size + req_slots[None, :], axis=0, mode="clip")
    current_all = every.transpose(2, 1, 3, 0, 4).reshape(steps, total, model_width)
    normed = layer_norm(current_all.reshape(rows, model_width), norm_gain, norm_bias)
    normed_part = lax.dynamic_slice_in_dim(normed, group_index * part_width, part_width, 1)

    part_query = jnp.dot(normed_part, w_query, preferred_element_type=jnp.float32)
    part_keyval = jnp.dot(normed_part, w_keyval, preferred_element_type=jnp.float32)
    first = sum_over(jnp.concatenate([part_query, part_keyval], axis=1), "req", req_size)
    part_up = jnp.dot(normed_part, w_up, preferred_element_type=jnp.float32)
    first, part_up = lax.optimization_barrier((first, part_up))
    request_ids = jnp.arange(total, dtype=jnp.int32)
    own_requests = lax.dynamic_slice_in_dim(placement, group_index * group_rows, group_rows, 0)
    own_serves = own_requests[:, None] == request_ids[None, :]
    slot_lengths = jnp.sum(jnp.where(own_serves, lengths[None, :], 0), axis=1)
    step_offsets = jnp.arange(steps, dtype=jnp.int32)
    positions = slot_lengths[None, :] + step_offsets[:, None]
    own_first = jnp.sum(
        jnp.where(own_serves[None, :, :, None], first.reshape(steps, 1, total, -1), 0.0), axis=2
    )
    own_query = own_first[:, :, :slice_width].astype(jnp.bfloat16)
    own_keyval = own_first[:, :, slice_width:]
    up_part = sum_over(part_up, "req", req_size)
    hidden = jax.nn.gelu(up_part, approximate=False).astype(jnp.bfloat16)
    down_half = w_down.shape[1] // 2
    down_parts = [
        jnp.dot(hidden, w_down[:, :down_half], preferred_element_type=jnp.float32),
        jnp.dot(hidden, w_down[:, down_half:], preferred_element_type=jnp.float32),
    ]

    query_all, riders = gather_xor(own_query, "seq", seq_size, {0: kv_cache})
    kv_cache = riders[0]
    query_all = jnp.take(query_all, seq_slots, axis=0, mode="clip")
    query_all = query_all.transpose(1, 2, 0, 3).reshape(steps, group_rows, model_width)
    flat_positions = positions.reshape(-1)
    query_rows = rotate(
        query_all.astype(jnp.float32).reshape(steps * group_rows, head_count, head_width),
        flat_positions,
    ).astype(jnp.bfloat16)
    own_keyval = own_keyval.reshape(steps * group_rows, 2 * head_width)
    new_key = rotate(own_keyval[:, None, :head_width], flat_positions)[:, 0, :]
    new_entry = jnp.concatenate([new_key, own_keyval[:, head_width:]], axis=-1).astype(jnp.bfloat16)
    new_entry = new_entry.reshape(steps, group_rows, 2 * head_width)

    local_slots = jnp.arange(seg_length, dtype=jnp.int32)
    global_positions = shard_index * seg_length + local_slots
    cache_now = kv_cache
    for step_index in range(steps):
        write_mask = global_positions[None, :] == positions[step_index][:, None]
        cache_now = jnp.where(write_mask[:, :, None], new_entry[step_index][:, None, :], cache_now)

    key_rows = cache_now[:, :, :head_width]
    value_rows = cache_now[:, :, head_width:]
    query_heads = (
        query_rows.reshape(steps, group_rows, head_count, head_width)
        .transpose(1, 0, 2, 3)
        .reshape(group_rows, steps * head_count, head_width)
    )
    scores = jnp.einsum(
        "gqd,gsd->gqs", query_heads, key_rows, preferred_element_type=jnp.float32
    ) * head_width ** (-0.5)
    head_positions = jnp.repeat(positions.T, head_count, axis=1)
    valid = global_positions[None, None, :] <= head_positions[:, :, None]
    local_peak = jnp.max(jnp.where(valid, scores, NEGATIVE), axis=-1)
    weights = jnp.where(valid, jnp.exp(scores - local_peak[:, :, None]), 0.0)
    local_total = jnp.sum(weights, axis=-1)
    local_weighted = jnp.einsum(
        "gqs,gsd->gqd", weights, value_rows, preferred_element_type=jnp.float32
    )

    own_mixed, down_parts = merge_over(
        local_peak, local_total, local_weighted, "seq", seq_size, down_parts, steps, slice_width
    )
    own_mixed = own_mixed.transpose(1, 0, 2).astype(jnp.bfloat16)
    every_mixed = gather_xor(own_mixed, "req", req_size)[0]
    serves = placement[:, None] == request_ids[None, :]
    inverse = jnp.sum(jnp.where(serves, request_ids[:, None], 0), axis=0)
    mixed_rows = xor_slot(group_index ^ (inverse // group_rows), req_size) * group_rows + (
        inverse % group_rows
    )
    mixed_part = every_mixed.transpose(1, 0, 2, 3).reshape(steps, total, slice_width)
    mixed_part = jnp.take(mixed_part, mixed_rows, axis=1, mode="clip").reshape(rows, slice_width)

    down_part = jnp.concatenate(down_parts, axis=1)
    partial_sum = jnp.dot(mixed_part, w_out, preferred_element_type=jnp.float32) + down_part
    chunks = seq_size // req_size
    by_request = partial_sum.reshape(steps, total, part_width)
    blocks = by_request.reshape(steps, req_size, group_rows, chunks, slice_width)
    blocks = blocks.transpose(1, 3, 0, 2, 4).reshape(seq_size, steps, group_rows, slice_width)
    levels = seq_size.bit_length() - 1
    half = seq_size // 2
    pair = scatter_sum(blocks, "seq", seq_size, levels - 1)
    high = shard_index >= half
    own_block = jnp.where(high, pair[1], pair[0])
    other_block = jnp.where(high, pair[0], pair[1])

    def owner(source_group, block):
        return (block // chunks) * seq_size + source_group * chunks + block % chunks

    own_routes, other_routes = [], []
    for source_group in range(req_size):
        for block in range(seq_size):
            source = source_group * seq_size + block
            own_routes.append((source, owner(source_group, block)))
            other_routes.append((source, owner(source_group, block ^ half)))
    own_branch = lax.ppermute(own_block, ALL, own_routes) + lax.ppermute(
        other_block, ALL, other_routes
    )
    new_states = (states.astype(jnp.float32) + own_branch).astype(jnp.bfloat16)
    return (new_states, cache_now)


def solution(mesh):
    in_specs = (
        P(None, "req", "seq"),
        P("req", "seq", None),
        P(),
        P(),
        P(),
        P(),
        P("req", "seq"),
        P("req", None),
        P("seq", "req"),
        P("req", "seq"),
        P("seq", "req"),
    )
    out_specs = (P(None, "req", "seq"), P("req", "seq", None))
    return jax.shard_map(shards, mesh=mesh, in_specs=in_specs, out_specs=out_specs, check_vma=False)
```

```python
import jax
import jax.numpy as jnp
from jax import lax
from jax.sharding import PartitionSpec as P


EPSILON = 1e-05
NEGATIVE = -1e30
ALL = ("req", "seq")


def xor_pairs(size, bit):
    return [(index, index ^ bit) for index in range(size)]


def gather_xor(block, axis, size, riders=None):
    levels = size.bit_length() - 1
    riders = dict(riders or {})
    stacked = block
    for level in range(levels):
        bit = 2 ** (levels - 1 - level)
        stacked = jnp.stack([stacked, lax.ppermute(stacked, axis, xor_pairs(size, bit))])
        if level in riders:
            stacked, riders[level] = lax.optimization_barrier((stacked, riders[level]))
    return stacked.reshape((size,) + block.shape), riders


def xor_slot(offset, size):
    levels = size.bit_length() - 1
    position = jnp.zeros_like(offset)
    for level in range(levels):
        bit = 2 ** (levels - 1 - level)
        position = position + ((offset // bit) % 2) * (2 ** level)
    return position


def sum_over(value, axis, size):
    bit = 1
    while bit < size:
        value = value + lax.ppermute(value, axis, xor_pairs(size, bit))
        bit *= 2
    return value


def scatter_sum(blocks, axis, size, rounds):
    index = lax.axis_index(axis)
    levels = size.bit_length() - 1
    blocks = blocks.reshape((2,) * levels + blocks.shape[1:])
    for level in range(rounds):
        bit = 2 ** level
        place = levels - 1 - level
        high = (index // bit) % 2 == 1
        lower = lax.index_in_dim(blocks, 0, place, keepdims=False)
        upper = lax.index_in_dim(blocks, 1, place, keepdims=False)
        keep = jnp.where(high, upper, lower)
        send = jnp.where(high, lower, upper)
        blocks = keep + lax.ppermute(send, axis, xor_pairs(size, bit))
    return blocks


def split_exact(value):
    high = lax.reduce_precision(value, exponent_bits=8, mantissa_bits=7)
    rest = value - high
    middle = lax.reduce_precision(rest, exponent_bits=8, mantissa_bits=7)
    low = rest - middle
    return [part.astype(jnp.bfloat16) for part in (high, middle, low)]


def join_exact(pieces):
    pieces = pieces.astype(jnp.float32)
    return (pieces[..., 0] + pieces[..., 1]) + pieces[..., 2]


def pack_merge(peak, total, weighted):
    return jnp.concatenate(
        [jnp.stack(split_exact(peak) + split_exact(total), axis=-1), weighted.astype(jnp.bfloat16)],
        axis=-1,
    )


def merge_pair(peak, total, weighted, other):
    peak_second = join_exact(other[..., 0:3])
    total_second = join_exact(other[..., 3:6])
    weighted_second = other[..., 6:].astype(jnp.float32)
    merged_peak = jnp.maximum(peak, peak_second)
    scale_first = jnp.exp(peak - merged_peak)
    scale_second = jnp.exp(peak_second - merged_peak)
    total = total * scale_first + total_second * scale_second
    weighted = weighted * scale_first[..., None] + weighted_second * scale_second[..., None]
    return merged_peak, total, weighted


def merge_over(peak, total, weighted, axis, size, carried, steps, chunk_width):
    index = lax.axis_index(axis)
    group_rows, step_heads, head_width = weighted.shape
    head_count = step_heads // steps
    span = min(head_count, (chunk_width + 2 * head_width - 2) // head_width)
    bit = 1
    while bit < size // 2:
        if bit == 4:
            carried[0], peak, total, weighted = lax.optimization_barrier(
                (carried[0], peak, total, weighted)
            )
        other = lax.ppermute(pack_merge(peak, total, weighted), axis, xor_pairs(size, bit))
        peak, total, weighted = merge_pair(peak, total, weighted, other)
        bit *= 2

    def first_head(position):
        return jnp.minimum((position * chunk_width) // head_width, head_count - span)

    def window(value, start):
        value = value.reshape((group_rows, steps, head_count) + value.shape[2:])
        return lax.dynamic_slice_in_dim(value, start, span, 2)

    if size >= 16:
        carried[1], peak, total, weighted = lax.optimization_barrier(
            (carried[1], peak, total, weighted)
        )
    partner_start = first_head(index ^ bit)
    own_start = first_head(index)
    sent = window(pack_merge(peak, total, weighted), partner_start)
    other = lax.ppermute(sent, axis, xor_pairs(size, bit))
    _, total, weighted = merge_pair(
        window(peak, own_start), window(total, own_start), window(weighted, own_start), other
    )
    mixed = (weighted / total[..., None]).reshape(group_rows, steps, span * head_width)
    offset = index * chunk_width - own_start * head_width
    return lax.dynamic_slice_in_dim(mixed, offset, chunk_width, 2), carried


def layer_norm(row_block, norm_gain, norm_bias):
    values = row_block.astype(jnp.float32)
    average = jnp.mean(values, axis=-1, keepdims=True)
    centered = values - average
    spread = jnp.mean(centered * centered, axis=-1, keepdims=True)
    scaled = centered * lax.rsqrt(spread + EPSILON)
    return (scaled * norm_gain.astype(jnp.float32) + norm_bias.astype(jnp.float32)).astype(
        jnp.bfloat16
    )


def rotate(vectors, positions):
    head_width = vectors.shape[-1]
    half_width = head_width // 2
    frequency = 10000.0 ** (-(jnp.arange(half_width, dtype=jnp.float32) * 2.0) / head_width)
    angles = positions.astype(jnp.float32)[:, None] * frequency[None, :]
    cosine = jnp.concatenate([jnp.cos(angles), jnp.cos(angles)], axis=-1)[:, None, :]
    sine_wave = jnp.concatenate([jnp.sin(angles), jnp.sin(angles)], axis=-1)[:, None, :]
    turned = jnp.concatenate([-vectors[..., half_width:], vectors[..., :half_width]], axis=-1)
    return vectors * cosine + turned * sine_wave


def shards(
    states,
    kv_cache,
    lengths,
    placement,
    norm_gain,
    norm_bias,
    w_query,
    w_keyval,
    w_out,
    w_up,
    w_down,
):
    steps = states.shape[0]
    group_rows = kv_cache.shape[0]
    seg_length = kv_cache.shape[1]
    head_width = kv_cache.shape[2] // 2
    model_width = norm_gain.shape[0]
    head_count = model_width // head_width
    slice_width = states.shape[2]
    part_width = w_query.shape[0]
    total = placement.shape[0]
    req_size = total // group_rows
    seq_size = model_width // slice_width
    rows = steps * total
    group_index = lax.axis_index("req")
    shard_index = lax.axis_index("seq")

    seq_ids = jnp.arange(seq_size, dtype=jnp.int32)
    req_ids = jnp.arange(req_size, dtype=jnp.int32)
    seq_slots = xor_slot(shard_index ^ seq_ids, seq_size)
    req_slots = xor_slot(group_index ^ req_ids, req_size)

    by_request, _ = gather_xor(states, "req", req_size)
    gain_level = min(1, seq_size.bit_length() - 2)
    every, riders = gather_xor(by_request, "seq", seq_size, {gain_level: (norm_gain, norm_bias)})
    norm_gain, norm_bias = riders[gain_level]
    every = every.reshape((seq_size * req_size,) + every.shape[2:])
    every = jnp.take(every, seq_slots[:, None] * req_size + req_slots[None, :], axis=0, mode="clip")
    current_all = every.transpose(2, 1, 3, 0, 4).reshape(steps, total, model_width)
    normed = layer_norm(current_all.reshape(rows, model_width), norm_gain, norm_bias)
    normed_part = lax.dynamic_slice_in_dim(normed, group_index * part_width, part_width, 1)

    part_query = jnp.dot(normed_part, w_query, preferred_element_type=jnp.float32)
    part_keyval = jnp.dot(normed_part, w_keyval, preferred_element_type=jnp.float32)
    first = sum_over(jnp.concatenate([part_query, part_keyval], axis=1), "req", req_size)
    part_up = jnp.dot(normed_part, w_up, preferred_element_type=jnp.float32)
    first, part_up = lax.optimization_barrier((first, part_up))
    request_ids = jnp.arange(total, dtype=jnp.int32)
    own_requests = lax.dynamic_slice_in_dim(placement, group_index * group_rows, group_rows, 0)
    own_serves = own_requests[:, None] == request_ids[None, :]
    slot_lengths = jnp.sum(jnp.where(own_serves, lengths[None, :], 0), axis=1)
    step_offsets = jnp.arange(steps, dtype=jnp.int32)
    positions = slot_lengths[None, :] + step_offsets[:, None]
    own_first = jnp.sum(
        jnp.where(own_serves[None, :, :, None], first.reshape(steps, 1, total, -1), 0.0), axis=2
    )
    own_query = own_first[:, :, :slice_width].astype(jnp.bfloat16)
    own_keyval = own_first[:, :, slice_width:]
    up_part = sum_over(part_up, "req", req_size)
    hidden = jax.nn.gelu(up_part, approximate=False).astype(jnp.bfloat16)
    down_half = w_down.shape[1] // 2
    down_parts = [
        jnp.dot(hidden, w_down[:, :down_half], preferred_element_type=jnp.float32),
        jnp.dot(hidden, w_down[:, down_half:], preferred_element_type=jnp.float32),
    ]

    cache_level = min(1, seq_size.bit_length() - 2)
    query_all, riders = gather_xor(own_query, "seq", seq_size, {cache_level: kv_cache})
    kv_cache = riders[cache_level]
    query_all = jnp.take(query_all, seq_slots, axis=0, mode="clip")
    query_all = query_all.transpose(1, 2, 0, 3).reshape(steps, group_rows, model_width)
    flat_positions = positions.reshape(-1)
    query_rows = rotate(
        query_all.astype(jnp.float32).reshape(steps * group_rows, head_count, head_width),
        flat_positions,
    ).astype(jnp.bfloat16)
    own_keyval = own_keyval.reshape(steps * group_rows, 2 * head_width)
    new_key = rotate(own_keyval[:, None, :head_width], flat_positions)[:, 0, :]
    new_entry = jnp.concatenate([new_key, own_keyval[:, head_width:]], axis=-1).astype(jnp.bfloat16)
    new_entry = new_entry.reshape(steps, group_rows, 2 * head_width)

    local_slots = jnp.arange(seg_length, dtype=jnp.int32)
    global_positions = shard_index * seg_length + local_slots
    cache_now = kv_cache
    for step_index in range(steps):
        write_mask = global_positions[None, :] == positions[step_index][:, None]
        cache_now = jnp.where(write_mask[:, :, None], new_entry[step_index][:, None, :], cache_now)

    key_rows = cache_now[:, :, :head_width]
    value_rows = cache_now[:, :, head_width:]
    query_heads = (
        query_rows.reshape(steps, group_rows, head_count, head_width)
        .transpose(1, 0, 2, 3)
        .reshape(group_rows, steps * head_count, head_width)
    )
    scores = jnp.einsum(
        "gqd,gsd->gqs", query_heads, key_rows, preferred_element_type=jnp.float32
    ) * head_width ** (-0.5)
    head_positions = jnp.repeat(positions.T, head_count, axis=1)
    valid = global_positions[None, None, :] <= head_positions[:, :, None]
    local_peak = jnp.max(jnp.where(valid, scores, NEGATIVE), axis=-1)
    weights = jnp.where(valid, jnp.exp(scores - local_peak[:, :, None]), 0.0)
    local_total = jnp.sum(weights, axis=-1)
    local_weighted = jnp.einsum(
        "gqs,gsd->gqd", weights, value_rows, preferred_element_type=jnp.float32
    )

    own_mixed, down_parts = merge_over(
        local_peak, local_total, local_weighted, "seq", seq_size, down_parts, steps, slice_width
    )
    own_mixed = own_mixed.transpose(1, 0, 2).astype(jnp.bfloat16)
    every_mixed = gather_xor(own_mixed, "req", req_size)[0]
    serves = placement[:, None] == request_ids[None, :]
    inverse = jnp.sum(jnp.where(serves, request_ids[:, None], 0), axis=0)
    mixed_rows = xor_slot(group_index ^ (inverse // group_rows), req_size) * group_rows + (
        inverse % group_rows
    )
    mixed_part = every_mixed.transpose(1, 0, 2, 3).reshape(steps, total, slice_width)
    mixed_part = jnp.take(mixed_part, mixed_rows, axis=1, mode="clip").reshape(rows, slice_width)

    down_part = jnp.concatenate(down_parts, axis=1)
    partial_sum = jnp.dot(mixed_part, w_out, preferred_element_type=jnp.float32) + down_part
    chunks = seq_size // req_size
    by_request = partial_sum.reshape(steps, total, part_width)
    blocks = by_request.reshape(steps, req_size, group_rows, chunks, slice_width)
    blocks = blocks.transpose(1, 3, 0, 2, 4).reshape(seq_size, steps, group_rows, slice_width)
    levels = seq_size.bit_length() - 1
    half = seq_size // 2
    pair = scatter_sum(blocks, "seq", seq_size, levels - 1)
    high = shard_index >= half
    own_block = jnp.where(high, pair[1], pair[0])
    other_block = jnp.where(high, pair[0], pair[1])

    def owner(source_group, block):
        return (block // chunks) * seq_size + source_group * chunks + block % chunks

    own_routes, other_routes = [], []
    for source_group in range(req_size):
        for block in range(seq_size):
            source = source_group * seq_size + block
            own_routes.append((source, owner(source_group, block)))
            other_routes.append((source, owner(source_group, block ^ half)))
    own_branch = lax.ppermute(own_block, ALL, own_routes) + lax.ppermute(
        other_block, ALL, other_routes
    )
    new_states = (states.astype(jnp.float32) + own_branch).astype(jnp.bfloat16)
    return (new_states, cache_now)


def solution(mesh):
    in_specs = (
        P(None, "req", "seq"),
        P("req", "seq", None),
        P(),
        P(),
        P(),
        P(),
        P("req", "seq"),
        P("req", None),
        P("seq", "req"),
        P("req", "seq"),
        P("seq", "req"),
    )
    out_specs = (P(None, "req", "seq"), P("req", "seq", None))
    return jax.shard_map(shards, mesh=mesh, in_specs=in_specs, out_specs=out_specs, check_vma=False)
```
